32 devices in a mesh: member: 4 (over y, core), band: 8 (over z, x).
Axes of the slice: x: 2, y: 2, z: 4, core: 2. Of those that a mesh axis runs over, the one named last changes fastest.
Arguments:
- obs_values: bfloat16 [65536, 128], P(('member', 'band')), parts along dimension 0, may hold values from -6 to 6
- obs_band: int32 [65536, 1], P(('member', 'band')), parts along dimension 0, may hold values from 0 to 7; in each aligned block of 2048 rows (0 to 2047, 2048 to 4095, ...) at most 256 rows name the same one
- obs_cell: int32 [65536], P(('member', 'band')), parts along dimension 0, may hold values from 0 to 2047
- obs_offset: int32 [65536], P(('member', 'band')), parts along dimension 0, may hold values from 0 to 7
- sat_values: bfloat16 [65536, 128], P(('member', 'band')), parts along dimension 0, may hold values from -6 to 6
- sat_cell: int32 [65536], P(('member', 'band')), parts along dimension 0, may hold values from 0 to 2047
- sat_offset: int32 [65536], P(('member', 'band')), parts along dimension 0, may hold values from 0 to 7
- density_embed: float32 [128], replicated, may hold values from -3 to 3
- conv1_weight: bfloat16 [3, 3, 128, 128], replicated, may hold values from -0.1875 to 0.1875
- conv1_bias: float32 [128], replicated, may hold values from -3 to 3
- conv2_weight: bfloat16 [3, 3, 128, 256], replicated, may hold values from -0.1875 to 0.1875
- conv2_bias: float32 [256], replicated, may hold values from -3 to 3
- proj_weight: bfloat16 [256, 256], replicated, may hold values from -0.375 to 0.375
Outputs:
- latents: bfloat16 [64, 64, 256], P('member'), parts along dimension 0
The draws below stay inside these ranges and needn't reach their ends.
There are 4 independent parts, one for each index of `member`. The reference program is written for one: setup_inputs(seed, part) draws one part's arguments, and reference() takes and returns one part's arrays. A program takes and returns all parts, laid end to end along the dimension named above; an argument that names none is the same for every part. Nothing has to cross between parts.
Inputs may be any that keep to these rules, and one draw needn't show every extreme that they name: `obs_band`: among the station rows of one device, at most 256 name the same band, and in every draw some band is named by exactly 256 rows of some device.
All inputs are finite; a program needn't handle non-finite values.
Results may differ from the reference program's by a relative error of at most 0.0061.
Values may be sent and summed in bfloat16 or wider, within the bound.
No kernel may reach another device: no remote copies, remote signals or barrier semaphores. Data moves between devices by JAX's collectives and lax.ppermute only.
A program may use at most 64 MiB of HBM per device.

```python
import math
import jax
import jax.numpy as jnp
import numpy as np

D_IN = 128
D_LAT = 256
LAT_DEV = 8
LON = 256
OBS_DEV = 2048
SAT_DEV = 2048
CAP = 256
BANDS = 8
CELLS = 2048
OBS = 16384
SAT = 16384
N_BAND = 8


def plant(array, key, least, high):
    dims = array.shape
    place = [jax.random.randint(jax.random.fold_in(key, axis), (), 0, dims[axis]) for axis in range(len(dims))]
    array = array.at[tuple(place)].set(least)
    longest = dims.index(max(dims))
    place[longest] = (place[longest] + 1) % dims[longest]
    return array.at[tuple(place)].set(high)


def level_of(key, shape, shards, low, high):
    def one(position, blocks):
        steps = jax.random.uniform(jax.random.fold_in(jax.random.fold_in(key, 6), position), (blocks,), jnp.float32, low / len(shards), high / len(shards))
        return jnp.repeat(jnp.exp(steps), shape[position] // blocks).reshape((-1,) + (1,) * (len(shape) - position - 1))

    loudness = one(*shards[0])
    for cut in shards[1:]:
        loudness = loudness * one(*cut)
    return loudness


def assign_block(stream_key, own, number, rows, amount, top, reach, skew):
    ranking = jax.random.permutation(stream_key, amount)
    crowded, common = shares(amount, rows * top, reach, skew, True), shares(amount, rows * top, reach, skew, False)
    places = jnp.arange(amount)

    def named(lengths, rotation):
        used = int((lengths > 0).sum())
        fixed = max(1, used // 4)
        moved = fixed + (places - fixed + rotation * (used - fixed)) % max(1, amount - fixed)
        return jnp.zeros((amount,), jnp.int32).at[ranking[jnp.where(places < fixed, places, moved)]].set(jnp.asarray(lengths, jnp.int32))

    lengths = jnp.where(number % 4 == 0, named(crowded, number // 4), named(common, number - number // 4 - 1))
    mixed = jax.random.permutation(jax.random.fold_in(own, 3), amount)
    donor, taker = mixed[0:amount // 2 * 2:2], mixed[1:amount // 2 * 2:2]
    margin = jnp.minimum(lengths[donor] - 1, reach - lengths[taker]) // 2
    margin = jnp.where((donor == ranking[0]) | (taker == ranking[0]) | (lengths[taker] == 0), 0, jnp.maximum(margin, 0))
    moved = jax.random.randint(jax.random.fold_in(own, 4), (amount // 2,), 0, 1 << 20) % (margin + 1)
    lengths = lengths.at[donor].add(-moved).at[taker].add(moved)
    members = jnp.searchsorted(jnp.cumsum(lengths), jnp.arange(rows * top), side="right").astype(jnp.int32)
    listing = members.reshape(top, rows).T
    listing = listing[jax.random.permutation(jax.random.fold_in(own, 1), rows)]
    rotation = jax.random.randint(jax.random.fold_in(own, 2), (rows, 1), 0, top)
    return jnp.take_along_axis(listing, (jnp.arange(top)[None, :] + rotation) % top, axis=1)


def shares(number_of, total, bound, skew, full):
    loads = [(1 << 20) // math.isqrt(grade ** skew) + 1 for grade in range(1, number_of + 1)]
    largest = bound if full else min(bound, max(-(-total // number_of), total * loads[0] // sum(loads)))
    least = 1 if total - largest >= number_of - 1 else 0
    given, spare = [largest] + [least] * (number_of - 1), total - largest - least * (number_of - 1)
    while spare > 0:
        candidates = [i for i in range(1, number_of) if given[i] < largest] or [i for i in range(1, number_of) if given[i] < bound]
        whole, remaining = sum([loads[i] for i in candidates]), spare
        for i in candidates:
            more = min(bound - given[i], max(1, remaining * loads[i] // whole), spare)
            given[i] = given[i] + more
            spare = spare - more
    return np.array(given)


def bell_draw(rng, extent, scale, limit, cuts=(), kind=jnp.bfloat16):
    loudness = level_of(rng, extent, cuts, -0.22, 0.18) if cuts else 1.0
    array = jax.random.normal(rng, extent, jnp.float32) * scale * loudness
    return jnp.minimum(jnp.maximum(array, -limit), limit).astype(kind)


def setup_inputs(seed: int = 0, part: int = 0) -> dict:
    streams_of = jax.random.split(jax.random.key(seed), 14)
    part_splits = jax.random.split(jax.random.fold_in(streams_of[13], part), 14)
    obs_values = bell_draw(part_splits[0], (OBS, D_IN), 1.0, 6.0, ((0, 8),))
    obs_band_keys = jax.random.split(jax.random.fold_in(part_splits[1], 1), OBS // OBS_DEV)
    obs_band_turns = jax.random.permutation(jax.random.fold_in(part_splits[1], 3), OBS // OBS_DEV)
    obs_band = jax.vmap(lambda own, number: assign_block(jax.random.fold_in(part_splits[1], 2), own, number, OBS_DEV, BANDS, 1, CAP, 2))(obs_band_keys, obs_band_turns).reshape((OBS, 1))
    obs_cell = plant(jax.random.randint(part_splits[2], (OBS,), 0, CELLS), jax.random.fold_in(part_splits[2], 1), 0, CELLS - 1).astype(jnp.int32)
    obs_offset = plant(jax.random.randint(part_splits[3], (OBS,), 0, 8), jax.random.fold_in(part_splits[3], 1), 0, 7).astype(jnp.int32)
    sat_values = bell_draw(part_splits[4], (SAT, D_IN), 1.0, 6.0, ((0, 8),))
    sat_cell = plant(jax.random.randint(part_splits[5], (SAT,), 0, CELLS), jax.random.fold_in(part_splits[5], 1), 0, CELLS - 1).astype(jnp.int32)
    sat_offset = plant(jax.random.randint(part_splits[6], (SAT,), 0, 8), jax.random.fold_in(part_splits[6], 1), 0, 7).astype(jnp.int32)
    density_embed = bell_draw(streams_of[7], (D_IN,), 0.5, 3.0, (), jnp.float32)
    conv1_weight = bell_draw(streams_of[8], (3, 3, D_IN, D_IN), (9 * D_IN) ** -0.5, 0.1875)
    conv1_bias = bell_draw(streams_of[9], (D_IN,), 0.5, 3.0, (), jnp.float32)
    conv2_weight = bell_draw(streams_of[10], (3, 3, D_IN, D_LAT), (9 * D_IN) ** -0.5, 0.1875)
    conv2_bias = bell_draw(streams_of[11], (D_LAT,), 0.5, 3.0, (), jnp.float32)
    proj_weight = bell_draw(streams_of[12], (D_LAT, D_LAT), D_LAT ** -0.5, 0.375)
    return {"obs_values": obs_values, "obs_band": obs_band, "obs_cell": obs_cell, "obs_offset": obs_offset, "sat_values": sat_values, "sat_cell": sat_cell, "sat_offset": sat_offset, "density_embed": density_embed, "conv1_weight": conv1_weight, "conv1_bias": conv1_bias, "conv2_weight": conv2_weight, "conv2_bias": conv2_bias, "proj_weight": proj_weight}


def weights_of(offsets):
    return jnp.exp(-(offsets.astype(jnp.float32) ** 2) / 32.0).astype(jnp.bfloat16)


def strided(padded, weight, bias):
    count, width, chans = padded.shape
    grid = jnp.pad(padded, ((0, 1), (1, 1), (0, 0)))
    parted = grid.reshape((count + 1) // 2, 2, (width + 2) // 2, 2, chans)
    rows = (count - 1) // 2
    cols = width // 2
    total = jnp.zeros((rows * cols, weight.shape[3]), jnp.float32)
    for first in range(3):
        for second in range(3):
            piece = parted[first // 2:first // 2 + rows, first % 2, second // 2:second // 2 + cols, second % 2, :]
            total = total + jnp.dot(piece.reshape(rows * cols, chans), weight[first, second], preferred_element_type=jnp.float32)
    return jax.nn.gelu(total + bias, approximate=False).reshape(rows, cols, weight.shape[3])


def reference(obs_values, obs_band, obs_cell, obs_offset, sat_values, sat_cell, sat_offset, density_embed, conv1_weight, conv1_bias, conv2_weight, conv2_bias, proj_weight):
    band_cells = LAT_DEV * LON
    station_ids = obs_band[:, 0].astype(jnp.int32) * band_cells + obs_cell.astype(jnp.int32)
    sat_bands = (jnp.arange(SAT_DEV * N_BAND, dtype=jnp.int32) // SAT_DEV).astype(jnp.int32)
    sat_ids = sat_bands * band_cells + sat_cell.astype(jnp.int32)
    ids = jnp.concatenate([station_ids, sat_ids]).astype(jnp.int32)
    values = jnp.concatenate([obs_values, sat_values]).astype(jnp.float32)
    weight = jnp.concatenate([weights_of(obs_offset), weights_of(sat_offset)]).astype(jnp.float32)
    total_cells = LAT_DEV * N_BAND * LON
    sums = jax.ops.segment_sum(values * weight[:, None], ids, num_segments=total_cells)
    density = jax.ops.segment_sum(weight, ids, num_segments=total_cells)
    grid0 = sums / jnp.maximum(density, 1.0)[:, None] + density[:, None] * density_embed[None, :]
    grid0 = grid0.astype(jnp.bfloat16).reshape(LAT_DEV * N_BAND, LON, D_IN)
    hidden1 = strided(jnp.pad(grid0, ((1, 0), (0, 0), (0, 0))), conv1_weight, conv1_bias).astype(jnp.bfloat16)
    latent = strided(jnp.pad(hidden1, ((1, 0), (0, 0), (0, 0))), conv2_weight, conv2_bias).astype(jnp.bfloat16)
    flat = jnp.dot(latent.reshape(-1, D_LAT), proj_weight, preferred_element_type=jnp.float32)
    return flat.astype(jnp.bfloat16).reshape(latent.shape)
```

```python
import jax
import jax.numpy as jnp
from jax import lax
from jax.sharding import PartitionSpec as P

LAT_DEV = 8
LON = 256
META = 16


def passed_along(value, axis, by):
    length = lax.axis_size(axis)
    pairs = [(i, i + by) for i in range(length) if 0 <= i + by < length]
    return lax.ppermute(value, axis, pairs)


def weights_of(offsets):
    return jnp.exp(-offsets.astype(jnp.float32) ** 2 / 32.0).astype(jnp.bfloat16)


def deposit(values, cells, weight, total_cells):
    block = min(512, total_cells)
    count = total_cells // block

    def one_block(start):
        ids = start + jnp.arange(block, dtype=jnp.int32)
        table = jnp.where(
            ids[:, None] == cells[None, :], weight[None, :], jnp.zeros((), jnp.bfloat16)
        )
        sums = jnp.dot(table, values, preferred_element_type=jnp.float32)
        density = jnp.sum(table, axis=1, dtype=jnp.float32)
        return (sums, density)

    starts = jnp.arange(count, dtype=jnp.int32) * block
    sums, density = lax.map(one_block, starts)
    return (sums.reshape(total_cells, values.shape[1]), density.reshape(total_cells))


def strided(padded, weight, bias):
    count, width, chans = padded.shape
    grid = jnp.pad(padded, ((0, 1), (1, 1), (0, 0)))
    parted = grid.reshape((count + 1) // 2, 2, (width + 2) // 2, 2, chans)
    rows = (count - 1) // 2
    cols = width // 2
    total = jnp.zeros((rows * cols, weight.shape[3]), jnp.float32)
    for first in range(3):
        for second in range(3):
            piece = parted[
                first // 2 : first // 2 + rows,
                first % 2,
                second // 2 : second // 2 + cols,
                second % 2,
                :,
            ]
            total = total + jnp.dot(
                piece.reshape(rows * cols, chans),
                weight[first, second],
                preferred_element_type=jnp.float32,
            )
    return jax.nn.gelu(total + bias, approximate=False).reshape(rows, cols, weight.shape[3])


def project(latent, proj_weight):
    flat = jnp.dot(
        latent.reshape(-1, latent.shape[2]), proj_weight, preferred_element_type=jnp.float32
    )
    return flat.astype(jnp.bfloat16).reshape(latent.shape)


def route(obs_values, obs_band, obs_cell, obs_offset, bands):
    obs_rows, d_in = obs_values.shape
    capacity = obs_rows // 8
    slots = bands * capacity
    target = obs_band[:, 0]
    choose = (target[:, None] == jnp.arange(bands, dtype=jnp.int32)[None, :]).astype(jnp.bfloat16)
    earlier = (
        jnp.arange(obs_rows, dtype=jnp.int32)[:, None] > jnp.arange(obs_rows, dtype=jnp.int32)[None, :]
    ).astype(jnp.bfloat16)
    before = jnp.dot(earlier, choose, preferred_element_type=jnp.float32)
    rank = jnp.sum(before * choose.astype(jnp.float32), axis=1).astype(jnp.int32)
    position = target * capacity + rank
    table = (jnp.arange(slots, dtype=jnp.int32)[:, None] == position[None, :]).astype(jnp.bfloat16)
    sent = jnp.dot(table, obs_values, preferred_element_type=jnp.float32).astype(jnp.bfloat16)
    meta = jnp.stack(
        [obs_cell // 64, obs_cell % 64, obs_offset + 1], axis=0
    ).astype(jnp.bfloat16)
    meta_sent = jnp.dot(meta, table.T, preferred_element_type=jnp.float32).astype(jnp.bfloat16)
    meta_sent = meta_sent.reshape(3, bands, capacity).transpose(1, 0, 2)
    meta_sent = meta_sent.reshape(bands, 3 * capacity // d_in, d_in)
    pad = jnp.zeros((bands, META - 3 * capacity // d_in, d_in), jnp.bfloat16)
    packet = jnp.concatenate([sent.reshape(bands, capacity, d_in), meta_sent, pad], axis=1)
    got = lax.all_to_all(packet, "band", split_axis=0, concat_axis=0, tiled=True)
    got_values = got[:, :capacity, :].reshape(slots, d_in)
    got_meta = got[:, capacity : capacity + 3 * capacity // d_in, :]
    got_meta = got_meta.reshape(bands, 3, capacity).transpose(1, 0, 2).reshape(3, slots)
    got_meta = got_meta.astype(jnp.int32)
    cells = got_meta[0] * 64 + got_meta[1]
    weight = jnp.where(got_meta[2] > 0, weights_of(got_meta[2] - 1), jnp.zeros((), jnp.bfloat16))
    return got_values, cells, weight


def body(
    obs_values,
    obs_band,
    obs_cell,
    obs_offset,
    sat_values,
    sat_cell,
    sat_offset,
    density_embed,
    conv1_weight,
    conv1_bias,
    conv2_weight,
    conv2_bias,
    proj_weight,
):
    bands = lax.axis_size("band")
    position_index = lax.axis_index("band")
    d_in = obs_values.shape[1]
    band_cells = LAT_DEV * LON
    got_values, got_cells, got_weight = route(obs_values, obs_band, obs_cell, obs_offset, bands)
    sat_sums, sat_density = deposit(sat_values, sat_cell, weights_of(sat_offset), band_cells)
    sta_sums, sta_density = deposit(got_values, got_cells, got_weight, band_cells)
    sums = sat_sums + sta_sums
    density = sat_density + sta_density
    grid0 = sums / jnp.maximum(density, 1.0)[:, None] + density[:, None] * density_embed[None, :]
    grid0 = grid0.astype(jnp.bfloat16).reshape(LAT_DEV, LON, d_in)
    above = passed_along(grid0[-3:], "band", 1)
    hidden1 = strided(jnp.concatenate([above, grid0], axis=0), conv1_weight, conv1_bias)
    keep_rows = (jnp.arange(hidden1.shape[0]) > 0) | (position_index > 0)
    hidden1 = jnp.where(keep_rows[:, None, None], hidden1, 0.0).astype(jnp.bfloat16)
    latent = strided(hidden1, conv2_weight, conv2_bias).astype(jnp.bfloat16)
    mine = project(latent, proj_weight)
    spread = jnp.broadcast_to(mine[None], (bands,) + mine.shape)
    gathered = lax.all_to_all(spread, "band", split_axis=0, concat_axis=0, tiled=True)
    return gathered.reshape((bands * mine.shape[0],) + mine.shape[1:])


def solution(mesh):
    placed = (
        P(("member", "band"), None),
        P(("member", "band"), None),
        P(("member", "band")),
        P(("member", "band")),
        P(("member", "band"), None),
        P(("member", "band")),
        P(("member", "band")),
        P(),
        P(),
        P(),
        P(),
        P(),
        P(),
    )
    return jax.shard_map(
        body, mesh=mesh, in_specs=placed, out_specs=P("member", None, None), check_vma=False
    )
```

```python
import jax
import jax.numpy as jnp
from jax import lax
from jax.sharding import PartitionSpec as P

LAT_DEV = 8
LON = 256
META = 16


def passed_along(value, axis, by):
    length = lax.axis_size(axis)
    pairs = [(i, i + by) for i in range(length) if 0 <= i + by < length]
    return lax.ppermute(value, axis, pairs)


def weights_of(offsets):
    return jnp.exp(-offsets.astype(jnp.float32) ** 2 / 32.0).astype(jnp.bfloat16)


def deposit(values, cells, weight, total_cells):
    block = min(512, total_cells)
    count = total_cells // block

    def one_block(start):
        ids = start + jnp.arange(block, dtype=jnp.int32)
        table = jnp.where(
            ids[:, None] == cells[None, :], weight[None, :], jnp.zeros((), jnp.bfloat16)
        )
        sums = jnp.dot(table, values, preferred_element_type=jnp.float32)
        density = jnp.sum(table, axis=1, dtype=jnp.float32)
        return (sums, density)

    starts = jnp.arange(count, dtype=jnp.int32) * block
    sums, density = lax.map(one_block, starts)
    return (sums.reshape(total_cells, values.shape[1]), density.reshape(total_cells))


def strided(padded, weight, bias):
    count, width, chans = padded.shape
    grid = jnp.pad(padded, ((0, 1), (1, 1), (0, 0)))
    parted = grid.reshape((count + 1) // 2, 2, (width + 2) // 2, 2, chans)
    rows = (count - 1) // 2
    cols = width // 2
    total = jnp.zeros((rows * cols, weight.shape[3]), jnp.float32)
    for first in range(3):
        for second in range(3):
            piece = parted[
                first // 2 : first // 2 + rows,
                first % 2,
                second // 2 : second // 2 + cols,
                second % 2,
                :,
            ]
            total = total + jnp.dot(
                piece.reshape(rows * cols, chans),
                weight[first, second],
                preferred_element_type=jnp.float32,
            )
    return jax.nn.gelu(total + bias, approximate=False).reshape(rows, cols, weight.shape[3])


def project(latent, proj_weight):
    flat = jnp.dot(
        latent.reshape(-1, latent.shape[2]), proj_weight, preferred_element_type=jnp.float32
    )
    return flat.astype(jnp.bfloat16).reshape(latent.shape)


def route(obs_values, obs_band, obs_cell, obs_offset, bands):
    obs_rows, d_in = obs_values.shape
    capacity = obs_rows // 8
    slots = bands * capacity
    target = obs_band[:, 0]
    choose = (target[:, None] == jnp.arange(bands, dtype=jnp.int32)[None, :]).astype(jnp.bfloat16)
    earlier = (
        jnp.arange(obs_rows, dtype=jnp.int32)[:, None] > jnp.arange(obs_rows, dtype=jnp.int32)[None, :]
    ).astype(jnp.bfloat16)
    before = jnp.dot(earlier, choose, preferred_element_type=jnp.float32)
    rank = jnp.sum(before * choose.astype(jnp.float32), axis=1).astype(jnp.int32)
    position = target * capacity + rank
    table = (jnp.arange(slots, dtype=jnp.int32)[:, None] == position[None, :]).astype(jnp.bfloat16)
    sent = jnp.dot(table, obs_values, preferred_element_type=jnp.float32).astype(jnp.bfloat16)
    meta = jnp.stack(
        [obs_cell // 64, obs_cell % 64, obs_offset + 1], axis=0
    ).astype(jnp.bfloat16)
    meta_sent = jnp.dot(meta, table.T, preferred_element_type=jnp.float32).astype(jnp.bfloat16)
    meta_sent = meta_sent.reshape(3, bands, capacity).transpose(1, 0, 2)
    meta_sent = meta_sent.reshape(bands, 3 * capacity // d_in, d_in)
    pad = jnp.zeros((bands, META - 3 * capacity // d_in, d_in), jnp.bfloat16)
    packet = jnp.concatenate([sent.reshape(bands, capacity, d_in), meta_sent, pad], axis=1)
    got = lax.all_to_all(packet, "band", split_axis=0, concat_axis=0, tiled=True)
    got_values = got[:, :capacity, :].reshape(slots, d_in)
    got_meta = got[:, capacity : capacity + 3 * capacity // d_in, :]
    got_meta = got_meta.reshape(bands, 3, capacity).transpose(1, 0, 2).reshape(3, slots)
    got_meta = got_meta.astype(jnp.int32)
    cells = got_meta[0] * 64 + got_meta[1]
    weight = jnp.where(got_meta[2] > 0, weights_of(got_meta[2] - 1), jnp.zeros((), jnp.bfloat16))
    return got_values, cells, weight


def body(
    obs_values,
    obs_band,
    obs_cell,
    obs_offset,
    sat_values,
    sat_cell,
    sat_offset,
    density_embed,
    conv1_weight,
    conv1_bias,
    conv2_weight,
    conv2_bias,
    proj_weight,
):
    bands = lax.axis_size("band")
    position_index = lax.axis_index("band")
    d_in = obs_values.shape[1]
    band_cells = LAT_DEV * LON
    got_values, got_cells, got_weight = route(obs_values, obs_band, obs_cell, obs_offset, bands)
    sat_sums, sat_density = deposit(sat_values, sat_cell, weights_of(sat_offset), band_cells)
    sta_sums, sta_density = deposit(got_values, got_cells, got_weight, band_cells)
    sums = sat_sums + sta_sums
    density = sat_density + sta_density
    grid0 = sums / jnp.maximum(density, 1.0)[:, None] + density[:, None] * density_embed[None, :]
    grid0 = grid0.astype(jnp.bfloat16).reshape(LAT_DEV, LON, d_in)
    above = passed_along(grid0[-3:], "band", 1)
    hidden1 = strided(jnp.concatenate([above, grid0], axis=0), conv1_weight, conv1_bias)
    keep_rows = (jnp.arange(hidden1.shape[0]) > 0) | (position_index > 0)
    hidden1 = jnp.where(keep_rows[:, None, None], hidden1, 0.0).astype(jnp.bfloat16)
    latent = strided(hidden1, conv2_weight, conv2_bias).astype(jnp.bfloat16)
    mine = project(latent, proj_weight)
    full = jnp.zeros((bands,) + mine.shape, mine.dtype)
    full = lax.dynamic_update_slice(full, mine[None], (position_index, 0, 0, 0))
    gathered = lax.psum(full, "band")
    return gathered.reshape((bands * mine.shape[0],) + mine.shape[1:])


def solution(mesh):
    placed = (
        P(("member", "band"), None),
        P(("member", "band"), None),
        P(("member", "band")),
        P(("member", "band")),
        P(("member", "band"), None),
        P(("member", "band")),
        P(("member", "band")),
        P(),
        P(),
        P(),
        P(),
        P(),
        P(),
    )
    return jax.shard_map(
        body, mesh=mesh, in_specs=placed, out_specs=P("member", None, None), check_vma=False
    )
```

```python
import functools

import jax
import jax.numpy as jnp
from jax import lax
from jax.experimental import pallas as pl
from jax.experimental.pallas import tpu as pltpu
from jax.sharding import PartitionSpec as P

LAT_DEV = 8
LON = 256
META = 16


def passed_along(value, axis, by):
    length = lax.axis_size(axis)
    pairs = [(i, i + by) for i in range(length) if 0 <= i + by < length]
    return lax.ppermute(value, axis, pairs)


def weights_of(offsets):
    return jnp.exp(-offsets.astype(jnp.float32) ** 2 / 32.0).astype(jnp.bfloat16)


CELL_BLOCK = 256
OBS_CHUNK = 512


def deposit_kernel(n_sat, n_sta, sat_v, sat_c, sat_w, sta_v, sta_c, sta_w, embed, out, acc_v, acc_d):
    base = pl.program_id(0) * CELL_BLOCK
    ids = base + lax.broadcasted_iota(jnp.int32, (CELL_BLOCK, OBS_CHUNK), 0)
    ones = jnp.ones((OBS_CHUNK, acc_d.shape[1]), jnp.bfloat16)
    acc_v[...] = jnp.zeros_like(acc_v)
    acc_d[...] = jnp.zeros_like(acc_d)

    def run(vals, cells_ref, w_ref, chunks):
        def step(i, carry):
            at = pl.ds(pl.multiple_of(i * OBS_CHUNK, OBS_CHUNK), OBS_CHUNK)
            cells = cells_ref[:, at]
            w = w_ref[:, at]
            table = jnp.where(cells == ids, w, 0.0).astype(jnp.bfloat16)
            acc_v[...] += jnp.dot(table, vals[at, :], preferred_element_type=jnp.float32)
            acc_d[...] += jnp.dot(table, ones, preferred_element_type=jnp.float32)
            return carry

        lax.fori_loop(0, chunks, step, 0)

    run(sat_v, sat_c, sat_w, n_sat // OBS_CHUNK)
    run(sta_v, sta_c, sta_w, n_sta // OBS_CHUNK)
    density = acc_d[...]
    grid = acc_v[...] / jnp.maximum(density, 1.0) + density * embed[...]
    out[...] = grid.astype(out.dtype)


def deposit_all(sat_values, sat_cells, sat_weight, sta_values, sta_cells, sta_weight, embed, total_cells):
    n_sat, d_in = sat_values.shape
    n_sta = sta_values.shape[0]
    whole = lambda shape: pl.BlockSpec(shape, lambda c: (0,) * len(shape))
    flops = 4 * total_cells * (n_sat + n_sta) * d_in
    return pl.pallas_call(
        functools.partial(deposit_kernel, n_sat, n_sta),
        grid=(total_cells // CELL_BLOCK,),
        in_specs=[
            whole((n_sat, d_in)),
            whole((1, n_sat)),
            whole((1, n_sat)),
            whole((n_sta, d_in)),
            whole((1, n_sta)),
            whole((1, n_sta)),
            whole((1, d_in)),
        ],
        out_specs=pl.BlockSpec((CELL_BLOCK, d_in), lambda c: (c, 0)),
        out_shape=jax.ShapeDtypeStruct((total_cells, d_in), jnp.bfloat16),
        scratch_shapes=[
            pltpu.VMEM((CELL_BLOCK, d_in), jnp.float32),
            pltpu.VMEM((CELL_BLOCK, d_in), jnp.float32),
        ],
        cost_estimate=pl.CostEstimate(
            flops=flops, transcendentals=0, bytes_accessed=2 * (n_sat + n_sta) * (d_in + 4)
        ),
    )(
        sat_values,
        sat_cells.reshape(1, n_sat),
        sat_weight.astype(jnp.float32).reshape(1, n_sat),
        sta_values,
        sta_cells.reshape(1, n_sta),
        sta_weight.astype(jnp.float32).reshape(1, n_sta),
        embed.reshape(1, d_in),
    )


def strided(padded, weight, bias):
    count, width, chans = padded.shape
    grid = jnp.pad(padded, ((0, 1), (1, 1), (0, 0)))
    parted = grid.reshape((count + 1) // 2, 2, (width + 2) // 2, 2, chans)
    rows = (count - 1) // 2
    cols = width // 2
    total = jnp.zeros((rows * cols, weight.shape[3]), jnp.float32)
    for first in range(3):
        for second in range(3):
            piece = parted[
                first // 2 : first // 2 + rows,
                first % 2,
                second // 2 : second // 2 + cols,
                second % 2,
                :,
            ]
            total = total + jnp.dot(
                piece.reshape(rows * cols, chans),
                weight[first, second],
                preferred_element_type=jnp.float32,
            )
    return jax.nn.gelu(total + bias, approximate=False).reshape(rows, cols, weight.shape[3])


def project(latent, proj_weight):
    flat = jnp.dot(
        latent.reshape(-1, latent.shape[2]), proj_weight, preferred_element_type=jnp.float32
    )
    return flat.astype(jnp.bfloat16).reshape(latent.shape)


def route(obs_values, obs_band, obs_cell, obs_offset, bands):
    obs_rows, d_in = obs_values.shape
    capacity = obs_rows // 8
    slots = bands * capacity
    target = obs_band[:, 0]
    choose = (target[:, None] == jnp.arange(bands, dtype=jnp.int32)[None, :]).astype(jnp.bfloat16)
    earlier = (
        jnp.arange(obs_rows, dtype=jnp.int32)[:, None] > jnp.arange(obs_rows, dtype=jnp.int32)[None, :]
    ).astype(jnp.bfloat16)
    before = jnp.dot(earlier, choose, preferred_element_type=jnp.float32)
    rank = jnp.sum(before * choose.astype(jnp.float32), axis=1).astype(jnp.int32)
    position = target * capacity + rank
    table = (jnp.arange(slots, dtype=jnp.int32)[:, None] == position[None, :]).astype(jnp.bfloat16)
    sent = jnp.dot(table, obs_values, preferred_element_type=jnp.float32).astype(jnp.bfloat16)
    meta = jnp.stack(
        [obs_cell // 64, obs_cell % 64, obs_offset + 1], axis=0
    ).astype(jnp.bfloat16)
    meta_sent = jnp.dot(meta, table.T, preferred_element_type=jnp.float32).astype(jnp.bfloat16)
    meta_sent = meta_sent.reshape(3, bands, capacity).transpose(1, 0, 2)
    meta_sent = meta_sent.reshape(bands, 3 * capacity // d_in, d_in)
    pad = jnp.zeros((bands, META - 3 * capacity // d_in, d_in), jnp.bfloat16)
    packet = jnp.concatenate([sent.reshape(bands, capacity, d_in), meta_sent, pad], axis=1)
    got = lax.all_to_all(packet, "band", split_axis=0, concat_axis=0, tiled=True)
    got_values = got[:, :capacity, :].reshape(slots, d_in)
    got_meta = got[:, capacity : capacity + 3 * capacity // d_in, :]
    got_meta = got_meta.reshape(bands, 3, capacity).transpose(1, 0, 2).reshape(3, slots)
    got_meta = got_meta.astype(jnp.int32)
    cells = got_meta[0] * 64 + got_meta[1]
    weight = jnp.where(got_meta[2] > 0, weights_of(got_meta[2] - 1), jnp.zeros((), jnp.bfloat16))
    return got_values, cells, weight


def body(
    obs_values,
    obs_band,
    obs_cell,
    obs_offset,
    sat_values,
    sat_cell,
    sat_offset,
    density_embed,
    conv1_weight,
    conv1_bias,
    conv2_weight,
    conv2_bias,
    proj_weight,
):
    bands = lax.axis_size("band")
    position_index = lax.axis_index("band")
    d_in = obs_values.shape[1]
    band_cells = LAT_DEV * LON
    got_values, got_cells, got_weight = route(obs_values, obs_band, obs_cell, obs_offset, bands)
    grid0 = deposit_all(
        sat_values, sat_cell, weights_of(sat_offset), got_values, got_cells, got_weight,
        density_embed, band_cells,
    ).reshape(LAT_DEV, LON, d_in)
    above = passed_along(grid0[-3:], "band", 1)
    hidden1 = strided(jnp.concatenate([above, grid0], axis=0), conv1_weight, conv1_bias)
    keep_rows = (jnp.arange(hidden1.shape[0]) > 0) | (position_index > 0)
    hidden1 = jnp.where(keep_rows[:, None, None], hidden1, 0.0).astype(jnp.bfloat16)
    latent = strided(hidden1, conv2_weight, conv2_bias).astype(jnp.bfloat16)
    mine = project(latent, proj_weight)
    spread = jnp.broadcast_to(mine[None], (bands,) + mine.shape)
    gathered = lax.all_to_all(spread, "band", split_axis=0, concat_axis=0, tiled=True)
    return gathered.reshape((bands * mine.shape[0],) + mine.shape[1:])


def solution(mesh):
    placed = (
        P(("member", "band"), None),
        P(("member", "band"), None),
        P(("member", "band")),
        P(("member", "band")),
        P(("member", "band"), None),
        P(("member", "band")),
        P(("member", "band")),
        P(),
        P(),
        P(),
        P(),
        P(),
        P(),
    )
    return jax.shard_map(
        body, mesh=mesh, in_specs=placed, out_specs=P("member", None, None), check_vma=False
    )
```

```python
import functools

import jax
import jax.numpy as jnp
from jax import lax
from jax.experimental import pallas as pl
from jax.experimental.pallas import tpu as pltpu
from jax.sharding import PartitionSpec as P

LAT_DEV = 8
LON = 256
META = 16


def passed_along(value, axis, by):
    length = lax.axis_size(axis)
    pairs = [(i, i + by) for i in range(length) if 0 <= i + by < length]
    return lax.ppermute(value, axis, pairs)


def weights_of(offsets):
    return jnp.exp(-offsets.astype(jnp.float32) ** 2 / 32.0).astype(jnp.bfloat16)


CELL_BLOCK = 256
OBS_CHUNK = 2048


def deposit_rows(v_ref, c_ref, w_ref, aug, block):
    n, d_in = v_ref.shape
    aug[:, :d_in] = v_ref[...]
    aug[:, d_in:] = jnp.ones((n, aug.shape[1] - d_in), jnp.bfloat16)
    chunk = min(n, OBS_CHUNK)
    ids = lax.broadcasted_iota(jnp.int32, (CELL_BLOCK, chunk), 0).astype(jnp.float32)
    ids = ids.astype(jnp.bfloat16)
    base = block * CELL_BLOCK
    total = jnp.zeros((CELL_BLOCK, aug.shape[1]), jnp.float32)
    for start in range(0, n, chunk):
        rel = c_ref[:, start : start + chunk] - base
        rel = jnp.where((rel >= 0) & (rel < CELL_BLOCK), rel, -1).astype(jnp.float32)
        w = w_ref[:, start : start + chunk].astype(jnp.bfloat16)
        table = jnp.where(rel.astype(jnp.bfloat16) == ids, w, jnp.zeros((), jnp.bfloat16))
        total = total + jnp.dot(table, aug[start : start + chunk, :], preferred_element_type=jnp.float32)
    return total


def sat_kernel(v_ref, c_ref, w_ref, out, aug):
    block = pl.program_id(0)
    out[...] = deposit_rows(v_ref, c_ref, w_ref, aug, block)


def station_kernel(acc, v_ref, c_ref, w_ref, embed, out, aug):
    block = pl.program_id(0)
    total = acc[...] + deposit_rows(v_ref, c_ref, w_ref, aug, block)
    d_in = out.shape[1]
    sums = total[:, :d_in]
    density = total[:, d_in:]
    grid = sums / jnp.maximum(density, 1.0) + density * embed[...]
    out[...] = grid.astype(out.dtype)


def whole(shape):
    return pl.BlockSpec(shape, lambda c: (0,) * len(shape))


def deposit_call(kernel, acc, values, cells, weight, extra, out_dtype, total_cells):
    n, d_in = values.shape
    wide = 2 * d_in
    ins = [values, cells.reshape(1, n), weight.astype(jnp.float32).reshape(1, n)]
    specs = [whole((n, d_in)), whole((1, n)), whole((1, n))]
    if acc is not None:
        ins = [acc] + ins
        specs = [pl.BlockSpec((CELL_BLOCK, wide), lambda c: (c, 0))] + specs
    for e in extra:
        ins.append(e)
        specs.append(whole(e.shape))
    out_cols = wide if out_dtype == jnp.float32 else d_in
    return pl.pallas_call(
        kernel,
        grid=(total_cells // CELL_BLOCK,),
        in_specs=specs,
        out_specs=pl.BlockSpec((CELL_BLOCK, out_cols), lambda c: (c, 0)),
        out_shape=jax.ShapeDtypeStruct((total_cells, out_cols), out_dtype),
        scratch_shapes=[pltpu.VMEM((n, wide), jnp.bfloat16)],
        cost_estimate=pl.CostEstimate(
            flops=2 * total_cells * n * wide, transcendentals=0, bytes_accessed=2 * n * (d_in + 4)
        ),
    )(*ins)


def strided(padded, weight, bias):
    count, width, chans = padded.shape
    grid = jnp.pad(padded, ((0, 1), (1, 1), (0, 0)))
    parted = grid.reshape((count + 1) // 2, 2, (width + 2) // 2, 2, chans)
    rows = (count - 1) // 2
    cols = width // 2
    total = jnp.zeros((rows * cols, weight.shape[3]), jnp.float32)
    for first in range(3):
        for second in range(3):
            piece = parted[
                first // 2 : first // 2 + rows,
                first % 2,
                second // 2 : second // 2 + cols,
                second % 2,
                :,
            ]
            total = total + jnp.dot(
                piece.reshape(rows * cols, chans),
                weight[first, second],
                preferred_element_type=jnp.float32,
            )
    return jax.nn.gelu(total + bias, approximate=False).reshape(rows, cols, weight.shape[3])


def project(latent, proj_weight):
    flat = jnp.dot(
        latent.reshape(-1, latent.shape[2]), proj_weight, preferred_element_type=jnp.float32
    )
    return flat.astype(jnp.bfloat16).reshape(latent.shape)


def route(obs_values, obs_band, obs_cell, obs_offset, bands):
    obs_rows, d_in = obs_values.shape
    capacity = obs_rows // 8
    slots = bands * capacity
    target = obs_band[:, 0]
    choose = (target[:, None] == jnp.arange(bands, dtype=jnp.int32)[None, :]).astype(jnp.bfloat16)
    earlier = (
        jnp.arange(obs_rows, dtype=jnp.int32)[:, None] > jnp.arange(obs_rows, dtype=jnp.int32)[None, :]
    ).astype(jnp.bfloat16)
    before = jnp.dot(earlier, choose, preferred_element_type=jnp.float32)
    rank = jnp.sum(before * choose.astype(jnp.float32), axis=1).astype(jnp.int32)
    position = target * capacity + rank
    table = (jnp.arange(slots, dtype=jnp.int32)[:, None] == position[None, :]).astype(jnp.bfloat16)
    sent = jnp.dot(table, obs_values, preferred_element_type=jnp.float32).astype(jnp.bfloat16)
    meta = jnp.stack(
        [obs_cell // 64, obs_cell % 64, obs_offset + 1], axis=0
    ).astype(jnp.bfloat16)
    meta_sent = jnp.dot(meta, table.T, preferred_element_type=jnp.float32).astype(jnp.bfloat16)
    meta_sent = meta_sent.reshape(3, bands, capacity).transpose(1, 0, 2)
    meta_sent = meta_sent.reshape(bands, 3 * capacity // d_in, d_in)
    pad = jnp.zeros((bands, META - 3 * capacity // d_in, d_in), jnp.bfloat16)
    packet = jnp.concatenate([sent.reshape(bands, capacity, d_in), meta_sent, pad], axis=1)
    got = lax.all_to_all(packet, "band", split_axis=0, concat_axis=0, tiled=True)
    got_values = got[:, :capacity, :].reshape(slots, d_in)
    got_meta = got[:, capacity : capacity + 3 * capacity // d_in, :]
    got_meta = got_meta.reshape(bands, 3, capacity).transpose(1, 0, 2).reshape(3, slots)
    got_meta = got_meta.astype(jnp.int32)
    cells = got_meta[0] * 64 + got_meta[1]
    weight = jnp.where(got_meta[2] > 0, weights_of(got_meta[2] - 1), jnp.zeros((), jnp.bfloat16))
    return got_values, cells, weight


def body(
    obs_values,
    obs_band,
    obs_cell,
    obs_offset,
    sat_values,
    sat_cell,
    sat_offset,
    density_embed,
    conv1_weight,
    conv1_bias,
    conv2_weight,
    conv2_bias,
    proj_weight,
):
    bands = lax.axis_size("band")
    position_index = lax.axis_index("band")
    d_in = obs_values.shape[1]
    band_cells = LAT_DEV * LON
    got_values, got_cells, got_weight = route(obs_values, obs_band, obs_cell, obs_offset, bands)
    sat_acc = deposit_call(
        sat_kernel, None, sat_values, sat_cell, weights_of(sat_offset), (), jnp.float32, band_cells
    )
    grid0 = deposit_call(
        station_kernel, sat_acc, got_values, got_cells, got_weight,
        (density_embed.reshape(1, d_in),), jnp.bfloat16, band_cells,
    ).reshape(LAT_DEV, LON, d_in)
    above = passed_along(grid0[-3:], "band", 1)
    hidden1 = strided(jnp.concatenate([above, grid0], axis=0), conv1_weight, conv1_bias)
    keep_rows = (jnp.arange(hidden1.shape[0]) > 0) | (position_index > 0)
    hidden1 = jnp.where(keep_rows[:, None, None], hidden1, 0.0).astype(jnp.bfloat16)
    latent = strided(hidden1, conv2_weight, conv2_bias).astype(jnp.bfloat16)
    mine = project(latent, proj_weight)
    spread = jnp.broadcast_to(mine[None], (bands,) + mine.shape)
    gathered = lax.all_to_all(spread, "band", split_axis=0, concat_axis=0, tiled=True)
    return gathered.reshape((bands * mine.shape[0],) + mine.shape[1:])


def solution(mesh):
    placed = (
        P(("member", "band"), None),
        P(("member", "band"), None),
        P(("member", "band")),
        P(("member", "band")),
        P(("member", "band"), None),
        P(("member", "band")),
        P(("member", "band")),
        P(),
        P(),
        P(),
        P(),
        P(),
        P(),
    )
    return jax.shard_map(
        body, mesh=mesh, in_specs=placed, out_specs=P("member", None, None), check_vma=False
    )
```

```python
import functools

import jax
import jax.numpy as jnp
from jax import lax
from jax.experimental import pallas as pl
from jax.experimental.pallas import tpu as pltpu
from jax.sharding import PartitionSpec as P

LAT_DEV = 8
LON = 256
META = 16


def passed_along(value, axis, by):
    length = lax.axis_size(axis)
    pairs = [(i, i + by) for i in range(length) if 0 <= i + by < length]
    return lax.ppermute(value, axis, pairs)


def weights_of(offsets):
    return jnp.exp(-offsets.astype(jnp.float32) ** 2 / 32.0).astype(jnp.bfloat16)


CELL_BLOCK = 256
OBS_CHUNK = 2048


def lookup(codes, table, shift):
    w = jnp.zeros(codes.shape, jnp.float32)
    for j in range(8):
        w = jnp.where(codes == j + shift, table[j], w)
    return w


def deposit_rows(aug, cells_s, w_s, block):
    n = aug.shape[0]
    chunk = min(n, OBS_CHUNK)
    ids = lax.broadcasted_iota(jnp.int32, (CELL_BLOCK, chunk), 0).astype(jnp.float32)
    ids = ids.astype(jnp.bfloat16)
    base = block * CELL_BLOCK
    total = jnp.zeros((CELL_BLOCK, aug.shape[1]), jnp.float32)
    for start in range(0, n, chunk):
        rel = cells_s[:, start : start + chunk] - base
        rel = jnp.where((rel >= 0) & (rel < CELL_BLOCK), rel, -1).astype(jnp.float32)
        w = w_s[:, start : start + chunk].astype(jnp.bfloat16)
        table = jnp.where(rel.astype(jnp.bfloat16) == ids, w, jnp.zeros((), jnp.bfloat16))
        total = total + jnp.dot(table, aug[start : start + chunk, :], preferred_element_type=jnp.float32)
    return total


def sat_kernel(v_ref, c_ref, o_ref, tbl, out, aug, cells_s, w_s):
    block = pl.program_id(0)

    @pl.when(block == 0)
    def _():
        n, d_in = v_ref.shape
        aug[:, :d_in] = v_ref[...]
        aug[:, d_in:] = jnp.ones((n, aug.shape[1] - d_in), jnp.bfloat16)
        cells_s[...] = c_ref[...]
        w_s[...] = lookup(o_ref[...], tbl, 0)

    out[...] = deposit_rows(aug, cells_s, w_s, block)


def station_kernel(capacity, acc, got, tbl, embed, out, aug, cells_s, w_s):
    block = pl.program_id(0)
    d_in = out.shape[1]

    @pl.when(block == 0)
    def _():
        bands = got.shape[0]
        aug[:, d_in:] = jnp.ones((aug.shape[0], aug.shape[1] - d_in), jnp.bfloat16)
        for t in range(bands):
            aug[t * capacity : (t + 1) * capacity, :d_in] = got[t, :capacity, :]
            meta = got[t, capacity : capacity + 6, :].astype(jnp.float32).astype(jnp.int32)
            for h in range(2):
                at = slice(t * capacity + h * d_in, t * capacity + (h + 1) * d_in)
                cells_s[:, at] = meta[h : h + 1] * 64 + meta[2 + h : 3 + h]
                w_s[:, at] = lookup(meta[4 + h : 5 + h], tbl, 1)

    total = acc[...] + deposit_rows(aug, cells_s, w_s, block)
    sums = total[:, :d_in]
    density = total[:, d_in:]
    grid = sums / jnp.maximum(density, 1.0) + density * embed[...]
    out[...] = grid.astype(out.dtype)


def whole(shape):
    return pl.BlockSpec(shape, lambda c: (0,) * len(shape))


SMEM = pl.BlockSpec(memory_space=pltpu.SMEM)


def sat_deposit(values, cells, offsets, table, total_cells):
    n, d_in = values.shape
    wide = 2 * d_in
    return pl.pallas_call(
        sat_kernel,
        grid=(total_cells // CELL_BLOCK,),
        in_specs=[whole((n, d_in)), whole((1, n)), whole((1, n)), SMEM],
        out_specs=pl.BlockSpec((CELL_BLOCK, wide), lambda c: (c, 0)),
        out_shape=jax.ShapeDtypeStruct((total_cells, wide), jnp.float32),
        scratch_shapes=[
            pltpu.VMEM((n, wide), jnp.bfloat16),
            pltpu.VMEM((1, n), jnp.int32),
            pltpu.VMEM((1, n), jnp.float32),
        ],
        cost_estimate=pl.CostEstimate(
            flops=2 * total_cells * n * wide, transcendentals=0, bytes_accessed=2 * n * (d_in + 4)
        ),
    )(values, cells.reshape(1, n), offsets.reshape(1, n), table)


def station_deposit(acc, got, table, embed, capacity, total_cells):
    bands, rows, d_in = got.shape
    n = bands * capacity
    wide = 2 * d_in
    return pl.pallas_call(
        functools.partial(station_kernel, capacity),
        grid=(total_cells // CELL_BLOCK,),
        in_specs=[
            pl.BlockSpec((CELL_BLOCK, wide), lambda c: (c, 0)),
            whole((bands, rows, d_in)),
            SMEM,
            whole((1, d_in)),
        ],
        out_specs=pl.BlockSpec((CELL_BLOCK, d_in), lambda c: (c, 0)),
        out_shape=jax.ShapeDtypeStruct((total_cells, d_in), jnp.bfloat16),
        scratch_shapes=[
            pltpu.VMEM((n, wide), jnp.bfloat16),
            pltpu.VMEM((1, n), jnp.int32),
            pltpu.VMEM((1, n), jnp.float32),
        ],
        cost_estimate=pl.CostEstimate(
            flops=2 * total_cells * n * wide, transcendentals=0, bytes_accessed=2 * n * (d_in + 4)
        ),
    )(acc, got, table, embed.reshape(1, d_in))


def strided(padded, weight, bias):
    count, width, chans = padded.shape
    grid = jnp.pad(padded, ((0, 1), (1, 1), (0, 0)))
    parted = grid.reshape((count + 1) // 2, 2, (width + 2) // 2, 2, chans)
    rows = (count - 1) // 2
    cols = width // 2
    total = jnp.zeros((rows * cols, weight.shape[3]), jnp.float32)
    for first in range(3):
        for second in range(3):
            piece = parted[
                first // 2 : first // 2 + rows,
                first % 2,
                second // 2 : second // 2 + cols,
                second % 2,
                :,
            ]
            total = total + jnp.dot(
                piece.reshape(rows * cols, chans),
                weight[first, second],
                preferred_element_type=jnp.float32,
            )
    return jax.nn.gelu(total + bias, approximate=False).reshape(rows, cols, weight.shape[3])


def project(latent, proj_weight):
    flat = jnp.dot(
        latent.reshape(-1, latent.shape[2]), proj_weight, preferred_element_type=jnp.float32
    )
    return flat.astype(jnp.bfloat16).reshape(latent.shape)


def route(obs_values, obs_band, obs_cell, obs_offset, bands):
    obs_rows, d_in = obs_values.shape
    capacity = obs_rows // 8
    slots = bands * capacity
    target = obs_band[:, 0]
    choose = (target[:, None] == jnp.arange(bands, dtype=jnp.int32)[None, :]).astype(jnp.bfloat16)
    earlier = (
        jnp.arange(obs_rows, dtype=jnp.int32)[:, None] > jnp.arange(obs_rows, dtype=jnp.int32)[None, :]
    ).astype(jnp.bfloat16)
    before = jnp.dot(earlier, choose, preferred_element_type=jnp.float32)
    rank = jnp.sum(before * choose.astype(jnp.float32), axis=1).astype(jnp.int32)
    position = target * capacity + rank
    table = (jnp.arange(slots, dtype=jnp.int32)[:, None] == position[None, :]).astype(jnp.bfloat16)
    sent = jnp.dot(table, obs_values, preferred_element_type=jnp.float32).astype(jnp.bfloat16)
    meta = jnp.stack(
        [obs_cell // 64, obs_cell % 64, obs_offset + 1], axis=0
    ).astype(jnp.bfloat16)
    meta_sent = jnp.dot(meta, table.T, preferred_element_type=jnp.float32).astype(jnp.bfloat16)
    meta_sent = meta_sent.reshape(3, bands, capacity).transpose(1, 0, 2)
    meta_sent = meta_sent.reshape(bands, 3 * capacity // d_in, d_in)
    pad = jnp.zeros((bands, META - 3 * capacity // d_in, d_in), jnp.bfloat16)
    packet = jnp.concatenate([sent.reshape(bands, capacity, d_in), meta_sent, pad], axis=1)
    got = lax.all_to_all(packet, "band", split_axis=0, concat_axis=0, tiled=True)
    return got


def body(
    obs_values,
    obs_band,
    obs_cell,
    obs_offset,
    sat_values,
    sat_cell,
    sat_offset,
    density_embed,
    conv1_weight,
    conv1_bias,
    conv2_weight,
    conv2_bias,
    proj_weight,
):
    bands = lax.axis_size("band")
    position_index = lax.axis_index("band")
    d_in = obs_values.shape[1]
    band_cells = LAT_DEV * LON
    table = weights_of(jnp.arange(8, dtype=jnp.int32)).astype(jnp.float32)
    sat_acc = sat_deposit(sat_values, sat_cell, sat_offset, table, band_cells)
    got = route(obs_values, obs_band, obs_cell, obs_offset, bands)
    capacity = obs_values.shape[0] // 8
    grid0 = station_deposit(sat_acc, got, table, density_embed, capacity, band_cells)
    grid0 = grid0.reshape(LAT_DEV, LON, d_in)
    above = passed_along(grid0[-3:], "band", 1)
    hidden1 = strided(jnp.concatenate([above, grid0], axis=0), conv1_weight, conv1_bias)
    keep_rows = (jnp.arange(hidden1.shape[0]) > 0) | (position_index > 0)
    hidden1 = jnp.where(keep_rows[:, None, None], hidden1, 0.0).astype(jnp.bfloat16)
    latent = strided(hidden1, conv2_weight, conv2_bias).astype(jnp.bfloat16)
    mine = project(latent, proj_weight)
    spread = jnp.broadcast_to(mine[None], (bands,) + mine.shape)
    gathered = lax.all_to_all(spread, "band", split_axis=0, concat_axis=0, tiled=True)
    return gathered.reshape((bands * mine.shape[0],) + mine.shape[1:])


def solution(mesh):
    placed = (
        P(("member", "band"), None),
        P(("member", "band"), None),
        P(("member", "band")),
        P(("member", "band")),
        P(("member", "band"), None),
        P(("member", "band")),
        P(("member", "band")),
        P(),
        P(),
        P(),
        P(),
        P(),
        P(),
    )
    return jax.shard_map(
        body, mesh=mesh, in_specs=placed, out_specs=P("member", None, None), check_vma=False
    )
```

```python
import functools

import jax
import jax.numpy as jnp
from jax import lax
from jax.experimental import pallas as pl
from jax.experimental.pallas import tpu as pltpu
from jax.sharding import PartitionSpec as P

LAT_DEV = 8
LON = 256
META = 16


def passed_along(value, axis, by):
    length = lax.axis_size(axis)
    pairs = [(i, i + by) for i in range(length) if 0 <= i + by < length]
    return lax.ppermute(value, axis, pairs)


def weights_of(offsets):
    return jnp.exp(-offsets.astype(jnp.float32) ** 2 / 32.0).astype(jnp.bfloat16)


CELL_BLOCK = 256
OBS_CHUNK = 2048


def lookup(codes, table, shift):
    w = jnp.zeros(codes.shape, jnp.float32)
    for j in range(8):
        w = jnp.where(codes == j + shift, table[j], w)
    return w


def deposit_rows(aug, cells_s, w_s, block):
    n = aug.shape[0]
    chunk = min(n, OBS_CHUNK)
    ids = lax.broadcasted_iota(jnp.int32, (CELL_BLOCK, chunk), 0).astype(jnp.float32)
    ids = ids.astype(jnp.bfloat16)
    base = block * CELL_BLOCK
    total = jnp.zeros((CELL_BLOCK, aug.shape[1]), jnp.float32)
    for start in range(0, n, chunk):
        rel = cells_s[:, start : start + chunk] - base
        rel = jnp.where((rel >= 0) & (rel < CELL_BLOCK), rel, -1).astype(jnp.float32)
        w = w_s[:, start : start + chunk].astype(jnp.bfloat16)
        table = jnp.where(rel.astype(jnp.bfloat16) == ids, w, jnp.zeros((), jnp.bfloat16))
        total = total + jnp.dot(table, aug[start : start + chunk, :], preferred_element_type=jnp.float32)
    return total


def sat_kernel(v_ref, c_ref, o_ref, tbl, out, aug, cells_s, w_s):
    block = pl.program_id(0)

    @pl.when(block == 0)
    def _():
        n, d_in = v_ref.shape
        aug[:, :d_in] = v_ref[...]
        aug[:, d_in:] = jnp.ones((n, aug.shape[1] - d_in), jnp.bfloat16)
        cells_s[...] = c_ref[...]
        w_s[...] = lookup(o_ref[...], tbl, 0)

    out[...] = deposit_rows(aug, cells_s, w_s, block)


def station_kernel(capacity, acc, got, tbl, embed, out, aug, cells_s, w_s):
    block = pl.program_id(0)
    d_in = out.shape[1]

    @pl.when(block == 0)
    def _():
        bands = got.shape[0]
        aug[:, d_in:] = jnp.ones((aug.shape[0], aug.shape[1] - d_in), jnp.bfloat16)
        for t in range(bands):
            aug[t * capacity : (t + 1) * capacity, :d_in] = got[t, :capacity, :]
            meta = got[t, capacity : capacity + 6, :].astype(jnp.float32).astype(jnp.int32)
            for h in range(2):
                at = slice(t * capacity + h * d_in, t * capacity + (h + 1) * d_in)
                cells_s[:, at] = meta[h : h + 1] * 64 + meta[2 + h : 3 + h]
                w_s[:, at] = lookup(meta[4 + h : 5 + h], tbl, 1)

    total = acc[...] + deposit_rows(aug, cells_s, w_s, block)
    sums = total[:, :d_in]
    density = total[:, d_in:]
    grid = sums / jnp.maximum(density, 1.0) + density * embed[...]
    out[...] = grid.astype(out.dtype)


def whole(shape):
    return pl.BlockSpec(shape, lambda c: (0,) * len(shape))


SMEM = pl.BlockSpec(memory_space=pltpu.SMEM)


def sat_deposit(values, cells, offsets, table, total_cells):
    n, d_in = values.shape
    wide = 2 * d_in
    return pl.pallas_call(
        sat_kernel,
        grid=(total_cells // CELL_BLOCK,),
        in_specs=[whole((n, d_in)), whole((1, n)), whole((1, n)), SMEM],
        out_specs=pl.BlockSpec((CELL_BLOCK, wide), lambda c: (c, 0)),
        out_shape=jax.ShapeDtypeStruct((total_cells, wide), jnp.float32),
        scratch_shapes=[
            pltpu.VMEM((n, wide), jnp.bfloat16),
            pltpu.VMEM((1, n), jnp.int32),
            pltpu.VMEM((1, n), jnp.float32),
        ],
        cost_estimate=pl.CostEstimate(
            flops=2 * total_cells * n * wide, transcendentals=0, bytes_accessed=2 * n * (d_in + 4)
        ),
    )(values, cells.reshape(1, n), offsets.reshape(1, n), table)


def station_deposit(acc, got, table, embed, capacity, total_cells):
    bands, rows, d_in = got.shape
    n = bands * capacity
    wide = 2 * d_in
    return pl.pallas_call(
        functools.partial(station_kernel, capacity),
        grid=(total_cells // CELL_BLOCK,),
        in_specs=[
            pl.BlockSpec((CELL_BLOCK, wide), lambda c: (c, 0)),
            whole((bands, rows, d_in)),
            SMEM,
            whole((1, d_in)),
        ],
        out_specs=pl.BlockSpec((CELL_BLOCK, d_in), lambda c: (c, 0)),
        out_shape=jax.ShapeDtypeStruct((total_cells, d_in), jnp.bfloat16),
        scratch_shapes=[
            pltpu.VMEM((n, wide), jnp.bfloat16),
            pltpu.VMEM((1, n), jnp.int32),
            pltpu.VMEM((1, n), jnp.float32),
        ],
        cost_estimate=pl.CostEstimate(
            flops=2 * total_cells * n * wide, transcendentals=0, bytes_accessed=2 * n * (d_in + 4)
        ),
    )(acc, got, table, embed.reshape(1, d_in))


def pick(scratch, value, start):
    rows, cols = value.shape
    lanes = scratch.shape[2]
    parts = []
    for k in range(cols // lanes):
        scratch[k, :rows, :] = value[:, k * lanes : (k + 1) * lanes]
        parts.append(scratch[k, pl.ds(start, rows // 2, stride=2), :])
    return parts[0] if len(parts) == 1 else jnp.concatenate(parts, axis=1)


def shifted_odd(scratch, value, period):
    odd = pick(scratch, value, 1)
    odd = pltpu.roll(odd, 1, 0)
    first = lax.broadcasted_iota(jnp.int32, odd.shape, 0) % period == 0
    return jnp.where(first, 0.0, odd)


def conv_taps(source, rows, width, weights):
    taps = []
    for e in range(3):
        total = None
        for a in range(3):
            piece = source[pl.ds(a, rows, stride=2)].reshape(rows * width, source.shape[2])
            part = jnp.dot(piece, weights[a, e], preferred_element_type=jnp.float32)
            total = part if total is None else total + part
        taps.append(total)
    return taps


def gelu(x):
    return 0.5 * x * (1.0 + lax.erf(x * 0.7071067811865476))


def conv_kernel(above, grid0, w1, b1, w2, b2, wp, out, xs, s1, h1, s2):
    lat, width, d_in = grid0.shape
    halo = above.shape[0]
    xs[:halo] = above[...]
    xs[halo:] = grid0[...]
    rows1 = (halo + lat - 1) // 2
    half = width // 2
    taps = conv_taps(xs, rows1, width, w1)
    pre1 = pick(s1, taps[1], 0) + pick(s1, taps[2], 1) + shifted_odd(s1, taps[0], half) + b1[...]
    hid = gelu(pre1)
    keep = (lax.broadcasted_iota(jnp.int32, hid.shape, 0) >= half) | (lax.axis_index("band") > 0)
    hid = jnp.where(keep, hid, 0.0).astype(jnp.bfloat16)
    h1[...] = hid.reshape(rows1, half, d_in)
    rows2 = (rows1 - 1) // 2
    quarter = half // 2
    taps = conv_taps(h1, rows2, half, w2)
    pre2 = pick(s2, taps[1], 0) + pick(s2, taps[2], 1) + shifted_odd(s2, taps[0], quarter) + b2[...]
    latent = gelu(pre2).astype(jnp.bfloat16)
    flat = jnp.dot(latent, wp[...], preferred_element_type=jnp.float32)
    out[...] = flat.astype(out.dtype).reshape(out.shape)


def convolve(above, grid0, w1, b1, w2, b2, wp):
    lat, width, d_in = grid0.shape
    halo = above.shape[0]
    d_lat = w2.shape[3]
    rows1 = (halo + lat - 1) // 2
    rows2 = (rows1 - 1) // 2
    vmem = pl.BlockSpec(memory_space=pltpu.VMEM)
    return pl.pallas_call(
        conv_kernel,
        in_specs=[vmem] * 7,
        out_specs=vmem,
        out_shape=jax.ShapeDtypeStruct((rows2, width // 4, d_lat), jnp.bfloat16),
        scratch_shapes=[
            pltpu.VMEM((halo + lat, width, d_in), jnp.bfloat16),
            pltpu.VMEM((1, rows1 * width, 128), jnp.float32),
            pltpu.VMEM((rows1, width // 2, d_in), jnp.bfloat16),
            pltpu.VMEM((d_lat // 128, rows2 * width // 2, 128), jnp.float32),
        ],
    )(above, grid0, w1, b1.reshape(1, -1), w2, b2.reshape(1, -1), wp)


def route(obs_values, obs_band, obs_cell, obs_offset, bands):
    obs_rows, d_in = obs_values.shape
    capacity = obs_rows // 8
    slots = bands * capacity
    target = obs_band[:, 0]
    choose = (target[:, None] == jnp.arange(bands, dtype=jnp.int32)[None, :]).astype(jnp.bfloat16)
    earlier = (
        jnp.arange(obs_rows, dtype=jnp.int32)[:, None] > jnp.arange(obs_rows, dtype=jnp.int32)[None, :]
    ).astype(jnp.bfloat16)
    before = jnp.dot(earlier, choose, preferred_element_type=jnp.float32)
    rank = jnp.sum(before * choose.astype(jnp.float32), axis=1).astype(jnp.int32)
    position = target * capacity + rank
    table = (jnp.arange(slots, dtype=jnp.int32)[:, None] == position[None, :]).astype(jnp.bfloat16)
    sent = jnp.dot(table, obs_values, preferred_element_type=jnp.float32).astype(jnp.bfloat16)
    meta = jnp.stack(
        [obs_cell // 64, obs_cell % 64, obs_offset + 1], axis=0
    ).astype(jnp.bfloat16)
    meta_sent = jnp.dot(meta, table.T, preferred_element_type=jnp.float32).astype(jnp.bfloat16)
    meta_sent = meta_sent.reshape(3, bands, capacity).transpose(1, 0, 2)
    meta_sent = meta_sent.reshape(bands, 3 * capacity // d_in, d_in)
    pad = jnp.zeros((bands, META - 3 * capacity // d_in, d_in), jnp.bfloat16)
    packet = jnp.concatenate([sent.reshape(bands, capacity, d_in), meta_sent, pad], axis=1)
    got = lax.all_to_all(packet, "band", split_axis=0, concat_axis=0, tiled=True)
    return got


def body(
    obs_values,
    obs_band,
    obs_cell,
    obs_offset,
    sat_values,
    sat_cell,
    sat_offset,
    density_embed,
    conv1_weight,
    conv1_bias,
    conv2_weight,
    conv2_bias,
    proj_weight,
):
    bands = lax.axis_size("band")
    position_index = lax.axis_index("band")
    d_in = obs_values.shape[1]
    band_cells = LAT_DEV * LON
    table = weights_of(jnp.arange(8, dtype=jnp.int32)).astype(jnp.float32)
    sat_acc = sat_deposit(sat_values, sat_cell, sat_offset, table, band_cells)
    got = route(obs_values, obs_band, obs_cell, obs_offset, bands)
    capacity = obs_values.shape[0] // 8
    grid0 = station_deposit(sat_acc, got, table, density_embed, capacity, band_cells)
    grid0 = grid0.reshape(LAT_DEV, LON, d_in)
    above = passed_along(grid0[-3:], "band", 1)
    mine = convolve(above, grid0, conv1_weight, conv1_bias, conv2_weight, conv2_bias, proj_weight)
    spread = jnp.broadcast_to(mine[None], (bands,) + mine.shape)
    gathered = lax.all_to_all(spread, "band", split_axis=0, concat_axis=0, tiled=True)
    return gathered.reshape((bands * mine.shape[0],) + mine.shape[1:])


def solution(mesh):
    placed = (
        P(("member", "band"), None),
        P(("member", "band"), None),
        P(("member", "band")),
        P(("member", "band")),
        P(("member", "band"), None),
        P(("member", "band")),
        P(("member", "band")),
        P(),
        P(),
        P(),
        P(),
        P(),
        P(),
    )
    return jax.shard_map(
        body, mesh=mesh, in_specs=placed, out_specs=P("member", None, None), check_vma=False
    )
```

```python
import functools

import jax
import jax.numpy as jnp
from jax import lax
from jax.experimental import pallas as pl
from jax.experimental.pallas import tpu as pltpu
from jax.sharding import PartitionSpec as P

LAT_DEV = 8
LON = 256
META = 16


def passed_along(value, axis, by):
    length = lax.axis_size(axis)
    pairs = [(i, i + by) for i in range(length) if 0 <= i + by < length]
    return lax.ppermute(value, axis, pairs)


def weights_of(offsets):
    return jnp.exp(-offsets.astype(jnp.float32) ** 2 / 32.0).astype(jnp.bfloat16)


CELL_BLOCK = 256
OBS_CHUNK = 2048


def lookup(codes, table, shift):
    w = jnp.zeros(codes.shape, jnp.float32)
    for j in range(8):
        w = jnp.where(codes == j + shift, table[j], w)
    return w


def deposit_rows(aug, cells_s, w_s, block):
    n = aug.shape[0]
    chunk = min(n, OBS_CHUNK)
    ids = lax.broadcasted_iota(jnp.int32, (CELL_BLOCK, chunk), 0).astype(jnp.float32)
    ids = ids.astype(jnp.bfloat16)
    base = block * CELL_BLOCK
    total = jnp.zeros((CELL_BLOCK, aug.shape[1]), jnp.float32)
    for start in range(0, n, chunk):
        rel = cells_s[:, start : start + chunk] - base
        rel = jnp.where((rel >= 0) & (rel < CELL_BLOCK), rel, -1).astype(jnp.float32)
        w = w_s[:, start : start + chunk].astype(jnp.bfloat16)
        table = jnp.where(rel.astype(jnp.bfloat16) == ids, w, jnp.zeros((), jnp.bfloat16))
        total = total + jnp.dot(table, aug[start : start + chunk, :], preferred_element_type=jnp.float32)
    return total


def sat_kernel(v_ref, c_ref, o_ref, tbl, out, aug, cells_s, w_s):
    block = pl.program_id(0)

    @pl.when(block == 0)
    def _():
        n, d_in = v_ref.shape
        aug[:, :d_in] = v_ref[...]
        aug[:, d_in:] = jnp.ones((n, aug.shape[1] - d_in), jnp.bfloat16)
        cells_s[...] = c_ref[...]
        w_s[...] = lookup(o_ref[...], tbl, 0)

    out[...] = deposit_rows(aug, cells_s, w_s, block)


def station_kernel(capacity, acc, got, tbl, embed, out, aug, cells_s, w_s):
    block = pl.program_id(0)
    d_in = out.shape[1]

    @pl.when(block == 0)
    def _():
        bands = got.shape[0]
        aug[:, d_in:] = jnp.ones((aug.shape[0], aug.shape[1] - d_in), jnp.bfloat16)
        for t in range(bands):
            aug[t * capacity : (t + 1) * capacity, :d_in] = got[t, :capacity, :]
            meta = got[t, capacity : capacity + 6, :].astype(jnp.float32).astype(jnp.int32)
            for h in range(2):
                at = slice(t * capacity + h * d_in, t * capacity + (h + 1) * d_in)
                cells_s[:, at] = meta[h : h + 1] * 64 + meta[2 + h : 3 + h]
                w_s[:, at] = lookup(meta[4 + h : 5 + h], tbl, 1)

    total = acc[...] + deposit_rows(aug, cells_s, w_s, block)
    sums = total[:, :d_in]
    density = total[:, d_in:]
    grid = sums / jnp.maximum(density, 1.0) + density * embed[...]
    out[...] = grid.astype(out.dtype)


def whole(shape):
    return pl.BlockSpec(shape, lambda c: (0,) * len(shape))


SMEM = pl.BlockSpec(memory_space=pltpu.SMEM)


def sat_deposit(values, cells, offsets, table, total_cells):
    n, d_in = values.shape
    wide = 2 * d_in
    return pl.pallas_call(
        sat_kernel,
        grid=(total_cells // CELL_BLOCK,),
        in_specs=[whole((n, d_in)), whole((1, n)), whole((1, n)), SMEM],
        out_specs=pl.BlockSpec((CELL_BLOCK, wide), lambda c: (c, 0)),
        out_shape=jax.ShapeDtypeStruct((total_cells, wide), jnp.float32),
        scratch_shapes=[
            pltpu.VMEM((n, wide), jnp.bfloat16),
            pltpu.VMEM((1, n), jnp.int32),
            pltpu.VMEM((1, n), jnp.float32),
        ],
        cost_estimate=pl.CostEstimate(
            flops=2 * total_cells * n * wide, transcendentals=0, bytes_accessed=2 * n * (d_in + 4)
        ),
    )(values, cells.reshape(1, n), offsets.reshape(1, n), table)


def station_deposit(acc, got, table, embed, capacity, total_cells):
    bands, rows, d_in = got.shape
    n = bands * capacity
    wide = 2 * d_in
    return pl.pallas_call(
        functools.partial(station_kernel, capacity),
        grid=(total_cells // CELL_BLOCK,),
        in_specs=[
            pl.BlockSpec((CELL_BLOCK, wide), lambda c: (c, 0)),
            whole((bands, rows, d_in)),
            SMEM,
            whole((1, d_in)),
        ],
        out_specs=pl.BlockSpec((CELL_BLOCK, d_in), lambda c: (c, 0)),
        out_shape=jax.ShapeDtypeStruct((total_cells, d_in), jnp.bfloat16),
        scratch_shapes=[
            pltpu.VMEM((n, wide), jnp.bfloat16),
            pltpu.VMEM((1, n), jnp.int32),
            pltpu.VMEM((1, n), jnp.float32),
        ],
        cost_estimate=pl.CostEstimate(
            flops=2 * total_cells * n * wide, transcendentals=0, bytes_accessed=2 * n * (d_in + 4)
        ),
    )(acc, got, table, embed.reshape(1, d_in))


def pick(scratch, value, start):
    rows, cols = value.shape
    lanes = scratch.shape[2]
    parts = []
    for k in range(cols // lanes):
        scratch[k, :rows, :] = value[:, k * lanes : (k + 1) * lanes]
        parts.append(scratch[k, pl.ds(start, rows // 2, stride=2), :])
    return parts[0] if len(parts) == 1 else jnp.concatenate(parts, axis=1)


def shifted_odd(scratch, value, period):
    odd = pick(scratch, value, 1)
    odd = pltpu.roll(odd, 1, 0)
    first = lax.broadcasted_iota(jnp.int32, odd.shape, 0) % period == 0
    return jnp.where(first, 0.0, odd)


def conv_taps(source, rows, width, weights):
    taps = []
    for e in range(3):
        total = None
        for a in range(3):
            piece = source[pl.ds(a, rows, stride=2)].reshape(rows * width, source.shape[2])
            part = jnp.dot(piece, weights[a, e], preferred_element_type=jnp.float32)
            total = part if total is None else total + part
        taps.append(total)
    return taps


def gelu(x):
    return 0.5 * x * (1.0 + lax.erf(x * 0.7071067811865476))


def conv_kernel(above, grid0, w1, b1, w2, b2, wp, out, xs, s1, h1, s2):
    lat, width, d_in = grid0.shape
    halo = above.shape[0]
    xs[:halo] = above[...]
    xs[halo:] = grid0[...]
    rows1 = (halo + lat - 1) // 2
    half = width // 2
    taps = conv_taps(xs, rows1, width, w1)
    pre1 = pick(s1, taps[1], 0) + pick(s1, taps[2], 1) + shifted_odd(s1, taps[0], half) + b1[...]
    hid = gelu(pre1)
    keep = (lax.broadcasted_iota(jnp.int32, hid.shape, 0) >= half) | (lax.axis_index("band") > 0)
    hid = jnp.where(keep, hid, 0.0).astype(jnp.bfloat16)
    h1[...] = hid.reshape(rows1, half, d_in)
    rows2 = (rows1 - 1) // 2
    quarter = half // 2
    taps = conv_taps(h1, rows2, half, w2)
    pre2 = pick(s2, taps[1], 0) + pick(s2, taps[2], 1) + shifted_odd(s2, taps[0], quarter) + b2[...]
    latent = gelu(pre2).astype(jnp.bfloat16)
    flat = jnp.dot(latent, wp[...], preferred_element_type=jnp.float32)
    out[...] = flat.astype(out.dtype).reshape(out.shape)


def convolve(above, grid0, w1, b1, w2, b2, wp):
    lat, width, d_in = grid0.shape
    halo = above.shape[0]
    d_lat = w2.shape[3]
    rows1 = (halo + lat - 1) // 2
    rows2 = (rows1 - 1) // 2
    vmem = pl.BlockSpec(memory_space=pltpu.VMEM)
    return pl.pallas_call(
        conv_kernel,
        in_specs=[vmem] * 7,
        out_specs=vmem,
        out_shape=jax.ShapeDtypeStruct((rows2, width // 4, d_lat), jnp.bfloat16),
        scratch_shapes=[
            pltpu.VMEM((halo + lat, width, d_in), jnp.bfloat16),
            pltpu.VMEM((1, rows1 * width, 128), jnp.float32),
            pltpu.VMEM((rows1, width // 2, d_in), jnp.bfloat16),
            pltpu.VMEM((d_lat // 128, rows2 * width // 2, 128), jnp.float32),
        ],
    )(above, grid0, w1, b1.reshape(1, -1), w2, b2.reshape(1, -1), wp)


def prefix_count(mask):
    total = mask
    step = 1
    lanes = lax.broadcasted_iota(jnp.int32, mask.shape, 1)
    while step < mask.shape[1]:
        moved = pltpu.roll(total, step, 1)
        total = total + jnp.where(lanes >= step, moved, 0)
        step *= 2
    return total - mask


def route_kernel(capacity, target, cells, offsets, values, out):
    bands, rows, d_in = out.shape
    n = values.shape[0]
    t = target[...]
    band_ids = lax.broadcasted_iota(jnp.int32, (bands, n), 0)
    mask = (t == band_ids).astype(jnp.int32)
    rank = jnp.sum(mask * prefix_count(mask), axis=0, keepdims=True)
    c = cells[...]
    meta = jnp.concatenate(
        [c // 64, c % 64, offsets[...] + 1, jnp.zeros((5, n), jnp.int32)], axis=0
    ).astype(jnp.float32).astype(jnp.bfloat16)
    slots = lax.broadcasted_iota(jnp.int32, (capacity, n), 0)
    per_row = capacity // d_in
    for b in range(bands):
        mine = jnp.where(t == b, rank, -1)
        table = jnp.where(mine == slots, 1.0, 0.0).astype(jnp.bfloat16)
        out[b, :capacity, :] = jnp.dot(
            table, values[...], preferred_element_type=jnp.float32
        ).astype(out.dtype)
        sent = lax.dot_general(
            meta, table, (((1,), (1,)), ((), ())), preferred_element_type=jnp.float32
        ).astype(out.dtype)
        for m in range(3):
            for h in range(per_row):
                row = capacity + m * per_row + h
                out[b, row : row + 1, :] = sent[m : m + 1, h * d_in : (h + 1) * d_in]
        out[b, capacity + 3 * per_row :, :] = jnp.zeros((rows - capacity - 3 * per_row, d_in), out.dtype)


def route(obs_values, obs_band, obs_cell, obs_offset, bands):
    obs_rows, d_in = obs_values.shape
    capacity = obs_rows // 8
    vmem = pl.BlockSpec(memory_space=pltpu.VMEM)
    packet = pl.pallas_call(
        functools.partial(route_kernel, capacity),
        in_specs=[vmem] * 4,
        out_specs=vmem,
        out_shape=jax.ShapeDtypeStruct((bands, capacity + META, d_in), jnp.bfloat16),
    )(
        obs_band.reshape(1, obs_rows),
        obs_cell.reshape(1, obs_rows),
        obs_offset.reshape(1, obs_rows),
        obs_values,
    )
    return lax.all_to_all(packet, "band", split_axis=0, concat_axis=0, tiled=True)


def body(
    obs_values,
    obs_band,
    obs_cell,
    obs_offset,
    sat_values,
    sat_cell,
    sat_offset,
    density_embed,
    conv1_weight,
    conv1_bias,
    conv2_weight,
    conv2_bias,
    proj_weight,
):
    bands = lax.axis_size("band")
    position_index = lax.axis_index("band")
    d_in = obs_values.shape[1]
    band_cells = LAT_DEV * LON
    table = weights_of(jnp.arange(8, dtype=jnp.int32)).astype(jnp.float32)
    sat_acc = sat_deposit(sat_values, sat_cell, sat_offset, table, band_cells)
    got = route(obs_values, obs_band, obs_cell, obs_offset, bands)
    capacity = obs_values.shape[0] // 8
    grid0 = station_deposit(sat_acc, got, table, density_embed, capacity, band_cells)
    grid0 = grid0.reshape(LAT_DEV, LON, d_in)
    above = passed_along(grid0[-3:], "band", 1)
    mine = convolve(above, grid0, conv1_weight, conv1_bias, conv2_weight, conv2_bias, proj_weight)
    spread = jnp.broadcast_to(mine[None], (bands,) + mine.shape)
    gathered = lax.all_to_all(spread, "band", split_axis=0, concat_axis=0, tiled=True)
    return gathered.reshape((bands * mine.shape[0],) + mine.shape[1:])


def solution(mesh):
    placed = (
        P(("member", "band"), None),
        P(("member", "band"), None),
        P(("member", "band")),
        P(("member", "band")),
        P(("member", "band"), None),
        P(("member", "band")),
        P(("member", "band")),
        P(),
        P(),
        P(),
        P(),
        P(),
        P(),
    )
    return jax.shard_map(
        body, mesh=mesh, in_specs=placed, out_specs=P("member", None, None), check_vma=False
    )
```

```python
import functools

import jax
import jax.numpy as jnp
from jax import lax
from jax.experimental import pallas as pl
from jax.experimental.pallas import tpu as pltpu
from jax.sharding import PartitionSpec as P

LAT_DEV = 8
LON = 256
META = 16


def passed_along(value, axis, by):
    length = lax.axis_size(axis)
    pairs = [(i, i + by) for i in range(length) if 0 <= i + by < length]
    return lax.ppermute(value, axis, pairs)


def weights_of(offsets):
    return jnp.exp(-offsets.astype(jnp.float32) ** 2 / 32.0).astype(jnp.bfloat16)


CELL_BLOCK = 256
OBS_CHUNK = 2048


def lookup(codes, table, shift):
    w = jnp.zeros(codes.shape, jnp.float32)
    for j in range(8):
        w = jnp.where(codes == j + shift, table[j], w)
    return w


def deposit_rows(aug, cells_s, w_s, block):
    n = aug.shape[0]
    chunk = min(n, OBS_CHUNK)
    ids = lax.broadcasted_iota(jnp.int32, (CELL_BLOCK, chunk), 0).astype(jnp.float32)
    ids = ids.astype(jnp.bfloat16)
    base = block * CELL_BLOCK
    total = jnp.zeros((CELL_BLOCK, aug.shape[1]), jnp.float32)
    for start in range(0, n, chunk):
        rel = cells_s[:, start : start + chunk] - base
        rel = jnp.where((rel >= 0) & (rel < CELL_BLOCK), rel, -1).astype(jnp.float32)
        w = w_s[:, start : start + chunk].astype(jnp.bfloat16)
        table = jnp.where(rel.astype(jnp.bfloat16) == ids, w, jnp.zeros((), jnp.bfloat16))
        total = total + jnp.dot(table, aug[start : start + chunk, :], preferred_element_type=jnp.float32)
    return total


def sat_kernel(v_ref, c_ref, o_ref, tbl, out, aug, cells_s, w_s):
    block = pl.program_id(0)

    @pl.when(block == 0)
    def _():
        n, d_in = v_ref.shape
        aug[:, :d_in] = v_ref[...]
        aug[:, d_in:] = jnp.ones((n, aug.shape[1] - d_in), jnp.bfloat16)
        cells_s[...] = c_ref[...]
        w_s[...] = lookup(o_ref[...], tbl, 0)

    out[...] = deposit_rows(aug, cells_s, w_s, block)


def station_kernel(capacity, first, acc, got, tbl, embed, out, aug, cells_s, w_s):
    step = pl.program_id(0)
    block = step + first
    d_in = out.shape[1]

    @pl.when(step == 0)
    def _():
        bands = got.shape[0]
        aug[:, d_in:] = jnp.ones((aug.shape[0], aug.shape[1] - d_in), jnp.bfloat16)
        for t in range(bands):
            aug[t * capacity : (t + 1) * capacity, :d_in] = got[t, :capacity, :]
            meta = got[t, capacity : capacity + 6, :].astype(jnp.float32).astype(jnp.int32)
            for h in range(2):
                at = slice(t * capacity + h * d_in, t * capacity + (h + 1) * d_in)
                cells_s[:, at] = meta[h : h + 1] * 64 + meta[2 + h : 3 + h]
                w_s[:, at] = lookup(meta[4 + h : 5 + h], tbl, 1)

    total = acc[...] + deposit_rows(aug, cells_s, w_s, block)
    sums = total[:, :d_in]
    density = total[:, d_in:]
    grid = sums / jnp.maximum(density, 1.0) + density * embed[...]
    out[...] = grid.astype(out.dtype)


def whole(shape):
    return pl.BlockSpec(shape, lambda c: (0,) * len(shape))


SMEM = pl.BlockSpec(memory_space=pltpu.SMEM)


def sat_deposit(values, cells, offsets, table, total_cells):
    n, d_in = values.shape
    wide = 2 * d_in
    return pl.pallas_call(
        sat_kernel,
        grid=(total_cells // CELL_BLOCK,),
        in_specs=[whole((n, d_in)), whole((1, n)), whole((1, n)), SMEM],
        out_specs=pl.BlockSpec((CELL_BLOCK, wide), lambda c: (c, 0)),
        out_shape=jax.ShapeDtypeStruct((total_cells, wide), jnp.float32),
        scratch_shapes=[
            pltpu.VMEM((n, wide), jnp.bfloat16),
            pltpu.VMEM((1, n), jnp.int32),
            pltpu.VMEM((1, n), jnp.float32),
        ],
        cost_estimate=pl.CostEstimate(
            flops=2 * total_cells * n * wide, transcendentals=0, bytes_accessed=2 * n * (d_in + 4)
        ),
    )(values, cells.reshape(1, n), offsets.reshape(1, n), table)


def station_deposit(acc, got, table, embed, capacity, first, count):
    bands, rows, d_in = got.shape
    n = bands * capacity
    wide = 2 * d_in
    return pl.pallas_call(
        functools.partial(station_kernel, capacity, first),
        grid=(count,),
        in_specs=[
            pl.BlockSpec((CELL_BLOCK, wide), lambda c: (c + first, 0)),
            whole((bands, rows, d_in)),
            SMEM,
            whole((1, d_in)),
        ],
        out_specs=pl.BlockSpec((CELL_BLOCK, d_in), lambda c: (c, 0)),
        out_shape=jax.ShapeDtypeStruct((count * CELL_BLOCK, d_in), jnp.bfloat16),
        scratch_shapes=[
            pltpu.VMEM((n, wide), jnp.bfloat16),
            pltpu.VMEM((1, n), jnp.int32),
            pltpu.VMEM((1, n), jnp.float32),
        ],
        cost_estimate=pl.CostEstimate(
            flops=2 * count * CELL_BLOCK * n * wide, transcendentals=0, bytes_accessed=2 * n * (d_in + 4)
        ),
    )(acc, got, table, embed.reshape(1, d_in))


def pick(scratch, value, start):
    rows, cols = value.shape
    lanes = scratch.shape[2]
    parts = []
    for k in range(cols // lanes):
        scratch[k, :rows, :] = value[:, k * lanes : (k + 1) * lanes]
        parts.append(scratch[k, pl.ds(start, rows // 2, stride=2), :])
    return parts[0] if len(parts) == 1 else jnp.concatenate(parts, axis=1)


def shifted_odd(scratch, value, period):
    odd = pick(scratch, value, 1)
    odd = pltpu.roll(odd, 1, 0)
    first = lax.broadcasted_iota(jnp.int32, odd.shape, 0) % period == 0
    return jnp.where(first, 0.0, odd)


def conv_taps(source, rows, width, weights):
    taps = []
    for e in range(3):
        total = None
        for a in range(3):
            piece = source[pl.ds(a, rows, stride=2)].reshape(rows * width, source.shape[2])
            part = jnp.dot(piece, weights[a, e], preferred_element_type=jnp.float32)
            total = part if total is None else total + part
        taps.append(total)
    return taps


def gelu(x):
    return 0.5 * x * (1.0 + lax.erf(x * 0.7071067811865476))


def conv_kernel(above, low, high, w1, b1, w2, b2, wp, out, xs, s1, h1, s2):
    halo, width, d_in = above.shape
    lat = low.shape[0] + high.shape[0]
    xs[:halo] = above[...]
    xs[halo : halo + low.shape[0]] = low[...]
    xs[halo + low.shape[0] :] = high[...]
    rows1 = (halo + lat - 1) // 2
    half = width // 2
    taps = conv_taps(xs, rows1, width, w1)
    pre1 = pick(s1, taps[1], 0) + pick(s1, taps[2], 1) + shifted_odd(s1, taps[0], half) + b1[...]
    hid = gelu(pre1)
    keep = (lax.broadcasted_iota(jnp.int32, hid.shape, 0) >= half) | (lax.axis_index("band") > 0)
    hid = jnp.where(keep, hid, 0.0).astype(jnp.bfloat16)
    h1[...] = hid.reshape(rows1, half, d_in)
    rows2 = (rows1 - 1) // 2
    quarter = half // 2
    taps = conv_taps(h1, rows2, half, w2)
    pre2 = pick(s2, taps[1], 0) + pick(s2, taps[2], 1) + shifted_odd(s2, taps[0], quarter) + b2[...]
    latent = gelu(pre2).astype(jnp.bfloat16)
    flat = jnp.dot(latent, wp[...], preferred_element_type=jnp.float32)
    out[...] = flat.astype(out.dtype).reshape(out.shape)


def convolve(above, low, high, w1, b1, w2, b2, wp):
    halo, width, d_in = above.shape
    lat = low.shape[0] + high.shape[0]
    d_lat = w2.shape[3]
    rows1 = (halo + lat - 1) // 2
    rows2 = (rows1 - 1) // 2
    vmem = pl.BlockSpec(memory_space=pltpu.VMEM)
    return pl.pallas_call(
        conv_kernel,
        in_specs=[vmem] * 8,
        out_specs=vmem,
        out_shape=jax.ShapeDtypeStruct((rows2, width // 4, d_lat), jnp.bfloat16),
        scratch_shapes=[
            pltpu.VMEM((halo + lat, width, d_in), jnp.bfloat16),
            pltpu.VMEM((1, rows1 * width, 128), jnp.float32),
            pltpu.VMEM((rows1, width // 2, d_in), jnp.bfloat16),
            pltpu.VMEM((d_lat // 128, rows2 * width // 2, 128), jnp.float32),
        ],
    )(above, low, high, w1, b1.reshape(1, -1), w2, b2.reshape(1, -1), wp)


def prefix_count(mask):
    total = mask
    step = 1
    lanes = lax.broadcasted_iota(jnp.int32, mask.shape, 1)
    while step < mask.shape[1]:
        moved = pltpu.roll(total, step, 1)
        total = total + jnp.where(lanes >= step, moved, 0)
        step *= 2
    return total - mask


def route_kernel(capacity, target, cells, offsets, values, out):
    bands, rows, d_in = out.shape
    n = values.shape[0]
    t = target[...]
    band_ids = lax.broadcasted_iota(jnp.int32, (bands, n), 0)
    mask = (t == band_ids).astype(jnp.int32)
    rank = jnp.sum(mask * prefix_count(mask), axis=0, keepdims=True)
    c = cells[...]
    meta = jnp.concatenate(
        [c // 64, c % 64, offsets[...] + 1, jnp.zeros((5, n), jnp.int32)], axis=0
    ).astype(jnp.float32).astype(jnp.bfloat16)
    slots = lax.broadcasted_iota(jnp.int32, (capacity, n), 0)
    per_row = capacity // d_in
    for b in range(bands):
        mine = jnp.where(t == b, rank, -1)
        table = jnp.where(mine == slots, 1.0, 0.0).astype(jnp.bfloat16)
        out[b, :capacity, :] = jnp.dot(
            table, values[...], preferred_element_type=jnp.float32
        ).astype(out.dtype)
        sent = lax.dot_general(
            meta, table, (((1,), (1,)), ((), ())), preferred_element_type=jnp.float32
        ).astype(out.dtype)
        for m in range(3):
            for h in range(per_row):
                row = capacity + m * per_row + h
                out[b, row : row + 1, :] = sent[m : m + 1, h * d_in : (h + 1) * d_in]
        out[b, capacity + 3 * per_row :, :] = jnp.zeros((rows - capacity - 3 * per_row, d_in), out.dtype)


def route(obs_values, obs_band, obs_cell, obs_offset, bands):
    obs_rows, d_in = obs_values.shape
    capacity = obs_rows // 8
    vmem = pl.BlockSpec(memory_space=pltpu.VMEM)
    packet = pl.pallas_call(
        functools.partial(route_kernel, capacity),
        in_specs=[vmem] * 4,
        out_specs=vmem,
        out_shape=jax.ShapeDtypeStruct((bands, capacity + META, d_in), jnp.bfloat16),
    )(
        obs_band.reshape(1, obs_rows),
        obs_cell.reshape(1, obs_rows),
        obs_offset.reshape(1, obs_rows),
        obs_values,
    )
    return lax.all_to_all(packet, "band", split_axis=0, concat_axis=0, tiled=True)


def body(
    obs_values,
    obs_band,
    obs_cell,
    obs_offset,
    sat_values,
    sat_cell,
    sat_offset,
    density_embed,
    conv1_weight,
    conv1_bias,
    conv2_weight,
    conv2_bias,
    proj_weight,
):
    bands = lax.axis_size("band")
    position_index = lax.axis_index("band")
    d_in = obs_values.shape[1]
    band_cells = LAT_DEV * LON
    table = weights_of(jnp.arange(8, dtype=jnp.int32)).astype(jnp.float32)
    sat_acc = sat_deposit(sat_values, sat_cell, sat_offset, table, band_cells)
    got = route(obs_values, obs_band, obs_cell, obs_offset, bands)
    capacity = obs_values.shape[0] // 8
    halo = 3
    lat_blocks = band_cells // CELL_BLOCK
    rows_per_block = CELL_BLOCK // LON
    high = station_deposit(
        sat_acc, got, table, density_embed, capacity, lat_blocks - halo // rows_per_block, halo // rows_per_block
    ).reshape(halo, LON, d_in)
    above = passed_along(high, "band", 1)
    low = station_deposit(
        sat_acc, got, table, density_embed, capacity, 0, lat_blocks - halo // rows_per_block
    ).reshape(LAT_DEV - halo, LON, d_in)
    mine = convolve(above, low, high, conv1_weight, conv1_bias, conv2_weight, conv2_bias, proj_weight)
    spread = jnp.broadcast_to(mine[None], (bands,) + mine.shape)
    gathered = lax.all_to_all(spread, "band", split_axis=0, concat_axis=0, tiled=True)
    return gathered.reshape((bands * mine.shape[0],) + mine.shape[1:])


def solution(mesh):
    placed = (
        P(("member", "band"), None),
        P(("member", "band"), None),
        P(("member", "band")),
        P(("member", "band")),
        P(("member", "band"), None),
        P(("member", "band")),
        P(("member", "band")),
        P(),
        P(),
        P(),
        P(),
        P(),
        P(),
    )
    return jax.shard_map(
        body, mesh=mesh, in_specs=placed, out_specs=P("member", None, None), check_vma=False
    )
```

```python
import functools

import jax
import jax.numpy as jnp
from jax import lax
from jax.experimental import pallas as pl
from jax.experimental.pallas import tpu as pltpu
from jax.sharding import PartitionSpec as P

LAT_DEV = 8
LON = 256
META = 16


def passed_along(value, axis, by):
    length = lax.axis_size(axis)
    pairs = [(i, i + by) for i in range(length) if 0 <= i + by < length]
    return lax.ppermute(value, axis, pairs)


def weights_of(offsets):
    return jnp.exp(-offsets.astype(jnp.float32) ** 2 / 32.0).astype(jnp.bfloat16)


CELL_BLOCK = 256
OBS_CHUNK = 2048


def lookup(codes, table, shift):
    w = jnp.zeros(codes.shape, jnp.float32)
    for j in range(8):
        w = jnp.where(codes == j + shift, table[j], w)
    return w


def deposit_rows(aug, cells_s, w_s, block):
    n = aug.shape[0]
    chunk = min(n, OBS_CHUNK)
    ids = lax.broadcasted_iota(jnp.int32, (CELL_BLOCK, chunk), 0).astype(jnp.float32)
    ids = ids.astype(jnp.bfloat16)
    base = block * CELL_BLOCK
    total = jnp.zeros((CELL_BLOCK, aug.shape[1]), jnp.float32)
    for start in range(0, n, chunk):
        rel = cells_s[:, start : start + chunk] - base
        rel = jnp.where((rel >= 0) & (rel < CELL_BLOCK), rel, -1).astype(jnp.float32)
        w = w_s[:, start : start + chunk].astype(jnp.bfloat16)
        table = jnp.where(rel.astype(jnp.bfloat16) == ids, w, jnp.zeros((), jnp.bfloat16))
        total = total + jnp.dot(table, aug[start : start + chunk, :], preferred_element_type=jnp.float32)
    return total


def sat_kernel(v_ref, c_ref, o_ref, tbl, out, aug, cells_s, w_s):
    block = pl.program_id(0)

    @pl.when(block == 0)
    def _():
        n, d_in = v_ref.shape
        aug[:, :d_in] = v_ref[...]
        aug[:, d_in:] = jnp.ones((n, aug.shape[1] - d_in), jnp.bfloat16)
        cells_s[...] = c_ref[...]
        w_s[...] = lookup(o_ref[...], tbl, 0)

    out[...] = deposit_rows(aug, cells_s, w_s, block)


def station_kernel(capacity, first, acc, got, tbl, embed, out, aug, cells_s, w_s):
    step = pl.program_id(0)
    block = step + first
    d_in = out.shape[1]

    @pl.when(step == 0)
    def _():
        bands = got.shape[0]
        aug[:, d_in:] = jnp.ones((aug.shape[0], aug.shape[1] - d_in), jnp.bfloat16)
        for t in range(bands):
            aug[t * capacity : (t + 1) * capacity, :d_in] = got[t, :capacity, :]
            meta = got[t, capacity : capacity + 6, :].astype(jnp.float32).astype(jnp.int32)
            for h in range(2):
                at = slice(t * capacity + h * d_in, t * capacity + (h + 1) * d_in)
                cells_s[:, at] = meta[h : h + 1] * 64 + meta[2 + h : 3 + h]
                w_s[:, at] = lookup(meta[4 + h : 5 + h], tbl, 1)

    total = acc[...] + deposit_rows(aug, cells_s, w_s, block)
    sums = total[:, :d_in]
    density = total[:, d_in:]
    grid = sums / jnp.maximum(density, 1.0) + density * embed[...]
    out[...] = grid.astype(out.dtype)


def whole(shape):
    return pl.BlockSpec(shape, lambda c: (0,) * len(shape))


SMEM = pl.BlockSpec(memory_space=pltpu.SMEM)


def sat_deposit(values, cells, offsets, table, total_cells):
    n, d_in = values.shape
    wide = 2 * d_in
    return pl.pallas_call(
        sat_kernel,
        grid=(total_cells // CELL_BLOCK,),
        in_specs=[whole((n, d_in)), whole((1, n)), whole((1, n)), SMEM],
        out_specs=pl.BlockSpec((CELL_BLOCK, wide), lambda c: (c, 0)),
        out_shape=jax.ShapeDtypeStruct((total_cells, wide), jnp.float32),
        scratch_shapes=[
            pltpu.VMEM((n, wide), jnp.bfloat16),
            pltpu.VMEM((1, n), jnp.int32),
            pltpu.VMEM((1, n), jnp.float32),
        ],
        cost_estimate=pl.CostEstimate(
            flops=2 * total_cells * n * wide, transcendentals=0, bytes_accessed=2 * n * (d_in + 4)
        ),
    )(values, cells.reshape(1, n), offsets.reshape(1, n), table)


def station_deposit(acc, got, table, embed, capacity, first, count):
    bands, rows, d_in = got.shape
    n = bands * capacity
    wide = 2 * d_in
    return pl.pallas_call(
        functools.partial(station_kernel, capacity, first),
        grid=(count,),
        in_specs=[
            pl.BlockSpec((CELL_BLOCK, wide), lambda c: (c + first, 0)),
            whole((bands, rows, d_in)),
            SMEM,
            whole((1, d_in)),
        ],
        out_specs=pl.BlockSpec((CELL_BLOCK, d_in), lambda c: (c, 0)),
        out_shape=jax.ShapeDtypeStruct((count * CELL_BLOCK, d_in), jnp.bfloat16),
        scratch_shapes=[
            pltpu.VMEM((n, wide), jnp.bfloat16),
            pltpu.VMEM((1, n), jnp.int32),
            pltpu.VMEM((1, n), jnp.float32),
        ],
        cost_estimate=pl.CostEstimate(
            flops=2 * count * CELL_BLOCK * n * wide, transcendentals=0, bytes_accessed=2 * n * (d_in + 4)
        ),
    )(acc, got, table, embed.reshape(1, d_in))


def pick(scratch, value, start):
    rows, cols = value.shape
    lanes = scratch.shape[2]
    parts = []
    for k in range(cols // lanes):
        scratch[k, :rows, :] = value[:, k * lanes : (k + 1) * lanes]
        parts.append(scratch[k, pl.ds(start, rows // 2, stride=2), :])
    return parts[0] if len(parts) == 1 else jnp.concatenate(parts, axis=1)


def shifted_odd(scratch, value, period):
    odd = pick(scratch, value, 1)
    odd = pltpu.roll(odd, 1, 0)
    first = lax.broadcasted_iota(jnp.int32, odd.shape, 0) % period == 0
    return jnp.where(first, 0.0, odd)


def conv_taps(source, rows, width, weights):
    taps = []
    for e in range(3):
        total = None
        for a in range(3):
            piece = source[pl.ds(a, rows, stride=2)].reshape(rows * width, source.shape[2])
            part = jnp.dot(piece, weights[a, e], preferred_element_type=jnp.float32)
            total = part if total is None else total + part
        taps.append(total)
    return taps


def gelu(x):
    return 0.5 * x * (1.0 + lax.erf(x * 0.7071067811865476))


def conv_kernel(above, low, high, w1, b1, w2, b2, wp, out, xs, s1, h1, s2):
    halo, width, d_in = above.shape
    lat = low.shape[0] + high.shape[0]
    xs[:halo] = above[...]
    xs[halo : halo + low.shape[0]] = low[...]
    xs[halo + low.shape[0] :] = high[...]
    rows1 = (halo + lat - 1) // 2
    half = width // 2
    taps = conv_taps(xs, rows1, width, w1)
    pre1 = pick(s1, taps[1], 0) + pick(s1, taps[2], 1) + shifted_odd(s1, taps[0], half) + b1[...]
    hid = gelu(pre1)
    keep = (lax.broadcasted_iota(jnp.int32, hid.shape, 0) >= half) | (lax.axis_index("band") > 0)
    hid = jnp.where(keep, hid, 0.0).astype(jnp.bfloat16)
    h1[...] = hid.reshape(rows1, half, d_in)
    rows2 = (rows1 - 1) // 2
    quarter = half // 2
    taps = conv_taps(h1, rows2, half, w2)
    pre2 = pick(s2, taps[1], 0) + pick(s2, taps[2], 1) + shifted_odd(s2, taps[0], quarter) + b2[...]
    latent = gelu(pre2).astype(jnp.bfloat16)
    flat = jnp.dot(latent, wp[...], preferred_element_type=jnp.float32)
    flat = flat.astype(out.dtype).reshape(out.shape[1:])
    for b in range(out.shape[0]):
        out[b] = flat


def convolve(bands, above, low, high, w1, b1, w2, b2, wp):
    halo, width, d_in = above.shape
    lat = low.shape[0] + high.shape[0]
    d_lat = w2.shape[3]
    rows1 = (halo + lat - 1) // 2
    rows2 = (rows1 - 1) // 2
    vmem = pl.BlockSpec(memory_space=pltpu.VMEM)
    return pl.pallas_call(
        conv_kernel,
        in_specs=[vmem] * 8,
        out_specs=vmem,
        out_shape=jax.ShapeDtypeStruct((bands, rows2, width // 4, d_lat), jnp.bfloat16),
        scratch_shapes=[
            pltpu.VMEM((halo + lat, width, d_in), jnp.bfloat16),
            pltpu.VMEM((1, rows1 * width, 128), jnp.float32),
            pltpu.VMEM((rows1, width // 2, d_in), jnp.bfloat16),
            pltpu.VMEM((d_lat // 128, rows2 * width // 2, 128), jnp.float32),
        ],
    )(above, low, high, w1, b1.reshape(1, -1), w2, b2.reshape(1, -1), wp)


def prefix_count(mask):
    total = mask
    step = 1
    lanes = lax.broadcasted_iota(jnp.int32, mask.shape, 1)
    while step < mask.shape[1]:
        moved = pltpu.roll(total, step, 1)
        total = total + jnp.where(lanes >= step, moved, 0)
        step *= 2
    return total - mask


def route_kernel(capacity, target, cells, offsets, values, out):
    bands, rows, d_in = out.shape
    n = values.shape[0]
    t = target[...]
    band_ids = lax.broadcasted_iota(jnp.int32, (bands, n), 0)
    mask = (t == band_ids).astype(jnp.int32)
    rank = jnp.sum(mask * prefix_count(mask), axis=0, keepdims=True)
    c = cells[...]
    meta = jnp.concatenate(
        [c // 64, c % 64, offsets[...] + 1, jnp.zeros((5, n), jnp.int32)], axis=0
    ).astype(jnp.float32).astype(jnp.bfloat16)
    slots = lax.broadcasted_iota(jnp.int32, (capacity, n), 0).astype(jnp.float32).astype(jnp.bfloat16)
    per_row = capacity // d_in
    one = jnp.ones((), jnp.bfloat16)
    zero = jnp.zeros((), jnp.bfloat16)
    for b in range(bands):
        mine = jnp.where(t == b, rank, -1).astype(jnp.float32).astype(jnp.bfloat16)
        table = jnp.where(mine == slots, one, zero)
        out[b, :capacity, :] = jnp.dot(
            table, values[...], preferred_element_type=jnp.float32
        ).astype(out.dtype)
        sent = lax.dot_general(
            meta, table, (((1,), (1,)), ((), ())), preferred_element_type=jnp.float32
        ).astype(out.dtype)
        for m in range(3):
            for h in range(per_row):
                row = capacity + m * per_row + h
                out[b, row : row + 1, :] = sent[m : m + 1, h * d_in : (h + 1) * d_in]
        out[b, capacity + 3 * per_row :, :] = jnp.zeros((rows - capacity - 3 * per_row, d_in), out.dtype)


def route(obs_values, obs_band, obs_cell, obs_offset, bands):
    obs_rows, d_in = obs_values.shape
    capacity = obs_rows // 8
    vmem = pl.BlockSpec(memory_space=pltpu.VMEM)
    packet = pl.pallas_call(
        functools.partial(route_kernel, capacity),
        in_specs=[vmem] * 4,
        out_specs=vmem,
        out_shape=jax.ShapeDtypeStruct((bands, capacity + META, d_in), jnp.bfloat16),
    )(
        obs_band.reshape(1, obs_rows),
        obs_cell.reshape(1, obs_rows),
        obs_offset.reshape(1, obs_rows),
        obs_values,
    )
    return lax.all_to_all(packet, "band", split_axis=0, concat_axis=0, tiled=True)


def body(
    obs_values,
    obs_band,
    obs_cell,
    obs_offset,
    sat_values,
    sat_cell,
    sat_offset,
    density_embed,
    conv1_weight,
    conv1_bias,
    conv2_weight,
    conv2_bias,
    proj_weight,
):
    bands = lax.axis_size("band")
    position_index = lax.axis_index("band")
    d_in = obs_values.shape[1]
    band_cells = LAT_DEV * LON
    table = weights_of(jnp.arange(8, dtype=jnp.int32)).astype(jnp.float32)
    sat_acc = sat_deposit(sat_values, sat_cell, sat_offset, table, band_cells)
    got = route(obs_values, obs_band, obs_cell, obs_offset, bands)
    capacity = obs_values.shape[0] // 8
    halo = 3
    lat_blocks = band_cells // CELL_BLOCK
    rows_per_block = CELL_BLOCK // LON
    high = station_deposit(
        sat_acc, got, table, density_embed, capacity, lat_blocks - halo // rows_per_block, halo // rows_per_block
    ).reshape(halo, LON, d_in)
    above = passed_along(high, "band", 1)
    low = station_deposit(
        sat_acc, got, table, density_embed, capacity, 0, lat_blocks - halo // rows_per_block
    ).reshape(LAT_DEV - halo, LON, d_in)
    spread = convolve(bands, above, low, high, conv1_weight, conv1_bias, conv2_weight, conv2_bias, proj_weight)
    gathered = lax.all_to_all(spread, "band", split_axis=0, concat_axis=0, tiled=True)
    return gathered.reshape((bands * spread.shape[1],) + spread.shape[2:])


def solution(mesh):
    placed = (
        P(("member", "band"), None),
        P(("member", "band"), None),
        P(("member", "band")),
        P(("member", "band")),
        P(("member", "band"), None),
        P(("member", "band")),
        P(("member", "band")),
        P(),
        P(),
        P(),
        P(),
        P(),
        P(),
    )
    return jax.shard_map(
        body, mesh=mesh, in_specs=placed, out_specs=P("member", None, None), check_vma=False
    )
```

```python
import functools

import jax
import jax.numpy as jnp
from jax import lax
from jax.experimental import pallas as pl
from jax.experimental.pallas import tpu as pltpu
from jax.sharding import PartitionSpec as P

LAT_DEV = 8
LON = 256
META = 16


def passed_along(value, axis, by):
    length = lax.axis_size(axis)
    pairs = [(i, i + by) for i in range(length) if 0 <= i + by < length]
    return lax.ppermute(value, axis, pairs)


def weights_of(offsets):
    return jnp.exp(-offsets.astype(jnp.float32) ** 2 / 32.0).astype(jnp.bfloat16)


CELL_BLOCK = 256
OBS_CHUNK = 2048


def lookup(codes, table, shift):
    w = jnp.zeros(codes.shape, jnp.float32)
    for j in range(8):
        w = jnp.where(codes == j + shift, table[j], w)
    return w


def deposit_rows(aug, cells_s, w_s, block):
    n = aug.shape[0]
    chunk = min(n, OBS_CHUNK)
    ids = lax.broadcasted_iota(jnp.int32, (CELL_BLOCK, chunk), 0).astype(jnp.float32)
    ids = ids.astype(jnp.bfloat16)
    base = block * CELL_BLOCK
    total = jnp.zeros((CELL_BLOCK, aug.shape[1]), jnp.float32)
    for start in range(0, n, chunk):
        rel = cells_s[:, start : start + chunk] - base
        rel = jnp.where((rel >= 0) & (rel < CELL_BLOCK), rel, -1).astype(jnp.float32)
        w = w_s[:, start : start + chunk].astype(jnp.bfloat16)
        table = jnp.where(rel.astype(jnp.bfloat16) == ids, w, jnp.zeros((), jnp.bfloat16))
        total = total + jnp.dot(table, aug[start : start + chunk, :], preferred_element_type=jnp.float32)
    return total


def sat_kernel(v_ref, c_ref, o_ref, tbl, out, aug, cells_s, w_s):
    block = pl.program_id(0)

    @pl.when(block == 0)
    def _():
        n, d_in = v_ref.shape
        aug[:, :d_in] = v_ref[...]
        aug[:, d_in:] = jnp.ones((n, aug.shape[1] - d_in), jnp.bfloat16)
        cells_s[...] = c_ref[...]
        w_s[...] = lookup(o_ref[...], tbl, 0)

    out[...] = deposit_rows(aug, cells_s, w_s, block)


def station_kernel(capacity, first, acc, got, tbl, embed, out, aug, cells_s, w_s):
    step = pl.program_id(0)
    block = step + first
    d_in = out.shape[1]

    @pl.when(step == 0)
    def _():
        bands = got.shape[0]
        aug[:, d_in:] = jnp.ones((aug.shape[0], aug.shape[1] - d_in), jnp.bfloat16)
        for t in range(bands):
            aug[t * capacity : (t + 1) * capacity, :d_in] = got[t, :capacity, :]
            meta = got[t, capacity : capacity + 6, :].astype(jnp.float32).astype(jnp.int32)
            for h in range(2):
                at = slice(t * capacity + h * d_in, t * capacity + (h + 1) * d_in)
                cells_s[:, at] = meta[h : h + 1] * 64 + meta[2 + h : 3 + h]
                w_s[:, at] = lookup(meta[4 + h : 5 + h], tbl, 1)

    total = acc[...] + deposit_rows(aug, cells_s, w_s, block)
    sums = total[:, :d_in]
    density = total[:, d_in:]
    grid = sums / jnp.maximum(density, 1.0) + density * embed[...]
    out[...] = grid.astype(out.dtype)


def whole(shape):
    return pl.BlockSpec(shape, lambda c: (0,) * len(shape))


SMEM = pl.BlockSpec(memory_space=pltpu.SMEM)


def sat_deposit(values, cells, offsets, table, total_cells):
    n, d_in = values.shape
    wide = 2 * d_in
    return pl.pallas_call(
        sat_kernel,
        grid=(total_cells // CELL_BLOCK,),
        in_specs=[whole((n, d_in)), whole((1, n)), whole((1, n)), SMEM],
        out_specs=pl.BlockSpec((CELL_BLOCK, wide), lambda c: (c, 0)),
        out_shape=jax.ShapeDtypeStruct((total_cells, wide), jnp.float32),
        scratch_shapes=[
            pltpu.VMEM((n, wide), jnp.bfloat16),
            pltpu.VMEM((1, n), jnp.int32),
            pltpu.VMEM((1, n), jnp.float32),
        ],
        cost_estimate=pl.CostEstimate(
            flops=2 * total_cells * n * wide, transcendentals=0, bytes_accessed=2 * n * (d_in + 4)
        ),
    )(values, cells.reshape(1, n), offsets.reshape(1, n), table)


def station_deposit(acc, got, table, embed, capacity, first, count):
    bands, rows, d_in = got.shape
    n = bands * capacity
    wide = 2 * d_in
    return pl.pallas_call(
        functools.partial(station_kernel, capacity, first),
        grid=(count,),
        in_specs=[
            pl.BlockSpec((CELL_BLOCK, wide), lambda c: (c + first, 0)),
            whole((bands, rows, d_in)),
            SMEM,
            whole((1, d_in)),
        ],
        out_specs=pl.BlockSpec((CELL_BLOCK, d_in), lambda c: (c, 0)),
        out_shape=jax.ShapeDtypeStruct((count * CELL_BLOCK, d_in), jnp.bfloat16),
        scratch_shapes=[
            pltpu.VMEM((n, wide), jnp.bfloat16),
            pltpu.VMEM((1, n), jnp.int32),
            pltpu.VMEM((1, n), jnp.float32),
        ],
        cost_estimate=pl.CostEstimate(
            flops=2 * count * CELL_BLOCK * n * wide, transcendentals=0, bytes_accessed=2 * n * (d_in + 4)
        ),
    )(acc, got, table, embed.reshape(1, d_in))


def pick(scratch, value, start):
    rows, cols = value.shape
    lanes = scratch.shape[2]
    parts = []
    for k in range(cols // lanes):
        scratch[k, :rows, :] = value[:, k * lanes : (k + 1) * lanes]
        parts.append(scratch[k, pl.ds(start, rows // 2, stride=2), :])
    return parts[0] if len(parts) == 1 else jnp.concatenate(parts, axis=1)


def shifted_odd(scratch, value, period):
    odd = pick(scratch, value, 1)
    odd = pltpu.roll(odd, 1, 0)
    first = lax.broadcasted_iota(jnp.int32, odd.shape, 0) % period == 0
    return jnp.where(first, 0.0, odd)


def conv_taps(source, rows, width, weights):
    taps = []
    for e in range(3):
        total = None
        for a in range(3):
            piece = source[pl.ds(a, rows, stride=2)].reshape(rows * width, source.shape[2])
            part = jnp.dot(piece, weights[a, e], preferred_element_type=jnp.float32)
            total = part if total is None else total + part
        taps.append(total)
    return taps


def gelu(x):
    return 0.5 * x * (1.0 + lax.erf(x * 0.7071067811865476))


def conv_kernel(above, low, high, w1, b1, w2, b2, wp, out, xs, s1, h1, s2):
    halo, width, d_in = above.shape
    lat = low.shape[0] + high.shape[0]
    xs[:halo] = above[...]
    xs[halo : halo + low.shape[0]] = low[...]
    xs[halo + low.shape[0] :] = high[...]
    rows1 = (halo + lat - 1) // 2
    half = width // 2
    taps = conv_taps(xs, rows1, width, w1)
    pre1 = pick(s1, taps[1], 0) + pick(s1, taps[2], 1) + shifted_odd(s1, taps[0], half) + b1[...]
    hid = gelu(pre1)
    keep = (lax.broadcasted_iota(jnp.int32, hid.shape, 0) >= half) | (lax.axis_index("band") > 0)
    hid = jnp.where(keep, hid, 0.0).astype(jnp.bfloat16)
    h1[...] = hid.reshape(rows1, half, d_in)
    rows2 = (rows1 - 1) // 2
    quarter = half // 2
    taps = conv_taps(h1, rows2, half, w2)
    pre2 = pick(s2, taps[1], 0) + pick(s2, taps[2], 1) + shifted_odd(s2, taps[0], quarter) + b2[...]
    latent = gelu(pre2).astype(jnp.bfloat16)
    flat = jnp.dot(latent, wp[...], preferred_element_type=jnp.float32)
    flat = flat.astype(out.dtype).reshape(out.shape[1:])
    for b in range(out.shape[0]):
        out[b] = flat


def convolve(bands, above, low, high, w1, b1, w2, b2, wp):
    halo, width, d_in = above.shape
    lat = low.shape[0] + high.shape[0]
    d_lat = w2.shape[3]
    rows1 = (halo + lat - 1) // 2
    rows2 = (rows1 - 1) // 2
    vmem = pl.BlockSpec(memory_space=pltpu.VMEM)
    return pl.pallas_call(
        conv_kernel,
        in_specs=[vmem] * 8,
        out_specs=vmem,
        out_shape=jax.ShapeDtypeStruct((bands, rows2, width // 4, d_lat), jnp.bfloat16),
        scratch_shapes=[
            pltpu.VMEM((halo + lat, width, d_in), jnp.bfloat16),
            pltpu.VMEM((1, rows1 * width, 128), jnp.float32),
            pltpu.VMEM((rows1, width // 2, d_in), jnp.bfloat16),
            pltpu.VMEM((d_lat // 128, rows2 * width // 2, 128), jnp.float32),
        ],
    )(above, low, high, w1, b1.reshape(1, -1), w2, b2.reshape(1, -1), wp)


def prefix_count(mask):
    total = mask
    step = 1
    lanes = lax.broadcasted_iota(jnp.int32, mask.shape, 1)
    while step < mask.shape[1]:
        moved = pltpu.roll(total, step, 1)
        total = total + jnp.where(lanes >= step, moved, 0)
        step *= 2
    return total - mask


def route_kernel(capacity, target, cells, offsets, values, out, vaug):
    bands, rows, d_in = out.shape
    n = values.shape[0]
    t = target[...]
    band_ids = lax.broadcasted_iota(jnp.int32, (bands, n), 0)
    mask = (t == band_ids).astype(jnp.int32)
    rank = jnp.sum(mask * prefix_count(mask), axis=0, keepdims=True)
    c = cells[...]
    vaug[:, :d_in] = values[...]
    vaug[:, d_in:] = jnp.zeros((n, vaug.shape[1] - d_in), jnp.bfloat16)
    codes = (c // 64, c % 64, offsets[...] + 1)
    for m, code in enumerate(codes):
        vaug[:, d_in + m : d_in + m + 1] = code.astype(jnp.float32).astype(jnp.bfloat16)
    slots = lax.broadcasted_iota(jnp.int32, (capacity, n), 0)
    per_row = capacity // d_in
    for b in range(bands):
        mine = jnp.where(t == b, rank, -1)
        table = jnp.where(mine == slots, 1.0, 0.0).astype(jnp.bfloat16)
        res = jnp.dot(table, vaug[...], preferred_element_type=jnp.float32)
        out[b, :capacity, :] = res[:, :d_in].astype(out.dtype)
        sent = jnp.transpose(res[:, d_in:]).astype(out.dtype)
        for m in range(3):
            for h in range(per_row):
                row = capacity + m * per_row + h
                out[b, row : row + 1, :] = sent[m : m + 1, h * d_in : (h + 1) * d_in]
        out[b, capacity + 3 * per_row :, :] = jnp.zeros((rows - capacity - 3 * per_row, d_in), out.dtype)


def route(obs_values, obs_band, obs_cell, obs_offset, bands):
    obs_rows, d_in = obs_values.shape
    capacity = obs_rows // 8
    vmem = pl.BlockSpec(memory_space=pltpu.VMEM)
    packet = pl.pallas_call(
        functools.partial(route_kernel, capacity),
        in_specs=[vmem] * 4,
        out_specs=vmem,
        out_shape=jax.ShapeDtypeStruct((bands, capacity + META, d_in), jnp.bfloat16),
        scratch_shapes=[pltpu.VMEM((obs_rows, 2 * d_in), jnp.bfloat16)],
    )(
        obs_band.reshape(1, obs_rows),
        obs_cell.reshape(obs_rows, 1),
        obs_offset.reshape(obs_rows, 1),
        obs_values,
    )
    return lax.all_to_all(packet, "band", split_axis=0, concat_axis=0, tiled=True)


def body(
    obs_values,
    obs_band,
    obs_cell,
    obs_offset,
    sat_values,
    sat_cell,
    sat_offset,
    density_embed,
    conv1_weight,
    conv1_bias,
    conv2_weight,
    conv2_bias,
    proj_weight,
):
    bands = lax.axis_size("band")
    position_index = lax.axis_index("band")
    d_in = obs_values.shape[1]
    band_cells = LAT_DEV * LON
    table = weights_of(jnp.arange(8, dtype=jnp.int32)).astype(jnp.float32)
    sat_acc = sat_deposit(sat_values, sat_cell, sat_offset, table, band_cells)
    got = route(obs_values, obs_band, obs_cell, obs_offset, bands)
    capacity = obs_values.shape[0] // 8
    halo = 3
    lat_blocks = band_cells // CELL_BLOCK
    rows_per_block = CELL_BLOCK // LON
    high = station_deposit(
        sat_acc, got, table, density_embed, capacity, lat_blocks - halo // rows_per_block, halo // rows_per_block
    ).reshape(halo, LON, d_in)
    above = passed_along(high, "band", 1)
    low = station_deposit(
        sat_acc, got, table, density_embed, capacity, 0, lat_blocks - halo // rows_per_block
    ).reshape(LAT_DEV - halo, LON, d_in)
    spread = convolve(bands, above, low, high, conv1_weight, conv1_bias, conv2_weight, conv2_bias, proj_weight)
    gathered = lax.all_to_all(spread, "band", split_axis=0, concat_axis=0, tiled=True)
    return gathered.reshape((bands * spread.shape[1],) + spread.shape[2:])


def solution(mesh):
    placed = (
        P(("member", "band"), None),
        P(("member", "band"), None),
        P(("member", "band")),
        P(("member", "band")),
        P(("member", "band"), None),
        P(("member", "band")),
        P(("member", "band")),
        P(),
        P(),
        P(),
        P(),
        P(),
        P(),
    )
    return jax.shard_map(
        body, mesh=mesh, in_specs=placed, out_specs=P("member", None, None), check_vma=False
    )
```

```python
import functools

import jax
import jax.numpy as jnp
from jax import lax
from jax.experimental import pallas as pl
from jax.experimental.pallas import tpu as pltpu
from jax.sharding import PartitionSpec as P

LAT_DEV = 8
LON = 256
META = 16


def passed_along(value, axis, by):
    length = lax.axis_size(axis)
    pairs = [(i, i + by) for i in range(length) if 0 <= i + by < length]
    return lax.ppermute(value, axis, pairs)


def weights_of(offsets):
    return jnp.exp(-offsets.astype(jnp.float32) ** 2 / 32.0).astype(jnp.bfloat16)


CELL_BLOCK = 256
OBS_CHUNK = 2048


def lookup(codes, table, shift):
    w = jnp.zeros(codes.shape, jnp.float32)
    for j in range(8):
        w = jnp.where(codes == j + shift, table[j], w)
    return w


def deposit_rows(aug, cells_s, w_s, first, count):
    n = aug.shape[0]
    chunk = min(n, OBS_CHUNK)
    ids = lax.broadcasted_iota(jnp.int32, (CELL_BLOCK, chunk), 0).astype(jnp.float32)
    ids = ids.astype(jnp.bfloat16)
    zero = jnp.zeros((), jnp.bfloat16)
    total = jnp.zeros((count * CELL_BLOCK, aug.shape[1]), jnp.float32)
    for start in range(0, n, chunk):
        cells = cells_s[:, start : start + chunk]
        w = w_s[:, start : start + chunk].astype(jnp.bfloat16)
        parts = []
        for k in range(count):
            rel = cells - (first + k) * CELL_BLOCK
            rel = jnp.where((rel >= 0) & (rel < CELL_BLOCK), rel, -1).astype(jnp.float32)
            parts.append(jnp.where(rel.astype(jnp.bfloat16) == ids, w, zero))
        table = parts[0] if count == 1 else jnp.concatenate(parts, axis=0)
        total = total + jnp.dot(table, aug[start : start + chunk, :], preferred_element_type=jnp.float32)
    return total


def sat_kernel(split, v_ref, c_ref, o_ref, tbl, low, high, aug, cells_s, w_s):
    n, d_in = v_ref.shape
    aug[:, :d_in] = v_ref[...]
    aug[:, d_in:] = jnp.ones((n, aug.shape[1] - d_in), jnp.bfloat16)
    cells_s[...] = c_ref[...]
    w_s[...] = lookup(o_ref[...], tbl, 0)
    high[...] = deposit_rows(aug, cells_s, w_s, split, high.shape[0] // CELL_BLOCK)
    low[...] = deposit_rows(aug, cells_s, w_s, 0, split)


def station_kernel(capacity, first, count, acc, got, tbl, embed, out, aug, cells_s, w_s):
    d_in = out.shape[1]
    bands = got.shape[0]
    aug[:, d_in:] = jnp.ones((aug.shape[0], aug.shape[1] - d_in), jnp.bfloat16)
    for t in range(bands):
        aug[t * capacity : (t + 1) * capacity, :d_in] = got[t, :capacity, :]
        meta = got[t, capacity : capacity + 6, :].astype(jnp.float32).astype(jnp.int32)
        for h in range(2):
            at = slice(t * capacity + h * d_in, t * capacity + (h + 1) * d_in)
            cells_s[:, at] = meta[h : h + 1] * 64 + meta[2 + h : 3 + h]
            w_s[:, at] = lookup(meta[4 + h : 5 + h], tbl, 1)
    total = acc[...] + deposit_rows(aug, cells_s, w_s, first, count)
    sums = total[:, :d_in]
    density = total[:, d_in:]
    grid = sums / jnp.maximum(density, 1.0) + density * embed[...]
    out[...] = grid.astype(out.dtype)


def whole(shape):
    return pl.BlockSpec(shape, lambda c: (0,) * len(shape))


SMEM = pl.BlockSpec(memory_space=pltpu.SMEM)


def sat_deposit(values, cells, offsets, table, split, total_cells):
    n, d_in = values.shape
    wide = 2 * d_in
    low_rows = split * CELL_BLOCK
    high_rows = total_cells - low_rows
    return pl.pallas_call(
        functools.partial(sat_kernel, split),
        grid=(1,),
        in_specs=[whole((n, d_in)), whole((1, n)), whole((1, n)), SMEM],
        out_specs=[whole((low_rows, wide)), whole((high_rows, wide))],
        out_shape=[
            jax.ShapeDtypeStruct((low_rows, wide), jnp.float32),
            jax.ShapeDtypeStruct((high_rows, wide), jnp.float32),
        ],
        scratch_shapes=[
            pltpu.VMEM((n, wide), jnp.bfloat16),
            pltpu.VMEM((1, n), jnp.int32),
            pltpu.VMEM((1, n), jnp.float32),
        ],
        cost_estimate=pl.CostEstimate(
            flops=2 * total_cells * n * wide, transcendentals=0, bytes_accessed=2 * n * (d_in + 4)
        ),
    )(values, cells.reshape(1, n), offsets.reshape(1, n), table)


def station_deposit(acc, got, table, embed, capacity, first, count):
    bands, rows, d_in = got.shape
    n = bands * capacity
    wide = 2 * d_in
    cells = count * CELL_BLOCK
    return pl.pallas_call(
        functools.partial(station_kernel, capacity, first, count),
        grid=(1,),
        in_specs=[whole((cells, wide)), whole((bands, rows, d_in)), SMEM, whole((1, d_in))],
        out_specs=whole((cells, d_in)),
        out_shape=jax.ShapeDtypeStruct((cells, d_in), jnp.bfloat16),
        scratch_shapes=[
            pltpu.VMEM((n, wide), jnp.bfloat16),
            pltpu.VMEM((1, n), jnp.int32),
            pltpu.VMEM((1, n), jnp.float32),
        ],
        cost_estimate=pl.CostEstimate(
            flops=2 * cells * n * wide, transcendentals=0, bytes_accessed=2 * n * (d_in + 4)
        ),
    )(acc, got, table, embed.reshape(1, d_in))


def pick(scratch, value, start):
    rows, cols = value.shape
    lanes = scratch.shape[2]
    parts = []
    for k in range(cols // lanes):
        scratch[k, :rows, :] = value[:, k * lanes : (k + 1) * lanes]
        parts.append(scratch[k, pl.ds(start, rows // 2, stride=2), :])
    return parts[0] if len(parts) == 1 else jnp.concatenate(parts, axis=1)


def shifted_odd(scratch, value, period):
    odd = pick(scratch, value, 1)
    odd = pltpu.roll(odd, 1, 0)
    first = lax.broadcasted_iota(jnp.int32, odd.shape, 0) % period == 0
    return jnp.where(first, 0.0, odd)


def conv_taps(source, rows, width, weights):
    taps = []
    for e in range(3):
        total = None
        for a in range(3):
            piece = source[pl.ds(a, rows, stride=2)].reshape(rows * width, source.shape[2])
            part = jnp.dot(piece, weights[a, e], preferred_element_type=jnp.float32)
            total = part if total is None else total + part
        taps.append(total)
    return taps


def gelu(x):
    return 0.5 * x * (1.0 + lax.erf(x * 0.7071067811865476))


def conv_kernel(above, low, high, w1, b1, w2, b2, wp, out, xs, s1, h1, s2):
    halo, width, d_in = above.shape
    lat = low.shape[0] + high.shape[0]
    xs[:halo] = above[...]
    xs[halo : halo + low.shape[0]] = low[...]
    xs[halo + low.shape[0] :] = high[...]
    rows1 = (halo + lat - 1) // 2
    half = width // 2
    taps = conv_taps(xs, rows1, width, w1)
    pre1 = pick(s1, taps[1], 0) + pick(s1, taps[2], 1) + shifted_odd(s1, taps[0], half) + b1[...]
    hid = gelu(pre1)
    keep = (lax.broadcasted_iota(jnp.int32, hid.shape, 0) >= half) | (lax.axis_index("band") > 0)
    hid = jnp.where(keep, hid, 0.0).astype(jnp.bfloat16)
    h1[...] = hid.reshape(rows1, half, d_in)
    rows2 = (rows1 - 1) // 2
    quarter = half // 2
    taps = conv_taps(h1, rows2, half, w2)
    pre2 = pick(s2, taps[1], 0) + pick(s2, taps[2], 1) + shifted_odd(s2, taps[0], quarter) + b2[...]
    latent = gelu(pre2).astype(jnp.bfloat16)
    flat = jnp.dot(latent, wp[...], preferred_element_type=jnp.float32)
    flat = flat.astype(out.dtype).reshape(out.shape[1:])
    for b in range(out.shape[0]):
        out[b] = flat


def convolve(bands, above, low, high, w1, b1, w2, b2, wp):
    halo, width, d_in = above.shape
    lat = low.shape[0] + high.shape[0]
    d_lat = w2.shape[3]
    rows1 = (halo + lat - 1) // 2
    rows2 = (rows1 - 1) // 2
    vmem = pl.BlockSpec(memory_space=pltpu.VMEM)
    return pl.pallas_call(
        conv_kernel,
        in_specs=[vmem] * 8,
        out_specs=vmem,
        out_shape=jax.ShapeDtypeStruct((bands, rows2, width // 4, d_lat), jnp.bfloat16),
        scratch_shapes=[
            pltpu.VMEM((halo + lat, width, d_in), jnp.bfloat16),
            pltpu.VMEM((1, rows1 * width, 128), jnp.float32),
            pltpu.VMEM((rows1, width // 2, d_in), jnp.bfloat16),
            pltpu.VMEM((d_lat // 128, rows2 * width // 2, 128), jnp.float32),
        ],
    )(above, low, high, w1, b1.reshape(1, -1), w2, b2.reshape(1, -1), wp)


def prefix_count(mask):
    total = mask
    step = 1
    lanes = lax.broadcasted_iota(jnp.int32, mask.shape, 1)
    while step < mask.shape[1]:
        moved = pltpu.roll(total, step, 1)
        total = total + jnp.where(lanes >= step, moved, 0)
        step *= 2
    return total - mask


def route_kernel(capacity, target, cells, offsets, values, out):
    bands, rows, d_in = out.shape
    n = values.shape[0]
    t = target[...]
    band_ids = lax.broadcasted_iota(jnp.int32, (bands, n), 0)
    mask = (t == band_ids).astype(jnp.int32)
    rank = jnp.sum(mask * prefix_count(mask), axis=0, keepdims=True)
    c = cells[...]
    meta = jnp.concatenate(
        [c // 64, c % 64, offsets[...] + 1, jnp.zeros((5, n), jnp.int32)], axis=0
    ).astype(jnp.float32).astype(jnp.bfloat16)
    slots = lax.broadcasted_iota(jnp.int32, (capacity, n), 0).astype(jnp.float32).astype(jnp.bfloat16)
    per_row = capacity // d_in
    one = jnp.ones((), jnp.bfloat16)
    zero = jnp.zeros((), jnp.bfloat16)
    for b in range(bands):
        mine = jnp.where(t == b, rank, -1).astype(jnp.float32).astype(jnp.bfloat16)
        table = jnp.where(mine == slots, one, zero)
        out[b, :capacity, :] = jnp.dot(
            table, values[...], preferred_element_type=jnp.float32
        ).astype(out.dtype)
        sent = lax.dot_general(
            meta, table, (((1,), (1,)), ((), ())), preferred_element_type=jnp.float32
        ).astype(out.dtype)
        for m in range(3):
            for h in range(per_row):
                row = capacity + m * per_row + h
                out[b, row : row + 1, :] = sent[m : m + 1, h * d_in : (h + 1) * d_in]
        out[b, capacity + 3 * per_row :, :] = jnp.zeros((rows - capacity - 3 * per_row, d_in), out.dtype)


def route(obs_values, obs_band, obs_cell, obs_offset, bands):
    obs_rows, d_in = obs_values.shape
    capacity = obs_rows // 8
    vmem = pl.BlockSpec(memory_space=pltpu.VMEM)
    packet = pl.pallas_call(
        functools.partial(route_kernel, capacity),
        in_specs=[vmem] * 4,
        out_specs=vmem,
        out_shape=jax.ShapeDtypeStruct((bands, capacity + META, d_in), jnp.bfloat16),
    )(
        obs_band.reshape(1, obs_rows),
        obs_cell.reshape(1, obs_rows),
        obs_offset.reshape(1, obs_rows),
        obs_values,
    )
    return lax.all_to_all(packet, "band", split_axis=0, concat_axis=0, tiled=True)


def body(
    obs_values,
    obs_band,
    obs_cell,
    obs_offset,
    sat_values,
    sat_cell,
    sat_offset,
    density_embed,
    conv1_weight,
    conv1_bias,
    conv2_weight,
    conv2_bias,
    proj_weight,
):
    bands = lax.axis_size("band")
    position_index = lax.axis_index("band")
    d_in = obs_values.shape[1]
    band_cells = LAT_DEV * LON
    table = weights_of(jnp.arange(8, dtype=jnp.int32)).astype(jnp.float32)
    halo = 3
    lat_blocks = band_cells // CELL_BLOCK
    high_blocks = halo * LON // CELL_BLOCK
    low_blocks = lat_blocks - high_blocks
    sat_low, sat_high = sat_deposit(sat_values, sat_cell, sat_offset, table, low_blocks, band_cells)
    got = route(obs_values, obs_band, obs_cell, obs_offset, bands)
    capacity = obs_values.shape[0] // 8
    high = station_deposit(sat_high, got, table, density_embed, capacity, low_blocks, high_blocks)
    high = high.reshape(halo, LON, d_in)
    above = passed_along(high, "band", 1)
    low = station_deposit(sat_low, got, table, density_embed, capacity, 0, low_blocks)
    low = low.reshape(LAT_DEV - halo, LON, d_in)
    spread = convolve(bands, above, low, high, conv1_weight, conv1_bias, conv2_weight, conv2_bias, proj_weight)
    gathered = lax.all_to_all(spread, "band", split_axis=0, concat_axis=0, tiled=True)
    return gathered.reshape((bands * spread.shape[1],) + spread.shape[2:])


def solution(mesh):
    placed = (
        P(("member", "band"), None),
        P(("member", "band"), None),
        P(("member", "band")),
        P(("member", "band")),
        P(("member", "band"), None),
        P(("member", "band")),
        P(("member", "band")),
        P(),
        P(),
        P(),
        P(),
        P(),
        P(),
    )
    return jax.shard_map(
        body, mesh=mesh, in_specs=placed, out_specs=P("member", None, None), check_vma=False
    )
```

```python
import functools

import jax
import jax.numpy as jnp
from jax import lax
from jax.experimental import pallas as pl
from jax.experimental.pallas import tpu as pltpu
from jax.sharding import PartitionSpec as P

LAT_DEV = 8
LON = 256
META = 16


def passed_along(value, axis, by):
    length = lax.axis_size(axis)
    pairs = [(i, i + by) for i in range(length) if 0 <= i + by < length]
    return lax.ppermute(value, axis, pairs)


def weights_of(offsets):
    return jnp.exp(-offsets.astype(jnp.float32) ** 2 / 32.0).astype(jnp.bfloat16)


CELL_BLOCK = 256
OBS_CHUNK = 2048
ROUTE_GROUP = 8


def lookup(codes, table, shift):
    w = jnp.zeros(codes.shape, jnp.float32)
    for j in range(8):
        w = jnp.where(codes == j + shift, table[j], w)
    return w


def deposit_rows(aug, cells_s, w_s, first, count):
    n = aug.shape[0]
    chunk = min(n, OBS_CHUNK)
    ids = lax.broadcasted_iota(jnp.int32, (CELL_BLOCK, chunk), 0).astype(jnp.float32)
    ids = ids.astype(jnp.bfloat16)
    zero = jnp.zeros((), jnp.bfloat16)
    total = jnp.zeros((count * CELL_BLOCK, aug.shape[1]), jnp.float32)
    for start in range(0, n, chunk):
        cells = cells_s[:, start : start + chunk]
        w = w_s[:, start : start + chunk].astype(jnp.bfloat16)
        parts = []
        for k in range(count):
            rel = cells - (first + k) * CELL_BLOCK
            rel = jnp.where((rel >= 0) & (rel < CELL_BLOCK), rel, -1).astype(jnp.float32)
            parts.append(jnp.where(rel.astype(jnp.bfloat16) == ids, w, zero))
        table = parts[0] if count == 1 else jnp.concatenate(parts, axis=0)
        total = total + jnp.dot(table, aug[start : start + chunk, :], preferred_element_type=jnp.float32)
    return total


def sat_kernel(split, v_ref, c_ref, o_ref, tbl, low, high, aug, cells_s, w_s):
    n, d_in = v_ref.shape
    aug[:, :d_in] = v_ref[...]
    aug[:, d_in:] = jnp.ones((n, aug.shape[1] - d_in), jnp.bfloat16)
    cells_s[...] = c_ref[...]
    w_s[...] = lookup(o_ref[...], tbl, 0)
    high[...] = deposit_rows(aug, cells_s, w_s, split, high.shape[0] // CELL_BLOCK)
    low[...] = deposit_rows(aug, cells_s, w_s, 0, split)


def station_kernel(capacity, first, count, acc, got, tbl, embed, out, aug, cells_s, w_s):
    d_in = out.shape[1]
    bands = got.shape[0]
    aug[:, d_in:] = jnp.ones((aug.shape[0], aug.shape[1] - d_in), jnp.bfloat16)
    for t in range(bands):
        aug[t * capacity : (t + 1) * capacity, :d_in] = got[t, :capacity, :]
        meta = got[t, capacity : capacity + 6, :].astype(jnp.float32).astype(jnp.int32)
        for h in range(2):
            at = slice(t * capacity + h * d_in, t * capacity + (h + 1) * d_in)
            cells_s[:, at] = meta[h : h + 1] * 64 + meta[2 + h : 3 + h]
            w_s[:, at] = lookup(meta[4 + h : 5 + h], tbl, 1)
    total = acc[...] + deposit_rows(aug, cells_s, w_s, first, count)
    sums = total[:, :d_in]
    density = total[:, d_in:]
    grid = sums / jnp.maximum(density, 1.0) + density * embed[...]
    out[...] = grid.astype(out.dtype)


def whole(shape):
    return pl.BlockSpec(shape, lambda c: (0,) * len(shape))


SMEM = pl.BlockSpec(memory_space=pltpu.SMEM)


def sat_deposit(values, cells, offsets, table, split, total_cells):
    n, d_in = values.shape
    wide = 2 * d_in
    low_rows = split * CELL_BLOCK
    high_rows = total_cells - low_rows
    return pl.pallas_call(
        functools.partial(sat_kernel, split),
        grid=(1,),
        in_specs=[whole((n, d_in)), whole((1, n)), whole((1, n)), SMEM],
        out_specs=[whole((low_rows, wide)), whole((high_rows, wide))],
        out_shape=[
            jax.ShapeDtypeStruct((low_rows, wide), jnp.float32),
            jax.ShapeDtypeStruct((high_rows, wide), jnp.float32),
        ],
        scratch_shapes=[
            pltpu.VMEM((n, wide), jnp.bfloat16),
            pltpu.VMEM((1, n), jnp.int32),
            pltpu.VMEM((1, n), jnp.float32),
        ],
        cost_estimate=pl.CostEstimate(
            flops=2 * total_cells * n * wide, transcendentals=0, bytes_accessed=2 * n * (d_in + 4)
        ),
    )(values, cells.reshape(1, n), offsets.reshape(1, n), table)


def station_deposit(acc, got, table, embed, capacity, first, count):
    bands, rows, d_in = got.shape
    n = bands * capacity
    wide = 2 * d_in
    cells = count * CELL_BLOCK
    return pl.pallas_call(
        functools.partial(station_kernel, capacity, first, count),
        grid=(1,),
        in_specs=[whole((cells, wide)), whole((bands, rows, d_in)), SMEM, whole((1, d_in))],
        out_specs=whole((cells, d_in)),
        out_shape=jax.ShapeDtypeStruct((cells, d_in), jnp.bfloat16),
        scratch_shapes=[
            pltpu.VMEM((n, wide), jnp.bfloat16),
            pltpu.VMEM((1, n), jnp.int32),
            pltpu.VMEM((1, n), jnp.float32),
        ],
        cost_estimate=pl.CostEstimate(
            flops=2 * cells * n * wide, transcendentals=0, bytes_accessed=2 * n * (d_in + 4)
        ),
    )(acc, got, table, embed.reshape(1, d_in))


def pick(scratch, value, start):
    rows, cols = value.shape
    lanes = scratch.shape[2]
    parts = []
    for k in range(cols // lanes):
        scratch[k, :rows, :] = value[:, k * lanes : (k + 1) * lanes]
        parts.append(scratch[k, pl.ds(start, rows // 2, stride=2), :])
    return parts[0] if len(parts) == 1 else jnp.concatenate(parts, axis=1)


def shifted_odd(scratch, value, period):
    odd = pick(scratch, value, 1)
    odd = pltpu.roll(odd, 1, 0)
    first = lax.broadcasted_iota(jnp.int32, odd.shape, 0) % period == 0
    return jnp.where(first, 0.0, odd)


def conv_taps(source, rows, width, weights):
    taps = []
    for e in range(3):
        total = None
        for a in range(3):
            piece = source[pl.ds(a, rows, stride=2)].reshape(rows * width, source.shape[2])
            part = jnp.dot(piece, weights[a, e], preferred_element_type=jnp.float32)
            total = part if total is None else total + part
        taps.append(total)
    return taps


def gelu(x):
    return 0.5 * x * (1.0 + lax.erf(x * 0.7071067811865476))


def conv_kernel(above, low, high, w1, b1, w2, b2, wp, out, xs, s1, h1, s2):
    halo, width, d_in = above.shape
    lat = low.shape[0] + high.shape[0]
    xs[:halo] = above[...]
    xs[halo : halo + low.shape[0]] = low[...]
    xs[halo + low.shape[0] :] = high[...]
    rows1 = (halo + lat - 1) // 2
    half = width // 2
    taps = conv_taps(xs, rows1, width, w1)
    pre1 = pick(s1, taps[1], 0) + pick(s1, taps[2], 1) + shifted_odd(s1, taps[0], half) + b1[...]
    hid = gelu(pre1)
    keep = (lax.broadcasted_iota(jnp.int32, hid.shape, 0) >= half) | (lax.axis_index("band") > 0)
    hid = jnp.where(keep, hid, 0.0).astype(jnp.bfloat16)
    h1[...] = hid.reshape(rows1, half, d_in)
    rows2 = (rows1 - 1) // 2
    quarter = half // 2
    taps = conv_taps(h1, rows2, half, w2)
    pre2 = pick(s2, taps[1], 0) + pick(s2, taps[2], 1) + shifted_odd(s2, taps[0], quarter) + b2[...]
    latent = gelu(pre2).astype(jnp.bfloat16)
    flat = jnp.dot(latent, wp[...], preferred_element_type=jnp.float32)
    flat = flat.astype(out.dtype).reshape(out.shape[1:])
    for b in range(out.shape[0]):
        out[b] = flat


def convolve(bands, above, low, high, w1, b1, w2, b2, wp):
    halo, width, d_in = above.shape
    lat = low.shape[0] + high.shape[0]
    d_lat = w2.shape[3]
    rows1 = (halo + lat - 1) // 2
    rows2 = (rows1 - 1) // 2
    vmem = pl.BlockSpec(memory_space=pltpu.VMEM)
    return pl.pallas_call(
        conv_kernel,
        in_specs=[vmem] * 8,
        out_specs=vmem,
        out_shape=jax.ShapeDtypeStruct((bands, rows2, width // 4, d_lat), jnp.bfloat16),
        scratch_shapes=[
            pltpu.VMEM((halo + lat, width, d_in), jnp.bfloat16),
            pltpu.VMEM((1, rows1 * width, 128), jnp.float32),
            pltpu.VMEM((rows1, width // 2, d_in), jnp.bfloat16),
            pltpu.VMEM((d_lat // 128, rows2 * width // 2, 128), jnp.float32),
        ],
    )(above, low, high, w1, b1.reshape(1, -1), w2, b2.reshape(1, -1), wp)


def prefix_count(mask):
    total = mask
    step = 1
    lanes = lax.broadcasted_iota(jnp.int32, mask.shape, 1)
    while step < mask.shape[1]:
        moved = pltpu.roll(total, step, 1)
        total = total + jnp.where(lanes >= step, moved, 0)
        step *= 2
    return total - mask


def route_kernel(capacity, target, cells, offsets, values, out):
    bands, rows, d_in = out.shape
    n = values.shape[0]
    t = target[...]
    band_ids = lax.broadcasted_iota(jnp.int32, (bands, n), 0)
    mask = (t == band_ids).astype(jnp.int32)
    rank = jnp.sum(mask * prefix_count(mask), axis=0, keepdims=True)
    c = cells[...]
    meta = jnp.concatenate(
        [c // 64, c % 64, offsets[...] + 1, jnp.zeros((5, n), jnp.int32)], axis=0
    ).astype(jnp.float32).astype(jnp.bfloat16)
    slots = lax.broadcasted_iota(jnp.int32, (capacity, n), 0).astype(jnp.float32).astype(jnp.bfloat16)
    per_row = capacity // d_in
    one = jnp.ones((), jnp.bfloat16)
    zero = jnp.zeros((), jnp.bfloat16)
    group = min(bands, ROUTE_GROUP)
    for g in range(0, bands, group):
        parts = []
        for b in range(g, g + group):
            mine = jnp.where(t == b, rank, -1).astype(jnp.float32).astype(jnp.bfloat16)
            parts.append(jnp.where(mine == slots, one, zero))
        table = jnp.concatenate(parts, axis=0) if group > 1 else parts[0]
        res = jnp.dot(table, values[...], preferred_element_type=jnp.float32).astype(out.dtype)
        sent = lax.dot_general(
            meta, table, (((1,), (1,)), ((), ())), preferred_element_type=jnp.float32
        ).astype(out.dtype)
        for k in range(group):
            b = g + k
            out[b, :capacity, :] = res[k * capacity : (k + 1) * capacity]
            for m in range(3):
                for h in range(per_row):
                    row = capacity + m * per_row + h
                    lane = k * capacity + h * d_in
                    out[b, row : row + 1, :] = sent[m : m + 1, lane : lane + d_in]
            out[b, capacity + 3 * per_row :, :] = jnp.zeros(
                (rows - capacity - 3 * per_row, d_in), out.dtype
            )


def route(obs_values, obs_band, obs_cell, obs_offset, bands):
    obs_rows, d_in = obs_values.shape
    capacity = obs_rows // 8
    vmem = pl.BlockSpec(memory_space=pltpu.VMEM)
    packet = pl.pallas_call(
        functools.partial(route_kernel, capacity),
        in_specs=[vmem] * 4,
        out_specs=vmem,
        out_shape=jax.ShapeDtypeStruct((bands, capacity + META, d_in), jnp.bfloat16),
    )(
        obs_band.reshape(1, obs_rows),
        obs_cell.reshape(1, obs_rows),
        obs_offset.reshape(1, obs_rows),
        obs_values,
    )
    return lax.all_to_all(packet, "band", split_axis=0, concat_axis=0, tiled=True)


def body(
    obs_values,
    obs_band,
    obs_cell,
    obs_offset,
    sat_values,
    sat_cell,
    sat_offset,
    density_embed,
    conv1_weight,
    conv1_bias,
    conv2_weight,
    conv2_bias,
    proj_weight,
):
    bands = lax.axis_size("band")
    position_index = lax.axis_index("band")
    d_in = obs_values.shape[1]
    band_cells = LAT_DEV * LON
    table = weights_of(jnp.arange(8, dtype=jnp.int32)).astype(jnp.float32)
    halo = 3
    lat_blocks = band_cells // CELL_BLOCK
    high_blocks = halo * LON // CELL_BLOCK
    low_blocks = lat_blocks - high_blocks
    sat_low, sat_high = sat_deposit(sat_values, sat_cell, sat_offset, table, low_blocks, band_cells)
    got = route(obs_values, obs_band, obs_cell, obs_offset, bands)
    capacity = obs_values.shape[0] // 8
    high = station_deposit(sat_high, got, table, density_embed, capacity, low_blocks, high_blocks)
    high = high.reshape(halo, LON, d_in)
    above = passed_along(high, "band", 1)
    low = station_deposit(sat_low, got, table, density_embed, capacity, 0, low_blocks)
    low = low.reshape(LAT_DEV - halo, LON, d_in)
    spread = convolve(bands, above, low, high, conv1_weight, conv1_bias, conv2_weight, conv2_bias, proj_weight)
    gathered = lax.all_to_all(spread, "band", split_axis=0, concat_axis=0, tiled=True)
    return gathered.reshape((bands * spread.shape[1],) + spread.shape[2:])


def solution(mesh):
    placed = (
        P(("member", "band"), None),
        P(("member", "band"), None),
        P(("member", "band")),
        P(("member", "band")),
        P(("member", "band"), None),
        P(("member", "band")),
        P(("member", "band")),
        P(),
        P(),
        P(),
        P(),
        P(),
        P(),
    )
    return jax.shard_map(
        body, mesh=mesh, in_specs=placed, out_specs=P("member", None, None), check_vma=False
    )
```

```python
import functools

import jax
import jax.numpy as jnp
from jax import lax
from jax.experimental import pallas as pl
from jax.experimental.pallas import tpu as pltpu
from jax.sharding import PartitionSpec as P

LAT_DEV = 8
LON = 256
META = 16


def passed_along(value, axis, by):
    length = lax.axis_size(axis)
    pairs = [(i, i + by) for i in range(length) if 0 <= i + by < length]
    return lax.ppermute(value, axis, pairs)


def weights_of(offsets):
    return jnp.exp(-offsets.astype(jnp.float32) ** 2 / 32.0).astype(jnp.bfloat16)


CELL_BLOCK = 256
OBS_CHUNK = 2048


def lookup(codes, table, shift):
    w = jnp.zeros(codes.shape, jnp.float32)
    for j in range(8):
        w = jnp.where(codes == j + shift, table[j], w)
    return w


def deposit_rows(aug, cells_s, w_s, first, count):
    n = aug.shape[0]
    chunk = min(n, OBS_CHUNK)
    ids = lax.broadcasted_iota(jnp.int32, (CELL_BLOCK, chunk), 0).astype(jnp.float32)
    ids = ids.astype(jnp.bfloat16)
    zero = jnp.zeros((), jnp.bfloat16)
    total = jnp.zeros((count * CELL_BLOCK, aug.shape[1]), jnp.float32)
    for start in range(0, n, chunk):
        cells = cells_s[:, start : start + chunk]
        w = w_s[:, start : start + chunk].astype(jnp.bfloat16)
        parts = []
        for k in range(count):
            rel = cells - (first + k) * CELL_BLOCK
            rel = jnp.where((rel >= 0) & (rel < CELL_BLOCK), rel, -1).astype(jnp.float32)
            parts.append(jnp.where(rel.astype(jnp.bfloat16) == ids, w, zero))
        table = parts[0] if count == 1 else jnp.concatenate(parts, axis=0)
        total = total + jnp.dot(table, aug[start : start + chunk, :], preferred_element_type=jnp.float32)
    return total


def sat_kernel(split, v_ref, c_ref, o_ref, tbl, low, high, aug, cells_s, w_s):
    n, d_in = v_ref.shape
    aug[:, :d_in] = v_ref[...]
    aug[:, d_in:] = jnp.ones((n, aug.shape[1] - d_in), jnp.bfloat16)
    cells_s[...] = c_ref[...]
    w_s[...] = lookup(o_ref[...], tbl, 0)
    high[...] = deposit_rows(aug, cells_s, w_s, split, high.shape[0] // CELL_BLOCK)
    low[...] = deposit_rows(aug, cells_s, w_s, 0, split)


def station_kernel(capacity, first, count, acc, got, tbl, embed, out, aug, cells_s, w_s):
    d_in = out.shape[1]
    bands = got.shape[0]
    aug[:, d_in:] = jnp.ones((aug.shape[0], aug.shape[1] - d_in), jnp.bfloat16)
    for t in range(bands):
        aug[t * capacity : (t + 1) * capacity, :d_in] = got[t, :capacity, :]
        meta = got[t, capacity : capacity + 6, :].astype(jnp.float32).astype(jnp.int32)
        for h in range(2):
            at = slice(t * capacity + h * d_in, t * capacity + (h + 1) * d_in)
            cells_s[:, at] = meta[h : h + 1] * 64 + meta[2 + h : 3 + h]
            w_s[:, at] = lookup(meta[4 + h : 5 + h], tbl, 1)
    total = acc[...] + deposit_rows(aug, cells_s, w_s, first, count)
    sums = total[:, :d_in]
    density = total[:, d_in:]
    grid = sums / jnp.maximum(density, 1.0) + density * embed[...]
    out[...] = grid.astype(out.dtype)


def whole(shape):
    return pl.BlockSpec(shape, lambda c: (0,) * len(shape))


SMEM = pl.BlockSpec(memory_space=pltpu.SMEM)


def sat_deposit(values, cells, offsets, table, split, total_cells):
    n, d_in = values.shape
    wide = 2 * d_in
    low_rows = split * CELL_BLOCK
    high_rows = total_cells - low_rows
    return pl.pallas_call(
        functools.partial(sat_kernel, split),
        grid=(1,),
        in_specs=[whole((n, d_in)), whole((1, n)), whole((1, n)), SMEM],
        out_specs=[whole((low_rows, wide)), whole((high_rows, wide))],
        out_shape=[
            jax.ShapeDtypeStruct((low_rows, wide), jnp.float32),
            jax.ShapeDtypeStruct((high_rows, wide), jnp.float32),
        ],
        scratch_shapes=[
            pltpu.VMEM((n, wide), jnp.bfloat16),
            pltpu.VMEM((1, n), jnp.int32),
            pltpu.VMEM((1, n), jnp.float32),
        ],
        cost_estimate=pl.CostEstimate(
            flops=2 * total_cells * n * wide, transcendentals=0, bytes_accessed=2 * n * (d_in + 4)
        ),
    )(values, cells.reshape(1, n), offsets.reshape(1, n), table)


def station_deposit(acc, got, table, embed, capacity, first, count):
    bands, rows, d_in = got.shape
    n = bands * capacity
    wide = 2 * d_in
    cells = count * CELL_BLOCK
    return pl.pallas_call(
        functools.partial(station_kernel, capacity, first, count),
        grid=(1,),
        in_specs=[whole((cells, wide)), whole((bands, rows, d_in)), SMEM, whole((1, d_in))],
        out_specs=whole((cells, d_in)),
        out_shape=jax.ShapeDtypeStruct((cells, d_in), jnp.bfloat16),
        scratch_shapes=[
            pltpu.VMEM((n, wide), jnp.bfloat16),
            pltpu.VMEM((1, n), jnp.int32),
            pltpu.VMEM((1, n), jnp.float32),
        ],
        cost_estimate=pl.CostEstimate(
            flops=2 * cells * n * wide, transcendentals=0, bytes_accessed=2 * n * (d_in + 4)
        ),
    )(acc, got, table, embed.reshape(1, d_in))


def pick(scratch, value, start):
    rows, cols = value.shape
    lanes = scratch.shape[2]
    parts = []
    for k in range(cols // lanes):
        scratch[k, :rows, :] = value[:, k * lanes : (k + 1) * lanes]
        parts.append(scratch[k, pl.ds(start, rows // 2, stride=2), :])
    return parts[0] if len(parts) == 1 else jnp.concatenate(parts, axis=1)


def shifted_odd(scratch, value, period):
    odd = pick(scratch, value, 1)
    odd = pltpu.roll(odd, 1, 0)
    first = lax.broadcasted_iota(jnp.int32, odd.shape, 0) % period == 0
    return jnp.where(first, 0.0, odd)


def conv_taps(source, rows, width, weights):
    taps = []
    for e in range(3):
        total = None
        for a in range(3):
            piece = source[pl.ds(a, rows, stride=2)].reshape(rows * width, source.shape[2])
            part = jnp.dot(piece, weights[a, e], preferred_element_type=jnp.float32)
            total = part if total is None else total + part
        taps.append(total)
    return taps


def gelu(x):
    return 0.5 * x * (1.0 + lax.erf(x * 0.7071067811865476))


def conv_kernel(above, low, high, w1, b1, w2, b2, wp, out, xs, s1, h1, s2):
    halo, width, d_in = above.shape
    lat = low.shape[0] + high.shape[0]
    xs[:halo] = above[...]
    xs[halo : halo + low.shape[0]] = low[...]
    xs[halo + low.shape[0] :] = high[...]
    rows1 = (halo + lat - 1) // 2
    half = width // 2
    taps = conv_taps(xs, rows1, width, w1)
    pre1 = pick(s1, taps[1], 0) + pick(s1, taps[2], 1) + shifted_odd(s1, taps[0], half) + b1[...]
    hid = gelu(pre1)
    keep = (lax.broadcasted_iota(jnp.int32, hid.shape, 0) >= half) | (lax.axis_index("band") > 0)
    hid = jnp.where(keep, hid, 0.0).astype(jnp.bfloat16)
    h1[...] = hid.reshape(rows1, half, d_in)
    rows2 = (rows1 - 1) // 2
    quarter = half // 2
    taps = conv_taps(h1, rows2, half, w2)
    pre2 = pick(s2, taps[1], 0) + pick(s2, taps[2], 1) + shifted_odd(s2, taps[0], quarter) + b2[...]
    latent = gelu(pre2).astype(jnp.bfloat16)
    flat = jnp.dot(latent, wp[...], preferred_element_type=jnp.float32)
    flat = flat.astype(out.dtype).reshape(out.shape[1:])
    for b in range(out.shape[0]):
        out[b] = flat


def convolve(bands, above, low, high, w1, b1, w2, b2, wp):
    halo, width, d_in = above.shape
    lat = low.shape[0] + high.shape[0]
    d_lat = w2.shape[3]
    rows1 = (halo + lat - 1) // 2
    rows2 = (rows1 - 1) // 2
    vmem = pl.BlockSpec(memory_space=pltpu.VMEM)
    return pl.pallas_call(
        conv_kernel,
        in_specs=[vmem] * 8,
        out_specs=vmem,
        out_shape=jax.ShapeDtypeStruct((bands, rows2, width // 4, d_lat), jnp.bfloat16),
        scratch_shapes=[
            pltpu.VMEM((halo + lat, width, d_in), jnp.bfloat16),
            pltpu.VMEM((1, rows1 * width, 128), jnp.float32),
            pltpu.VMEM((rows1, width // 2, d_in), jnp.bfloat16),
            pltpu.VMEM((d_lat // 128, rows2 * width // 2, 128), jnp.float32),
        ],
    )(above, low, high, w1, b1.reshape(1, -1), w2, b2.reshape(1, -1), wp)


def prefix_count(mask):
    total = mask
    step = 1
    lanes = lax.broadcasted_iota(jnp.int32, mask.shape, 1)
    while step < mask.shape[1]:
        moved = pltpu.roll(total, step, 1)
        total = total + jnp.where(lanes >= step, moved, 0)
        step *= 2
    return total - mask


def route_kernel(capacity, target, cells, offsets, values, out, vaug):
    bands, rows, d_in = out.shape
    n = values.shape[0]
    t = target[...]
    band_ids = lax.broadcasted_iota(jnp.int32, (bands, n), 0)
    mask = (t == band_ids).astype(jnp.int32)
    rank = jnp.sum(mask * prefix_count(mask), axis=0, keepdims=True)
    c = cells[...]
    meta = jnp.concatenate(
        [c // 64, c % 64, offsets[...] + 1, jnp.zeros((d_in - 3, n), jnp.int32)], axis=0
    ).astype(jnp.float32)
    vaug[:, :d_in] = values[...]
    vaug[:, d_in:] = jnp.transpose(meta).astype(jnp.bfloat16)
    slots = lax.broadcasted_iota(jnp.int32, (capacity, n), 0).astype(jnp.float32).astype(jnp.bfloat16)
    per_row = capacity // d_in
    one = jnp.ones((), jnp.bfloat16)
    zero = jnp.zeros((), jnp.bfloat16)
    for b in range(bands):
        mine = jnp.where(t == b, rank, -1).astype(jnp.float32).astype(jnp.bfloat16)
        table = jnp.where(mine == slots, one, zero)
        res = jnp.dot(table, vaug[...], preferred_element_type=jnp.float32)
        out[b, :capacity, :] = res[:, :d_in].astype(out.dtype)
        sent = jnp.transpose(res[:, d_in:]).astype(out.dtype)
        for m in range(3):
            for h in range(per_row):
                row = capacity + m * per_row + h
                out[b, row : row + 1, :] = sent[m : m + 1, h * d_in : (h + 1) * d_in]
        out[b, capacity + 3 * per_row :, :] = jnp.zeros((rows - capacity - 3 * per_row, d_in), out.dtype)


def route(obs_values, obs_band, obs_cell, obs_offset, bands):
    obs_rows, d_in = obs_values.shape
    capacity = obs_rows // 8
    vmem = pl.BlockSpec(memory_space=pltpu.VMEM)
    packet = pl.pallas_call(
        functools.partial(route_kernel, capacity),
        in_specs=[vmem] * 4,
        out_specs=vmem,
        out_shape=jax.ShapeDtypeStruct((bands, capacity + META, d_in), jnp.bfloat16),
        scratch_shapes=[pltpu.VMEM((obs_rows, 2 * d_in), jnp.bfloat16)],
    )(
        obs_band.reshape(1, obs_rows),
        obs_cell.reshape(1, obs_rows),
        obs_offset.reshape(1, obs_rows),
        obs_values,
    )
    return lax.all_to_all(packet, "band", split_axis=0, concat_axis=0, tiled=True)


def body(
    obs_values,
    obs_band,
    obs_cell,
    obs_offset,
    sat_values,
    sat_cell,
    sat_offset,
    density_embed,
    conv1_weight,
    conv1_bias,
    conv2_weight,
    conv2_bias,
    proj_weight,
):
    bands = lax.axis_size("band")
    position_index = lax.axis_index("band")
    d_in = obs_values.shape[1]
    band_cells = LAT_DEV * LON
    table = weights_of(jnp.arange(8, dtype=jnp.int32)).astype(jnp.float32)
    halo = 3
    lat_blocks = band_cells // CELL_BLOCK
    high_blocks = halo * LON // CELL_BLOCK
    low_blocks = lat_blocks - high_blocks
    sat_low, sat_high = sat_deposit(sat_values, sat_cell, sat_offset, table, low_blocks, band_cells)
    got = route(obs_values, obs_band, obs_cell, obs_offset, bands)
    capacity = obs_values.shape[0] // 8
    high = station_deposit(sat_high, got, table, density_embed, capacity, low_blocks, high_blocks)
    high = high.reshape(halo, LON, d_in)
    above = passed_along(high, "band", 1)
    low = station_deposit(sat_low, got, table, density_embed, capacity, 0, low_blocks)
    low = low.reshape(LAT_DEV - halo, LON, d_in)
    spread = convolve(bands, above, low, high, conv1_weight, conv1_bias, conv2_weight, conv2_bias, proj_weight)
    gathered = lax.all_to_all(spread, "band", split_axis=0, concat_axis=0, tiled=True)
    return gathered.reshape((bands * spread.shape[1],) + spread.shape[2:])


def solution(mesh):
    placed = (
        P(("member", "band"), None),
        P(("member", "band"), None),
        P(("member", "band")),
        P(("member", "band")),
        P(("member", "band"), None),
        P(("member", "band")),
        P(("member", "band")),
        P(),
        P(),
        P(),
        P(),
        P(),
        P(),
    )
    return jax.shard_map(
        body, mesh=mesh, in_specs=placed, out_specs=P("member", None, None), check_vma=False
    )
```

```python
import functools

import jax
import jax.numpy as jnp
from jax import lax
from jax.experimental import pallas as pl
from jax.experimental.pallas import tpu as pltpu
from jax.sharding import PartitionSpec as P


LAT_DEV = 8
LON = 256
META = 16


def passed_along(value, axis, by):
    length = lax.axis_size(axis)
    pairs = [(i, i + by) for i in range(length) if 0 <= i + by < length]
    return lax.ppermute(value, axis, pairs)


def weights_of(offsets):
    return jnp.exp(-offsets.astype(jnp.float32) ** 2 / 32.0).astype(jnp.bfloat16)


CELL_BLOCK = 256
OBS_CHUNK = 2048


def lookup(codes, table, shift):
    w = jnp.zeros(codes.shape, jnp.float32)
    for j in range(8):
        w = jnp.where(codes == j + shift, table[j], w)
    return w


def deposit_rows(aug, cells_s, w_s, first, count):
    n = aug.shape[0]
    chunk = min(n, OBS_CHUNK)
    ids = lax.broadcasted_iota(jnp.int32, (CELL_BLOCK, chunk), 0).astype(jnp.float32)
    ids = ids.astype(jnp.bfloat16)
    zero = jnp.zeros((), jnp.bfloat16)
    total = jnp.zeros((count * CELL_BLOCK, aug.shape[1]), jnp.float32)
    for start in range(0, n, chunk):
        cells = cells_s[:, start : start + chunk]
        w = w_s[:, start : start + chunk].astype(jnp.bfloat16)
        parts = []
        for k in range(count):
            rel = cells - (first + k) * CELL_BLOCK
            rel = jnp.where((rel >= 0) & (rel < CELL_BLOCK), rel, -1).astype(jnp.float32)
            parts.append(jnp.where(rel.astype(jnp.bfloat16) == ids, w, zero))
        table = parts[0] if count == 1 else jnp.concatenate(parts, axis=0)
        total = total + jnp.dot(table, aug[start : start + chunk, :], preferred_element_type=jnp.float32)
    return total


def sat_kernel(split, v_ref, c_ref, o_ref, tbl, low, high, aug, cells_s, w_s):
    n, d_in = v_ref.shape
    aug[:, :d_in] = v_ref[...]
    aug[:, d_in:] = jnp.ones((n, aug.shape[1] - d_in), jnp.bfloat16)
    cells_s[...] = c_ref[...]
    w_s[...] = lookup(o_ref[...], tbl, 0)
    high[...] = deposit_rows(aug, cells_s, w_s, split, high.shape[0] // CELL_BLOCK)
    low[...] = deposit_rows(aug, cells_s, w_s, 0, split)


def station_kernel(capacity, first, count, acc, got, tbl, embed, out, aug, cells_s, w_s):
    d_in = out.shape[1]
    bands = got.shape[0]
    aug[:, d_in:] = jnp.ones((aug.shape[0], aug.shape[1] - d_in), jnp.bfloat16)
    for t in range(bands):
        aug[t * capacity : (t + 1) * capacity, :d_in] = got[t, :capacity, :]
        meta = got[t, capacity : capacity + 6, :].astype(jnp.float32).astype(jnp.int32)
        for h in range(2):
            at = slice(t * capacity + h * d_in, t * capacity + (h + 1) * d_in)
            cells_s[:, at] = meta[h : h + 1] * 64 + meta[2 + h : 3 + h]
            w_s[:, at] = lookup(meta[4 + h : 5 + h], tbl, 1)
    total = acc[...] + deposit_rows(aug, cells_s, w_s, first, count)
    sums = total[:, :d_in]
    density = total[:, d_in:]
    grid = sums / jnp.maximum(density, 1.0) + density * embed[...]
    out[...] = grid.astype(out.dtype)


def whole(shape):
    return pl.BlockSpec(shape, lambda c: (0,) * len(shape))


SMEM = pl.BlockSpec(memory_space=pltpu.SMEM)


def sat_deposit(values, cells, offsets, table, split, total_cells):
    n, d_in = values.shape
    wide = 2 * d_in
    low_rows = split * CELL_BLOCK
    high_rows = total_cells - low_rows
    return pl.pallas_call(
        functools.partial(sat_kernel, split),
        grid=(1,),
        in_specs=[whole((n, d_in)), whole((1, n)), whole((1, n)), SMEM],
        out_specs=[whole((low_rows, wide)), whole((high_rows, wide))],
        out_shape=[
            jax.ShapeDtypeStruct((low_rows, wide), jnp.float32),
            jax.ShapeDtypeStruct((high_rows, wide), jnp.float32),
        ],
        scratch_shapes=[
            pltpu.VMEM((n, wide), jnp.bfloat16),
            pltpu.VMEM((1, n), jnp.int32),
            pltpu.VMEM((1, n), jnp.float32),
        ],
        cost_estimate=pl.CostEstimate(
            flops=2 * total_cells * n * wide, transcendentals=0, bytes_accessed=2 * n * (d_in + 4)
        ),
    )(values, cells.reshape(1, n), offsets.reshape(1, n), table)


def station_deposit(acc, got, table, embed, capacity, first, count):
    bands, rows, d_in = got.shape
    n = bands * capacity
    wide = 2 * d_in
    cells = count * CELL_BLOCK
    return pl.pallas_call(
        functools.partial(station_kernel, capacity, first, count),
        grid=(1,),
        in_specs=[whole((cells, wide)), whole((bands, rows, d_in)), SMEM, whole((1, d_in))],
        out_specs=whole((cells, d_in)),
        out_shape=jax.ShapeDtypeStruct((cells, d_in), jnp.bfloat16),
        scratch_shapes=[
            pltpu.VMEM((n, wide), jnp.bfloat16),
            pltpu.VMEM((1, n), jnp.int32),
            pltpu.VMEM((1, n), jnp.float32),
        ],
        cost_estimate=pl.CostEstimate(
            flops=2 * cells * n * wide, transcendentals=0, bytes_accessed=2 * n * (d_in + 4)
        ),
    )(acc, got, table, embed.reshape(1, d_in))


def pick(scratch, value, start):
    rows, cols = value.shape
    lanes = scratch.shape[2]
    parts = []
    for k in range(cols // lanes):
        scratch[k, :rows, :] = value[:, k * lanes : (k + 1) * lanes]
        parts.append(scratch[k, pl.ds(start, rows // 2, stride=2), :])
    return parts[0] if len(parts) == 1 else jnp.concatenate(parts, axis=1)


def shifted_odd(scratch, value, period):
    odd = pick(scratch, value, 1)
    odd = pltpu.roll(odd, 1, 0)
    first = lax.broadcasted_iota(jnp.int32, odd.shape, 0) % period == 0
    return jnp.where(first, 0.0, odd)


def conv_taps(source, rows, width, weights):
    taps = []
    for e in range(3):
        total = None
        for a in range(3):
            piece = source[pl.ds(a, rows, stride=2)].reshape(rows * width, source.shape[2])
            part = jnp.dot(piece, weights[a, e], preferred_element_type=jnp.float32)
            total = part if total is None else total + part
        taps.append(total)
    return taps


def gelu(x):
    return 0.5 * x * (1.0 + lax.erf(x * 0.7071067811865476))


def conv_kernel(above, low, high, w1, b1, w2, b2, wp, out, xs, s1, h1, s2):
    halo, width, d_in = above.shape
    lat = low.shape[0] + high.shape[0]
    xs[:halo] = above[...]
    xs[halo : halo + low.shape[0]] = low[...]
    xs[halo + low.shape[0] :] = high[...]
    rows1 = (halo + lat - 1) // 2
    half = width // 2
    taps = conv_taps(xs, rows1, width, w1)
    pre1 = pick(s1, taps[1], 0) + pick(s1, taps[2], 1) + shifted_odd(s1, taps[0], half) + b1[...]
    hid = gelu(pre1)
    keep = (lax.broadcasted_iota(jnp.int32, hid.shape, 0) >= half) | (lax.axis_index("band") > 0)
    hid = jnp.where(keep, hid, 0.0).astype(jnp.bfloat16)
    h1[...] = hid.reshape(rows1, half, d_in)
    rows2 = (rows1 - 1) // 2
    quarter = half // 2
    taps = conv_taps(h1, rows2, half, w2)
    pre2 = pick(s2, taps[1], 0) + pick(s2, taps[2], 1) + shifted_odd(s2, taps[0], quarter) + b2[...]
    latent = gelu(pre2).astype(jnp.bfloat16)
    flat = jnp.dot(latent, wp[...], preferred_element_type=jnp.float32)
    flat = flat.astype(out.dtype).reshape(out.shape[1:])
    for b in range(out.shape[0]):
        out[b] = flat


def convolve(bands, above, low, high, w1, b1, w2, b2, wp):
    halo, width, d_in = above.shape
    lat = low.shape[0] + high.shape[0]
    d_lat = w2.shape[3]
    rows1 = (halo + lat - 1) // 2
    rows2 = (rows1 - 1) // 2
    vmem = pl.BlockSpec(memory_space=pltpu.VMEM)
    return pl.pallas_call(
        conv_kernel,
        in_specs=[vmem] * 8,
        out_specs=vmem,
        out_shape=jax.ShapeDtypeStruct((bands, rows2, width // 4, d_lat), jnp.bfloat16),
        scratch_shapes=[
            pltpu.VMEM((halo + lat, width, d_in), jnp.bfloat16),
            pltpu.VMEM((1, rows1 * width, 128), jnp.float32),
            pltpu.VMEM((rows1, width // 2, d_in), jnp.bfloat16),
            pltpu.VMEM((d_lat // 128, rows2 * width // 2, 128), jnp.float32),
        ],
    )(above, low, high, w1, b1.reshape(1, -1), w2, b2.reshape(1, -1), wp)


def prefix_count(mask):
    total = mask
    step = 1
    lanes = lax.broadcasted_iota(jnp.int32, mask.shape, 1)
    while step < mask.shape[1]:
        moved = pltpu.roll(total, step, 1)
        total = total + jnp.where(lanes >= step, moved, 0)
        step *= 2
    return total - mask


def route_kernel(capacity, target, cells, offsets, values, out, vaug):
    bands, rows, d_in = out.shape
    n = values.shape[0]
    t = target[...]
    band_ids = lax.broadcasted_iota(jnp.int32, (bands, n), 0)
    mask = (t == band_ids).astype(jnp.int32)
    rank = jnp.sum(mask * prefix_count(mask), axis=0, keepdims=True)
    c = cells[...]
    meta = jnp.concatenate(
        [c // 64, c % 64, offsets[...] + 1, jnp.zeros((d_in - 3, n), jnp.int32)], axis=0
    ).astype(jnp.float32)
    vaug[:, :d_in] = values[...]
    vaug[:, d_in:] = jnp.transpose(meta).astype(jnp.bfloat16)
    slots = lax.broadcasted_iota(jnp.int32, (capacity, n), 0).astype(jnp.float32).astype(jnp.bfloat16)
    per_row = capacity // d_in
    one = jnp.ones((), jnp.bfloat16)
    zero = jnp.zeros((), jnp.bfloat16)
    me = lax.axis_index("band")
    for b in range(bands):
        mine = jnp.where(t == b, rank, -1).astype(jnp.float32).astype(jnp.bfloat16)
        table = jnp.where(mine == slots, one, zero)
        res = jnp.dot(table, vaug[...], preferred_element_type=jnp.float32)
        k = (b - me + bands) % bands
        out[k, :capacity, :] = res[:, :d_in].astype(out.dtype)
        sent = jnp.transpose(res[:, d_in:]).astype(out.dtype)
        for m in range(3):
            for h in range(per_row):
                row = capacity + m * per_row + h
                out[k, row : row + 1, :] = sent[m : m + 1, h * d_in : (h + 1) * d_in]
        out[k, capacity + 3 * per_row :, :] = jnp.zeros((rows - capacity - 3 * per_row, d_in), out.dtype)


def route(obs_values, obs_band, obs_cell, obs_offset, bands):
    obs_rows, d_in = obs_values.shape
    capacity = obs_rows // 8
    vmem = pl.BlockSpec(memory_space=pltpu.VMEM)
    packet = pl.pallas_call(
        functools.partial(route_kernel, capacity),
        in_specs=[vmem] * 4,
        out_specs=vmem,
        out_shape=jax.ShapeDtypeStruct((bands, capacity + META, d_in), jnp.bfloat16),
        scratch_shapes=[pltpu.VMEM((obs_rows, 2 * d_in), jnp.bfloat16)],
    )(
        obs_band.reshape(1, obs_rows),
        obs_cell.reshape(1, obs_rows),
        obs_offset.reshape(1, obs_rows),
        obs_values,
    )
    moved = [packet[0:1]]
    for k in range(1, bands):
        pairs = [(j, (j + k) % bands) for j in range(bands)]
        moved.append(lax.ppermute(packet[k : k + 1], "band", pairs))
    return jnp.concatenate(moved, axis=0)


def body(
    obs_values,
    obs_band,
    obs_cell,
    obs_offset,
    sat_values,
    sat_cell,
    sat_offset,
    density_embed,
    conv1_weight,
    conv1_bias,
    conv2_weight,
    conv2_bias,
    proj_weight,
):
    bands = lax.axis_size("band")
    position_index = lax.axis_index("band")
    d_in = obs_values.shape[1]
    band_cells = LAT_DEV * LON
    table = weights_of(jnp.arange(8, dtype=jnp.int32)).astype(jnp.float32)
    halo = 3
    lat_blocks = band_cells // CELL_BLOCK
    high_blocks = halo * LON // CELL_BLOCK
    low_blocks = lat_blocks - high_blocks
    sat_low, sat_high = sat_deposit(sat_values, sat_cell, sat_offset, table, low_blocks, band_cells)
    got = route(obs_values, obs_band, obs_cell, obs_offset, bands)
    capacity = obs_values.shape[0] // 8
    high = station_deposit(sat_high, got, table, density_embed, capacity, low_blocks, high_blocks)
    high = high.reshape(halo, LON, d_in)
    above = passed_along(high, "band", 1)
    low = station_deposit(sat_low, got, table, density_embed, capacity, 0, low_blocks)
    low = low.reshape(LAT_DEV - halo, LON, d_in)
    spread = convolve(bands, above, low, high, conv1_weight, conv1_bias, conv2_weight, conv2_bias, proj_weight)
    gathered = lax.all_to_all(spread, "band", split_axis=0, concat_axis=0, tiled=True)
    return gathered.reshape((bands * spread.shape[1],) + spread.shape[2:])


def solution(mesh):
    placed = (
        P(("member", "band"), None),
        P(("member", "band"), None),
        P(("member", "band")),
        P(("member", "band")),
        P(("member", "band"), None),
        P(("member", "band")),
        P(("member", "band")),
        P(),
        P(),
        P(),
        P(),
        P(),
        P(),
    )
    return jax.shard_map(
        body, mesh=mesh, in_specs=placed, out_specs=P("member", None, None), check_vma=False
    )
```

```python
import functools

import jax
import jax.numpy as jnp
from jax import lax
from jax.experimental import pallas as pl
from jax.experimental.pallas import tpu as pltpu
from jax.sharding import PartitionSpec as P


LAT_DEV = 8
LON = 256
META = 16


def passed_along(value, axis, by):
    length = lax.axis_size(axis)
    pairs = [(i, i + by) for i in range(length) if 0 <= i + by < length]
    return lax.ppermute(value, axis, pairs)


def weights_of(offsets):
    return jnp.exp(-offsets.astype(jnp.float32) ** 2 / 32.0).astype(jnp.bfloat16)


CELL_BLOCK = 256
OBS_CHUNK = 2048


def lookup(codes, table, shift):
    w = jnp.zeros(codes.shape, jnp.float32)
    for j in range(8):
        w = jnp.where(codes == j + shift, table[j], w)
    return w


def deposit_rows(aug, cells_s, w_s, first, count):
    n = aug.shape[0]
    chunk = min(n, OBS_CHUNK)
    ids = lax.broadcasted_iota(jnp.int32, (CELL_BLOCK, chunk), 0).astype(jnp.float32)
    ids = ids.astype(jnp.bfloat16)
    zero = jnp.zeros((), jnp.bfloat16)
    total = jnp.zeros((count * CELL_BLOCK, aug.shape[1]), jnp.float32)
    for start in range(0, n, chunk):
        cells = cells_s[:, start : start + chunk]
        w = w_s[:, start : start + chunk].astype(jnp.bfloat16)
        parts = []
        for k in range(count):
            rel = cells - (first + k) * CELL_BLOCK
            rel = jnp.where((rel >= 0) & (rel < CELL_BLOCK), rel, -1).astype(jnp.float32)
            parts.append(jnp.where(rel.astype(jnp.bfloat16) == ids, w, zero))
        table = parts[0] if count == 1 else jnp.concatenate(parts, axis=0)
        total = total + jnp.dot(table, aug[start : start + chunk, :], preferred_element_type=jnp.float32)
    return total


def sat_kernel(split, v_ref, c_ref, o_ref, tbl, low, high, aug, cells_s, w_s):
    n, d_in = v_ref.shape
    aug[:, :d_in] = v_ref[...]
    aug[:, d_in:] = jnp.ones((n, aug.shape[1] - d_in), jnp.bfloat16)
    cells_s[...] = c_ref[...]
    w_s[...] = lookup(o_ref[...], tbl, 0)
    high[...] = deposit_rows(aug, cells_s, w_s, split, high.shape[0] // CELL_BLOCK)
    low[...] = deposit_rows(aug, cells_s, w_s, 0, split)


def station_kernel(capacity, first, count, acc, got, tbl, embed, out, aug, cells_s, w_s):
    d_in = out.shape[1]
    bands = got.shape[0]
    aug[:, d_in:] = jnp.ones((aug.shape[0], aug.shape[1] - d_in), jnp.bfloat16)
    for t in range(bands):
        aug[t * capacity : (t + 1) * capacity, :d_in] = got[t, :capacity, :]
        meta = got[t, capacity : capacity + 6, :].astype(jnp.float32).astype(jnp.int32)
        for h in range(2):
            at = slice(t * capacity + h * d_in, t * capacity + (h + 1) * d_in)
            cells_s[:, at] = meta[h : h + 1] * 64 + meta[2 + h : 3 + h]
            w_s[:, at] = lookup(meta[4 + h : 5 + h], tbl, 1)
    total = acc[...] + deposit_rows(aug, cells_s, w_s, first, count)
    sums = total[:, :d_in]
    density = total[:, d_in:]
    grid = sums / jnp.maximum(density, 1.0) + density * embed[...]
    out[...] = grid.astype(out.dtype)


def whole(shape):
    return pl.BlockSpec(shape, lambda c: (0,) * len(shape))


SMEM = pl.BlockSpec(memory_space=pltpu.SMEM)


def sat_deposit(values, cells, offsets, table, split, total_cells):
    n, d_in = values.shape
    wide = 2 * d_in
    low_rows = split * CELL_BLOCK
    high_rows = total_cells - low_rows
    return pl.pallas_call(
        functools.partial(sat_kernel, split),
        grid=(1,),
        in_specs=[whole((n, d_in)), whole((1, n)), whole((1, n)), SMEM],
        out_specs=[whole((low_rows, wide)), whole((high_rows, wide))],
        out_shape=[
            jax.ShapeDtypeStruct((low_rows, wide), jnp.float32),
            jax.ShapeDtypeStruct((high_rows, wide), jnp.float32),
        ],
        scratch_shapes=[
            pltpu.VMEM((n, wide), jnp.bfloat16),
            pltpu.VMEM((1, n), jnp.int32),
            pltpu.VMEM((1, n), jnp.float32),
        ],
        cost_estimate=pl.CostEstimate(
            flops=2 * total_cells * n * wide, transcendentals=0, bytes_accessed=2 * n * (d_in + 4)
        ),
    )(values, cells.reshape(1, n), offsets.reshape(1, n), table)


def station_deposit(acc, got, table, embed, capacity, first, count):
    bands, rows, d_in = got.shape
    n = bands * capacity
    wide = 2 * d_in
    cells = count * CELL_BLOCK
    return pl.pallas_call(
        functools.partial(station_kernel, capacity, first, count),
        grid=(1,),
        in_specs=[whole((cells, wide)), whole((bands, rows, d_in)), SMEM, whole((1, d_in))],
        out_specs=whole((cells, d_in)),
        out_shape=jax.ShapeDtypeStruct((cells, d_in), jnp.bfloat16),
        scratch_shapes=[
            pltpu.VMEM((n, wide), jnp.bfloat16),
            pltpu.VMEM((1, n), jnp.int32),
            pltpu.VMEM((1, n), jnp.float32),
        ],
        cost_estimate=pl.CostEstimate(
            flops=2 * cells * n * wide, transcendentals=0, bytes_accessed=2 * n * (d_in + 4)
        ),
    )(acc, got, table, embed.reshape(1, d_in))


def pick(scratch, value, start):
    rows, cols = value.shape
    lanes = scratch.shape[2]
    parts = []
    for k in range(cols // lanes):
        scratch[k, :rows, :] = value[:, k * lanes : (k + 1) * lanes]
        parts.append(scratch[k, pl.ds(start, rows // 2, stride=2), :])
    return parts[0] if len(parts) == 1 else jnp.concatenate(parts, axis=1)


def shifted_odd(scratch, value, period):
    odd = pick(scratch, value, 1)
    odd = pltpu.roll(odd, 1, 0)
    first = lax.broadcasted_iota(jnp.int32, odd.shape, 0) % period == 0
    return jnp.where(first, 0.0, odd)


def conv_taps(source, rows, width, weights):
    taps = []
    for e in range(3):
        total = None
        for a in range(3):
            piece = source[pl.ds(a, rows, stride=2)].reshape(rows * width, source.shape[2])
            part = jnp.dot(piece, weights[a, e], preferred_element_type=jnp.float32)
            total = part if total is None else total + part
        taps.append(total)
    return taps


def gelu(x):
    return 0.5 * x * (1.0 + lax.erf(x * 0.7071067811865476))


def conv_kernel(above, low, high, w1, b1, w2, b2, wp, out, xs, s1, h1, s2):
    halo, width, d_in = above.shape
    lat = low.shape[0] + high.shape[0]
    xs[:halo] = above[...]
    xs[halo : halo + low.shape[0]] = low[...]
    xs[halo + low.shape[0] :] = high[...]
    rows1 = (halo + lat - 1) // 2
    half = width // 2
    taps = conv_taps(xs, rows1, width, w1)
    pre1 = pick(s1, taps[1], 0) + pick(s1, taps[2], 1) + shifted_odd(s1, taps[0], half) + b1[...]
    hid = gelu(pre1)
    keep = (lax.broadcasted_iota(jnp.int32, hid.shape, 0) >= half) | (lax.axis_index("band") > 0)
    hid = jnp.where(keep, hid, 0.0).astype(jnp.bfloat16)
    h1[...] = hid.reshape(rows1, half, d_in)
    rows2 = (rows1 - 1) // 2
    quarter = half // 2
    taps = conv_taps(h1, rows2, half, w2)
    pre2 = pick(s2, taps[1], 0) + pick(s2, taps[2], 1) + shifted_odd(s2, taps[0], quarter) + b2[...]
    latent = gelu(pre2).astype(jnp.bfloat16)
    flat = jnp.dot(latent, wp[...], preferred_element_type=jnp.float32)
    out[...] = flat.astype(out.dtype).reshape(out.shape)


def convolve(bands, above, low, high, w1, b1, w2, b2, wp):
    halo, width, d_in = above.shape
    lat = low.shape[0] + high.shape[0]
    d_lat = w2.shape[3]
    rows1 = (halo + lat - 1) // 2
    rows2 = (rows1 - 1) // 2
    vmem = pl.BlockSpec(memory_space=pltpu.VMEM)
    return pl.pallas_call(
        conv_kernel,
        in_specs=[vmem] * 8,
        out_specs=vmem,
        out_shape=jax.ShapeDtypeStruct((1, rows2, width // 4, d_lat), jnp.bfloat16),
        scratch_shapes=[
            pltpu.VMEM((halo + lat, width, d_in), jnp.bfloat16),
            pltpu.VMEM((1, rows1 * width, 128), jnp.float32),
            pltpu.VMEM((rows1, width // 2, d_in), jnp.bfloat16),
            pltpu.VMEM((d_lat // 128, rows2 * width // 2, 128), jnp.float32),
        ],
    )(above, low, high, w1, b1.reshape(1, -1), w2, b2.reshape(1, -1), wp)


def prefix_count(mask):
    total = mask
    step = 1
    lanes = lax.broadcasted_iota(jnp.int32, mask.shape, 1)
    while step < mask.shape[1]:
        moved = pltpu.roll(total, step, 1)
        total = total + jnp.where(lanes >= step, moved, 0)
        step *= 2
    return total - mask


def route_kernel(capacity, target, cells, offsets, values, out, vaug):
    bands, rows, d_in = out.shape
    n = values.shape[0]
    t = target[...]
    band_ids = lax.broadcasted_iota(jnp.int32, (bands, n), 0)
    mask = (t == band_ids).astype(jnp.int32)
    rank = jnp.sum(mask * prefix_count(mask), axis=0, keepdims=True)
    c = cells[...]
    meta = jnp.concatenate(
        [c // 64, c % 64, offsets[...] + 1, jnp.zeros((d_in - 3, n), jnp.int32)], axis=0
    ).astype(jnp.float32)
    vaug[:, :d_in] = values[...]
    vaug[:, d_in:] = jnp.transpose(meta).astype(jnp.bfloat16)
    slots = lax.broadcasted_iota(jnp.int32, (capacity, n), 0).astype(jnp.float32).astype(jnp.bfloat16)
    per_row = capacity // d_in
    one = jnp.ones((), jnp.bfloat16)
    zero = jnp.zeros((), jnp.bfloat16)
    me = lax.axis_index("band")
    for b in range(bands):
        mine = jnp.where(t == b, rank, -1).astype(jnp.float32).astype(jnp.bfloat16)
        table = jnp.where(mine == slots, one, zero)
        res = jnp.dot(table, vaug[...], preferred_element_type=jnp.float32)
        k = (b - me + bands) % bands
        out[k, :capacity, :] = res[:, :d_in].astype(out.dtype)
        sent = jnp.transpose(res[:, d_in:]).astype(out.dtype)
        for m in range(3):
            for h in range(per_row):
                row = capacity + m * per_row + h
                out[k, row : row + 1, :] = sent[m : m + 1, h * d_in : (h + 1) * d_in]
        out[k, capacity + 3 * per_row :, :] = jnp.zeros((rows - capacity - 3 * per_row, d_in), out.dtype)


def route(obs_values, obs_band, obs_cell, obs_offset, bands):
    obs_rows, d_in = obs_values.shape
    capacity = obs_rows // 8
    vmem = pl.BlockSpec(memory_space=pltpu.VMEM)
    packet = pl.pallas_call(
        functools.partial(route_kernel, capacity),
        in_specs=[vmem] * 4,
        out_specs=vmem,
        out_shape=jax.ShapeDtypeStruct((bands, capacity + META, d_in), jnp.bfloat16),
        scratch_shapes=[pltpu.VMEM((obs_rows, 2 * d_in), jnp.bfloat16)],
    )(
        obs_band.reshape(1, obs_rows),
        obs_cell.reshape(1, obs_rows),
        obs_offset.reshape(1, obs_rows),
        obs_values,
    )
    moved = [packet[0:1]]
    for k in range(1, bands):
        pairs = [(j, (j + k) % bands) for j in range(bands)]
        moved.append(lax.ppermute(packet[k : k + 1], "band", pairs))
    return jnp.concatenate(moved, axis=0)


def body(
    obs_values,
    obs_band,
    obs_cell,
    obs_offset,
    sat_values,
    sat_cell,
    sat_offset,
    density_embed,
    conv1_weight,
    conv1_bias,
    conv2_weight,
    conv2_bias,
    proj_weight,
):
    bands = lax.axis_size("band")
    position_index = lax.axis_index("band")
    d_in = obs_values.shape[1]
    band_cells = LAT_DEV * LON
    table = weights_of(jnp.arange(8, dtype=jnp.int32)).astype(jnp.float32)
    halo = 3
    lat_blocks = band_cells // CELL_BLOCK
    high_blocks = halo * LON // CELL_BLOCK
    low_blocks = lat_blocks - high_blocks
    sat_low, sat_high = sat_deposit(sat_values, sat_cell, sat_offset, table, low_blocks, band_cells)
    got = route(obs_values, obs_band, obs_cell, obs_offset, bands)
    capacity = obs_values.shape[0] // 8
    high = station_deposit(sat_high, got, table, density_embed, capacity, low_blocks, high_blocks)
    high = high.reshape(halo, LON, d_in)
    above = passed_along(high, "band", 1)
    low = station_deposit(sat_low, got, table, density_embed, capacity, 0, low_blocks)
    low = low.reshape(LAT_DEV - halo, LON, d_in)
    spread = convolve(bands, above, low, high, conv1_weight, conv1_bias, conv2_weight, conv2_bias, proj_weight)
    moved = [spread]
    for k in range(1, bands):
        pairs = [(j, (j + k) % bands) for j in range(bands)]
        moved.append(lax.ppermute(spread, "band", pairs))
    stacked = jnp.concatenate(moved, axis=0)
    order = (position_index - jnp.arange(bands, dtype=jnp.int32) + bands) % bands
    gathered = jnp.take(stacked, order, axis=0)
    return gathered.reshape((bands * spread.shape[1],) + spread.shape[2:])


def solution(mesh):
    placed = (
        P(("member", "band"), None),
        P(("member", "band"), None),
        P(("member", "band")),
        P(("member", "band")),
        P(("member", "band"), None),
        P(("member", "band")),
        P(("member", "band")),
        P(),
        P(),
        P(),
        P(),
        P(),
        P(),
    )
    return jax.shard_map(
        body, mesh=mesh, in_specs=placed, out_specs=P("member", None, None), check_vma=False
    )
```

```python
import functools

import jax
import jax.numpy as jnp
from jax import lax
from jax.experimental import pallas as pl
from jax.experimental.pallas import tpu as pltpu
from jax.sharding import PartitionSpec as P


LAT_DEV = 8
LON = 256
META = 16


def passed_along(value, axis, by):
    length = lax.axis_size(axis)
    pairs = [(i, i + by) for i in range(length) if 0 <= i + by < length]
    return lax.ppermute(value, axis, pairs)


def weights_of(offsets):
    return jnp.exp(-offsets.astype(jnp.float32) ** 2 / 32.0).astype(jnp.bfloat16)


CELL_BLOCK = 256
OBS_CHUNK = 2048


def lookup(codes, table, shift):
    w = jnp.zeros(codes.shape, jnp.float32)
    for j in range(8):
        w = jnp.where(codes == j + shift, table[j], w)
    return w


def deposit_rows(aug, cells_s, w_s, first, count):
    n = aug.shape[0]
    chunk = min(n, OBS_CHUNK)
    ids = lax.broadcasted_iota(jnp.int32, (CELL_BLOCK, chunk), 0).astype(jnp.float32)
    ids = ids.astype(jnp.bfloat16)
    zero = jnp.zeros((), jnp.bfloat16)
    total = jnp.zeros((count * CELL_BLOCK, aug.shape[1]), jnp.float32)
    for start in range(0, n, chunk):
        cells = cells_s[:, start : start + chunk]
        w = w_s[:, start : start + chunk].astype(jnp.bfloat16)
        parts = []
        for k in range(count):
            rel = cells - (first + k) * CELL_BLOCK
            rel = jnp.where((rel >= 0) & (rel < CELL_BLOCK), rel, -1).astype(jnp.float32)
            parts.append(jnp.where(rel.astype(jnp.bfloat16) == ids, w, zero))
        table = parts[0] if count == 1 else jnp.concatenate(parts, axis=0)
        total = total + jnp.dot(table, aug[start : start + chunk, :], preferred_element_type=jnp.float32)
    return total


def sat_kernel(split, v_ref, c_ref, o_ref, tbl, low, high, aug, cells_s, w_s):
    n, d_in = v_ref.shape
    aug[:, :d_in] = v_ref[...]
    aug[:, d_in:] = jnp.ones((n, aug.shape[1] - d_in), jnp.bfloat16)
    cells_s[...] = c_ref[...]
    w_s[...] = lookup(o_ref[...], tbl, 0)
    high[...] = deposit_rows(aug, cells_s, w_s, split, high.shape[0] // CELL_BLOCK)
    low[...] = deposit_rows(aug, cells_s, w_s, 0, split)


def station_kernel(capacity, first, count, acc, got, tbl, embed, out, aug, cells_s, w_s):
    d_in = out.shape[1]
    bands = got.shape[0]
    aug[:, d_in:] = jnp.ones((aug.shape[0], aug.shape[1] - d_in), jnp.bfloat16)
    for t in range(bands):
        aug[t * capacity : (t + 1) * capacity, :d_in] = got[t, :capacity, :]
        meta = got[t, capacity : capacity + 6, :].astype(jnp.float32).astype(jnp.int32)
        for h in range(2):
            at = slice(t * capacity + h * d_in, t * capacity + (h + 1) * d_in)
            cells_s[:, at] = meta[h : h + 1] * 64 + meta[2 + h : 3 + h]
            w_s[:, at] = lookup(meta[4 + h : 5 + h], tbl, 1)
    total = acc[...] + deposit_rows(aug, cells_s, w_s, first, count)
    sums = total[:, :d_in]
    density = total[:, d_in:]
    grid = sums / jnp.maximum(density, 1.0) + density * embed[...]
    out[...] = grid.astype(out.dtype)


def whole(shape):
    return pl.BlockSpec(shape, lambda c: (0,) * len(shape))


SMEM = pl.BlockSpec(memory_space=pltpu.SMEM)


def sat_deposit(values, cells, offsets, table, split, total_cells):
    n, d_in = values.shape
    wide = 2 * d_in
    low_rows = split * CELL_BLOCK
    high_rows = total_cells - low_rows
    return pl.pallas_call(
        functools.partial(sat_kernel, split),
        grid=(1,),
        in_specs=[whole((n, d_in)), whole((1, n)), whole((1, n)), SMEM],
        out_specs=[whole((low_rows, wide)), whole((high_rows, wide))],
        out_shape=[
            jax.ShapeDtypeStruct((low_rows, wide), jnp.float32),
            jax.ShapeDtypeStruct((high_rows, wide), jnp.float32),
        ],
        scratch_shapes=[
            pltpu.VMEM((n, wide), jnp.bfloat16),
            pltpu.VMEM((1, n), jnp.int32),
            pltpu.VMEM((1, n), jnp.float32),
        ],
        cost_estimate=pl.CostEstimate(
            flops=2 * total_cells * n * wide, transcendentals=0, bytes_accessed=2 * n * (d_in + 4)
        ),
    )(values, cells.reshape(1, n), offsets.reshape(1, n), table)


def station_deposit(acc, got, table, embed, capacity, first, count):
    bands, rows, d_in = got.shape
    n = bands * capacity
    wide = 2 * d_in
    cells = count * CELL_BLOCK
    return pl.pallas_call(
        functools.partial(station_kernel, capacity, first, count),
        grid=(1,),
        in_specs=[whole((cells, wide)), whole((bands, rows, d_in)), SMEM, whole((1, d_in))],
        out_specs=whole((cells, d_in)),
        out_shape=jax.ShapeDtypeStruct((cells, d_in), jnp.bfloat16),
        scratch_shapes=[
            pltpu.VMEM((n, wide), jnp.bfloat16),
            pltpu.VMEM((1, n), jnp.int32),
            pltpu.VMEM((1, n), jnp.float32),
        ],
        cost_estimate=pl.CostEstimate(
            flops=2 * cells * n * wide, transcendentals=0, bytes_accessed=2 * n * (d_in + 4)
        ),
    )(acc, got, table, embed.reshape(1, d_in))


def pick(scratch, value, start):
    rows, cols = value.shape
    lanes = scratch.shape[2]
    parts = []
    for k in range(cols // lanes):
        scratch[k, :rows, :] = value[:, k * lanes : (k + 1) * lanes]
        parts.append(scratch[k, pl.ds(start, rows // 2, stride=2), :])
    return parts[0] if len(parts) == 1 else jnp.concatenate(parts, axis=1)


def shifted_odd(scratch, value, period):
    odd = pick(scratch, value, 1)
    odd = pltpu.roll(odd, 1, 0)
    first = lax.broadcasted_iota(jnp.int32, odd.shape, 0) % period == 0
    return jnp.where(first, 0.0, odd)


def conv_taps(source, rows, width, weights):
    taps = []
    for e in range(3):
        total = None
        for a in range(3):
            piece = source[pl.ds(a, rows, stride=2)].reshape(rows * width, source.shape[2])
            part = jnp.dot(piece, weights[a, e], preferred_element_type=jnp.float32)
            total = part if total is None else total + part
        taps.append(total)
    return taps


def gelu(x):
    return 0.5 * x * (1.0 + lax.erf(x * 0.7071067811865476))


def conv_kernel(above, low, high, w1, b1, w2, b2, wp, out, xs, s1, h1, s2):
    halo, width, d_in = above.shape
    lat = low.shape[0] + high.shape[0]
    xs[:halo] = above[...]
    xs[halo : halo + low.shape[0]] = low[...]
    xs[halo + low.shape[0] :] = high[...]
    rows1 = (halo + lat - 1) // 2
    half = width // 2
    taps = conv_taps(xs, rows1, width, w1)
    pre1 = pick(s1, taps[1], 0) + pick(s1, taps[2], 1) + shifted_odd(s1, taps[0], half) + b1[...]
    hid = gelu(pre1)
    keep = (lax.broadcasted_iota(jnp.int32, hid.shape, 0) >= half) | (lax.axis_index("band") > 0)
    hid = jnp.where(keep, hid, 0.0).astype(jnp.bfloat16)
    h1[...] = hid.reshape(rows1, half, d_in)
    rows2 = (rows1 - 1) // 2
    quarter = half // 2
    taps = conv_taps(h1, rows2, half, w2)
    pre2 = pick(s2, taps[1], 0) + pick(s2, taps[2], 1) + shifted_odd(s2, taps[0], quarter) + b2[...]
    latent = gelu(pre2).astype(jnp.bfloat16)
    flat = jnp.dot(latent, wp[...], preferred_element_type=jnp.float32)
    out[...] = flat.astype(out.dtype).reshape(out.shape)


def convolve(bands, above, low, high, w1, b1, w2, b2, wp):
    halo, width, d_in = above.shape
    lat = low.shape[0] + high.shape[0]
    d_lat = w2.shape[3]
    rows1 = (halo + lat - 1) // 2
    rows2 = (rows1 - 1) // 2
    vmem = pl.BlockSpec(memory_space=pltpu.VMEM)
    return pl.pallas_call(
        conv_kernel,
        in_specs=[vmem] * 8,
        out_specs=vmem,
        out_shape=jax.ShapeDtypeStruct((1, rows2, width // 4, d_lat), jnp.bfloat16),
        scratch_shapes=[
            pltpu.VMEM((halo + lat, width, d_in), jnp.bfloat16),
            pltpu.VMEM((1, rows1 * width, 128), jnp.float32),
            pltpu.VMEM((rows1, width // 2, d_in), jnp.bfloat16),
            pltpu.VMEM((d_lat // 128, rows2 * width // 2, 128), jnp.float32),
        ],
    )(above, low, high, w1, b1.reshape(1, -1), w2, b2.reshape(1, -1), wp)


def prefix_count(mask):
    total = mask
    step = 1
    lanes = lax.broadcasted_iota(jnp.int32, mask.shape, 1)
    while step < mask.shape[1]:
        moved = pltpu.roll(total, step, 1)
        total = total + jnp.where(lanes >= step, moved, 0)
        step *= 2
    return total - mask


def route_kernel(capacity, target, cells, offsets, values, *refs):
    outs, vaug = refs[:-1], refs[-1]
    bands = len(outs)
    rows, d_in = outs[0].shape
    n = values.shape[0]
    t = target[...]
    band_ids = lax.broadcasted_iota(jnp.int32, (bands, n), 0)
    mask = (t == band_ids).astype(jnp.int32)
    rank = jnp.sum(mask * prefix_count(mask), axis=0, keepdims=True)
    c = cells[...]
    meta = jnp.concatenate(
        [c // 64, c % 64, offsets[...] + 1, jnp.zeros((d_in - 3, n), jnp.int32)], axis=0
    ).astype(jnp.float32)
    vaug[:, :d_in] = values[...]
    vaug[:, d_in:] = jnp.transpose(meta).astype(jnp.bfloat16)
    slots = lax.broadcasted_iota(jnp.int32, (capacity, n), 0).astype(jnp.float32).astype(jnp.bfloat16)
    per_row = capacity // d_in
    one = jnp.ones((), jnp.bfloat16)
    zero = jnp.zeros((), jnp.bfloat16)
    me = lax.axis_index("band")
    for k in range(bands):
        out = outs[k]
        b = (me + k) % bands
        mine = jnp.where(t == b, rank, -1).astype(jnp.float32).astype(jnp.bfloat16)
        table = jnp.where(mine == slots, one, zero)
        res = jnp.dot(table, vaug[...], preferred_element_type=jnp.float32)
        out[:capacity, :] = res[:, :d_in].astype(out.dtype)
        sent = jnp.transpose(res[:, d_in:]).astype(out.dtype)
        for m in range(3):
            for h in range(per_row):
                row = capacity + m * per_row + h
                out[row : row + 1, :] = sent[m : m + 1, h * d_in : (h + 1) * d_in]
        out[capacity + 3 * per_row :, :] = jnp.zeros((rows - capacity - 3 * per_row, d_in), out.dtype)


def route(obs_values, obs_band, obs_cell, obs_offset, bands):
    obs_rows, d_in = obs_values.shape
    capacity = obs_rows // 8
    vmem = pl.BlockSpec(memory_space=pltpu.VMEM)
    packet = pl.pallas_call(
        functools.partial(route_kernel, capacity),
        in_specs=[vmem] * 4,
        out_specs=[vmem] * bands,
        out_shape=[jax.ShapeDtypeStruct((capacity + META, d_in), jnp.bfloat16)] * bands,
        scratch_shapes=[pltpu.VMEM((obs_rows, 2 * d_in), jnp.bfloat16)],
    )(
        obs_band.reshape(1, obs_rows),
        obs_cell.reshape(1, obs_rows),
        obs_offset.reshape(1, obs_rows),
        obs_values,
    )
    moved = [packet[0][None]]
    for k in range(1, bands):
        pairs = [(j, (j + k) % bands) for j in range(bands)]
        moved.append(lax.ppermute(packet[k][None], "band", pairs))
    return jnp.concatenate(moved, axis=0)


def body(
    obs_values,
    obs_band,
    obs_cell,
    obs_offset,
    sat_values,
    sat_cell,
    sat_offset,
    density_embed,
    conv1_weight,
    conv1_bias,
    conv2_weight,
    conv2_bias,
    proj_weight,
):
    bands = lax.axis_size("band")
    position_index = lax.axis_index("band")
    d_in = obs_values.shape[1]
    band_cells = LAT_DEV * LON
    table = weights_of(jnp.arange(8, dtype=jnp.int32)).astype(jnp.float32)
    halo = 3
    lat_blocks = band_cells // CELL_BLOCK
    high_blocks = halo * LON // CELL_BLOCK
    low_blocks = lat_blocks - high_blocks
    sat_low, sat_high = sat_deposit(sat_values, sat_cell, sat_offset, table, low_blocks, band_cells)
    got = route(obs_values, obs_band, obs_cell, obs_offset, bands)
    capacity = obs_values.shape[0] // 8
    high = station_deposit(sat_high, got, table, density_embed, capacity, low_blocks, high_blocks)
    high = high.reshape(halo, LON, d_in)
    above = passed_along(high, "band", 1)
    low = station_deposit(sat_low, got, table, density_embed, capacity, 0, low_blocks)
    low = low.reshape(LAT_DEV - halo, LON, d_in)
    spread = convolve(bands, above, low, high, conv1_weight, conv1_bias, conv2_weight, conv2_bias, proj_weight)
    moved = [spread]
    for k in range(1, bands):
        pairs = [(j, (j + k) % bands) for j in range(bands)]
        moved.append(lax.ppermute(spread, "band", pairs))
    stacked = jnp.concatenate(moved, axis=0)
    order = (position_index - jnp.arange(bands, dtype=jnp.int32) + bands) % bands
    gathered = jnp.take(stacked, order, axis=0)
    return gathered.reshape((bands * spread.shape[1],) + spread.shape[2:])


def solution(mesh):
    placed = (
        P(("member", "band"), None),
        P(("member", "band"), None),
        P(("member", "band")),
        P(("member", "band")),
        P(("member", "band"), None),
        P(("member", "band")),
        P(("member", "band")),
        P(),
        P(),
        P(),
        P(),
        P(),
        P(),
    )
    return jax.shard_map(
        body, mesh=mesh, in_specs=placed, out_specs=P("member", None, None), check_vma=False
    )
```

```python
import functools

import jax
import jax.numpy as jnp
from jax import lax
from jax.experimental import pallas as pl
from jax.experimental.pallas import tpu as pltpu
from jax.sharding import PartitionSpec as P


LAT_DEV = 8
LON = 256
META = 16


def passed_along(value, axis, by):
    length = lax.axis_size(axis)
    pairs = [(i, i + by) for i in range(length) if 0 <= i + by < length]
    return lax.ppermute(value, axis, pairs)


def weights_of(offsets):
    return jnp.exp(-offsets.astype(jnp.float32) ** 2 / 32.0).astype(jnp.bfloat16)


CELL_BLOCK = 256
OBS_CHUNK = 2048


def lookup(codes, table, shift):
    w = jnp.zeros(codes.shape, jnp.float32)
    for j in range(8):
        w = jnp.where(codes == j + shift, table[j], w)
    return w


def deposit_rows(aug, cells_s, w_s, first, count):
    n = aug.shape[0]
    chunk = min(n, OBS_CHUNK)
    ids = lax.broadcasted_iota(jnp.int32, (CELL_BLOCK, chunk), 0).astype(jnp.float32)
    ids = ids.astype(jnp.bfloat16)
    zero = jnp.zeros((), jnp.bfloat16)
    total = jnp.zeros((count * CELL_BLOCK, aug.shape[1]), jnp.float32)
    for start in range(0, n, chunk):
        cells = cells_s[:, start : start + chunk]
        w = w_s[:, start : start + chunk].astype(jnp.bfloat16)
        parts = []
        for k in range(count):
            rel = cells - (first + k) * CELL_BLOCK
            rel = jnp.where((rel >= 0) & (rel < CELL_BLOCK), rel, -1).astype(jnp.float32)
            parts.append(jnp.where(rel.astype(jnp.bfloat16) == ids, w, zero))
        table = parts[0] if count == 1 else jnp.concatenate(parts, axis=0)
        total = total + jnp.dot(table, aug[start : start + chunk, :], preferred_element_type=jnp.float32)
    return total


def sat_kernel(split, v_ref, c_ref, o_ref, tbl, low, high, aug, cells_s, w_s):
    n, d_in = v_ref.shape
    aug[:, :d_in] = v_ref[...]
    aug[:, d_in:] = jnp.ones((n, aug.shape[1] - d_in), jnp.bfloat16)
    cells_s[...] = c_ref[...]
    w_s[...] = lookup(o_ref[...], tbl, 0)
    high[...] = deposit_rows(aug, cells_s, w_s, split, high.shape[0] // CELL_BLOCK)
    low[...] = deposit_rows(aug, cells_s, w_s, 0, split)


def station_kernel(capacity, first, count, bands, acc, *refs):
    got = refs[:bands]
    tbl, embed, out, aug, cells_s, w_s = refs[bands:]
    d_in = out.shape[1]
    aug[:, d_in:] = jnp.ones((aug.shape[0], aug.shape[1] - d_in), jnp.bfloat16)
    for t in range(bands):
        aug[t * capacity : (t + 1) * capacity, :d_in] = got[t][:capacity, :]
        meta = got[t][capacity : capacity + 6, :].astype(jnp.float32).astype(jnp.int32)
        for h in range(2):
            at = slice(t * capacity + h * d_in, t * capacity + (h + 1) * d_in)
            cells_s[:, at] = meta[h : h + 1] * 64 + meta[2 + h : 3 + h]
            w_s[:, at] = lookup(meta[4 + h : 5 + h], tbl, 1)
    total = acc[...] + deposit_rows(aug, cells_s, w_s, first, count)
    sums = total[:, :d_in]
    density = total[:, d_in:]
    grid = sums / jnp.maximum(density, 1.0) + density * embed[...]
    out[...] = grid.astype(out.dtype)


def whole(shape):
    return pl.BlockSpec(shape, lambda c: (0,) * len(shape))


SMEM = pl.BlockSpec(memory_space=pltpu.SMEM)


def sat_deposit(values, cells, offsets, table, split, total_cells):
    n, d_in = values.shape
    wide = 2 * d_in
    low_rows = split * CELL_BLOCK
    high_rows = total_cells - low_rows
    return pl.pallas_call(
        functools.partial(sat_kernel, split),
        grid=(1,),
        in_specs=[whole((n, d_in)), whole((1, n)), whole((1, n)), SMEM],
        out_specs=[whole((low_rows, wide)), whole((high_rows, wide))],
        out_shape=[
            jax.ShapeDtypeStruct((low_rows, wide), jnp.float32),
            jax.ShapeDtypeStruct((high_rows, wide), jnp.float32),
        ],
        scratch_shapes=[
            pltpu.VMEM((n, wide), jnp.bfloat16),
            pltpu.VMEM((1, n), jnp.int32),
            pltpu.VMEM((1, n), jnp.float32),
        ],
        cost_estimate=pl.CostEstimate(
            flops=2 * total_cells * n * wide, transcendentals=0, bytes_accessed=2 * n * (d_in + 4)
        ),
    )(values, cells.reshape(1, n), offsets.reshape(1, n), table)


def station_deposit(acc, got, table, embed, capacity, first, count):
    bands = len(got)
    rows, d_in = got[0].shape
    n = bands * capacity
    wide = 2 * d_in
    cells = count * CELL_BLOCK
    return pl.pallas_call(
        functools.partial(station_kernel, capacity, first, count, bands),
        grid=(1,),
        in_specs=[whole((cells, wide))] + [whole((rows, d_in))] * bands + [SMEM, whole((1, d_in))],
        out_specs=whole((cells, d_in)),
        out_shape=jax.ShapeDtypeStruct((cells, d_in), jnp.bfloat16),
        scratch_shapes=[
            pltpu.VMEM((n, wide), jnp.bfloat16),
            pltpu.VMEM((1, n), jnp.int32),
            pltpu.VMEM((1, n), jnp.float32),
        ],
        cost_estimate=pl.CostEstimate(
            flops=2 * cells * n * wide, transcendentals=0, bytes_accessed=2 * n * (d_in + 4)
        ),
    )(acc, *got, table, embed.reshape(1, d_in))


def pick(scratch, value, start):
    rows, cols = value.shape
    lanes = scratch.shape[2]
    parts = []
    for k in range(cols // lanes):
        scratch[k, :rows, :] = value[:, k * lanes : (k + 1) * lanes]
        parts.append(scratch[k, pl.ds(start, rows // 2, stride=2), :])
    return parts[0] if len(parts) == 1 else jnp.concatenate(parts, axis=1)


def shifted_odd(scratch, value, period):
    odd = pick(scratch, value, 1)
    odd = pltpu.roll(odd, 1, 0)
    first = lax.broadcasted_iota(jnp.int32, odd.shape, 0) % period == 0
    return jnp.where(first, 0.0, odd)


def conv_taps(source, rows, width, weights):
    taps = []
    for e in range(3):
        total = None
        for a in range(3):
            piece = source[pl.ds(a, rows, stride=2)].reshape(rows * width, source.shape[2])
            part = jnp.dot(piece, weights[a, e], preferred_element_type=jnp.float32)
            total = part if total is None else total + part
        taps.append(total)
    return taps


def gelu(x):
    return 0.5 * x * (1.0 + lax.erf(x * 0.7071067811865476))


def conv_kernel(above, low, high, w1, b1, w2, b2, wp, out, xs, s1, h1, s2):
    halo, width, d_in = above.shape
    lat = low.shape[0] + high.shape[0]
    xs[:halo] = above[...]
    xs[halo : halo + low.shape[0]] = low[...]
    xs[halo + low.shape[0] :] = high[...]
    rows1 = (halo + lat - 1) // 2
    half = width // 2
    taps = conv_taps(xs, rows1, width, w1)
    pre1 = pick(s1, taps[1], 0) + pick(s1, taps[2], 1) + shifted_odd(s1, taps[0], half) + b1[...]
    hid = gelu(pre1)
    keep = (lax.broadcasted_iota(jnp.int32, hid.shape, 0) >= half) | (lax.axis_index("band") > 0)
    hid = jnp.where(keep, hid, 0.0).astype(jnp.bfloat16)
    h1[...] = hid.reshape(rows1, half, d_in)
    rows2 = (rows1 - 1) // 2
    quarter = half // 2
    taps = conv_taps(h1, rows2, half, w2)
    pre2 = pick(s2, taps[1], 0) + pick(s2, taps[2], 1) + shifted_odd(s2, taps[0], quarter) + b2[...]
    latent = gelu(pre2).astype(jnp.bfloat16)
    flat = jnp.dot(latent, wp[...], preferred_element_type=jnp.float32)
    out[...] = flat.astype(out.dtype).reshape(out.shape)


def convolve(bands, above, low, high, w1, b1, w2, b2, wp):
    halo, width, d_in = above.shape
    lat = low.shape[0] + high.shape[0]
    d_lat = w2.shape[3]
    rows1 = (halo + lat - 1) // 2
    rows2 = (rows1 - 1) // 2
    vmem = pl.BlockSpec(memory_space=pltpu.VMEM)
    return pl.pallas_call(
        conv_kernel,
        in_specs=[vmem] * 8,
        out_specs=vmem,
        out_shape=jax.ShapeDtypeStruct((1, rows2, width // 4, d_lat), jnp.bfloat16),
        scratch_shapes=[
            pltpu.VMEM((halo + lat, width, d_in), jnp.bfloat16),
            pltpu.VMEM((1, rows1 * width, 128), jnp.float32),
            pltpu.VMEM((rows1, width // 2, d_in), jnp.bfloat16),
            pltpu.VMEM((d_lat // 128, rows2 * width // 2, 128), jnp.float32),
        ],
    )(above, low, high, w1, b1.reshape(1, -1), w2, b2.reshape(1, -1), wp)


def prefix_count(mask):
    total = mask
    step = 1
    lanes = lax.broadcasted_iota(jnp.int32, mask.shape, 1)
    while step < mask.shape[1]:
        moved = pltpu.roll(total, step, 1)
        total = total + jnp.where(lanes >= step, moved, 0)
        step *= 2
    return total - mask


def route_kernel(capacity, target, cells, offsets, values, *refs):
    outs, vaug = refs[:-1], refs[-1]
    bands = len(outs)
    rows, d_in = outs[0].shape
    n = values.shape[0]
    t = target[...]
    band_ids = lax.broadcasted_iota(jnp.int32, (bands, n), 0)
    mask = (t == band_ids).astype(jnp.int32)
    rank = jnp.sum(mask * prefix_count(mask), axis=0, keepdims=True)
    c = cells[...]
    meta = jnp.concatenate(
        [c // 64, c % 64, offsets[...] + 1, jnp.zeros((d_in - 3, n), jnp.int32)], axis=0
    ).astype(jnp.float32)
    vaug[:, :d_in] = values[...]
    vaug[:, d_in:] = jnp.transpose(meta).astype(jnp.bfloat16)
    slots = lax.broadcasted_iota(jnp.int32, (capacity, n), 0).astype(jnp.float32).astype(jnp.bfloat16)
    per_row = capacity // d_in
    one = jnp.ones((), jnp.bfloat16)
    zero = jnp.zeros((), jnp.bfloat16)
    me = lax.axis_index("band")
    for k in range(bands):
        out = outs[k]
        b = (me + k) % bands
        mine = jnp.where(t == b, rank, -1).astype(jnp.float32).astype(jnp.bfloat16)
        table = jnp.where(mine == slots, one, zero)
        res = jnp.dot(table, vaug[...], preferred_element_type=jnp.float32)
        out[:capacity, :] = res[:, :d_in].astype(out.dtype)
        sent = jnp.transpose(res[:, d_in:]).astype(out.dtype)
        for m in range(3):
            for h in range(per_row):
                row = capacity + m * per_row + h
                out[row : row + 1, :] = sent[m : m + 1, h * d_in : (h + 1) * d_in]
        out[capacity + 3 * per_row :, :] = jnp.zeros((rows - capacity - 3 * per_row, d_in), out.dtype)


def route(obs_values, obs_band, obs_cell, obs_offset, bands):
    obs_rows, d_in = obs_values.shape
    capacity = obs_rows // 8
    vmem = pl.BlockSpec(memory_space=pltpu.VMEM)
    packet = pl.pallas_call(
        functools.partial(route_kernel, capacity),
        in_specs=[vmem] * 4,
        out_specs=[vmem] * bands,
        out_shape=[jax.ShapeDtypeStruct((capacity + META, d_in), jnp.bfloat16)] * bands,
        scratch_shapes=[pltpu.VMEM((obs_rows, 2 * d_in), jnp.bfloat16)],
    )(
        obs_band.reshape(1, obs_rows),
        obs_cell.reshape(1, obs_rows),
        obs_offset.reshape(1, obs_rows),
        obs_values,
    )
    moved = [packet[0]]
    for k in range(1, bands):
        pairs = [(j, (j + k) % bands) for j in range(bands)]
        moved.append(lax.ppermute(packet[k], "band", pairs))
    return moved


def body(
    obs_values,
    obs_band,
    obs_cell,
    obs_offset,
    sat_values,
    sat_cell,
    sat_offset,
    density_embed,
    conv1_weight,
    conv1_bias,
    conv2_weight,
    conv2_bias,
    proj_weight,
):
    bands = lax.axis_size("band")
    position_index = lax.axis_index("band")
    d_in = obs_values.shape[1]
    band_cells = LAT_DEV * LON
    table = weights_of(jnp.arange(8, dtype=jnp.int32)).astype(jnp.float32)
    halo = 3
    lat_blocks = band_cells // CELL_BLOCK
    high_blocks = halo * LON // CELL_BLOCK
    low_blocks = lat_blocks - high_blocks
    sat_low, sat_high = sat_deposit(sat_values, sat_cell, sat_offset, table, low_blocks, band_cells)
    got = route(obs_values, obs_band, obs_cell, obs_offset, bands)
    capacity = obs_values.shape[0] // 8
    high = station_deposit(sat_high, got, table, density_embed, capacity, low_blocks, high_blocks)
    high = high.reshape(halo, LON, d_in)
    above = passed_along(high, "band", 1)
    low = station_deposit(sat_low, got, table, density_embed, capacity, 0, low_blocks)
    low = low.reshape(LAT_DEV - halo, LON, d_in)
    spread = convolve(bands, above, low, high, conv1_weight, conv1_bias, conv2_weight, conv2_bias, proj_weight)
    moved = [spread]
    for k in range(1, bands):
        pairs = [(j, (j + k) % bands) for j in range(bands)]
        moved.append(lax.ppermute(spread, "band", pairs))
    stacked = jnp.concatenate(moved, axis=0)
    order = (position_index - jnp.arange(bands, dtype=jnp.int32) + bands) % bands
    gathered = jnp.take(stacked, order, axis=0)
    return gathered.reshape((bands * spread.shape[1],) + spread.shape[2:])


def solution(mesh):
    placed = (
        P(("member", "band"), None),
        P(("member", "band"), None),
        P(("member", "band")),
        P(("member", "band")),
        P(("member", "band"), None),
        P(("member", "band")),
        P(("member", "band")),
        P(),
        P(),
        P(),
        P(),
        P(),
        P(),
    )
    return jax.shard_map(
        body, mesh=mesh, in_specs=placed, out_specs=P("member", None, None), check_vma=False
    )
```

```python
import functools

import jax
import jax.numpy as jnp
from jax import lax
from jax.experimental import pallas as pl
from jax.experimental.pallas import tpu as pltpu
from jax.sharding import PartitionSpec as P


LAT_DEV = 8
LON = 256
META = 16


def passed_along(value, axis, by):
    length = lax.axis_size(axis)
    pairs = [(i, i + by) for i in range(length) if 0 <= i + by < length]
    return lax.ppermute(value, axis, pairs)


def weights_of(offsets):
    return jnp.exp(-offsets.astype(jnp.float32) ** 2 / 32.0).astype(jnp.bfloat16)


CELL_BLOCK = 256
OBS_CHUNK = 2048


def lookup(codes, table, shift):
    w = jnp.zeros(codes.shape, jnp.float32)
    for j in range(8):
        w = jnp.where(codes == j + shift, table[j], w)
    return w


def deposit_rows(aug, cells_s, w_s, first, count):
    n = aug.shape[0]
    chunk = min(n, OBS_CHUNK)
    ids = lax.broadcasted_iota(jnp.int32, (CELL_BLOCK, chunk), 0).astype(jnp.float32)
    ids = ids.astype(jnp.bfloat16)
    zero = jnp.zeros((), jnp.bfloat16)
    total = jnp.zeros((count * CELL_BLOCK, aug.shape[1]), jnp.float32)
    for start in range(0, n, chunk):
        cells = cells_s[:, start : start + chunk]
        w = w_s[:, start : start + chunk].astype(jnp.bfloat16)
        parts = []
        for k in range(count):
            rel = cells - (first + k) * CELL_BLOCK
            rel = jnp.where((rel >= 0) & (rel < CELL_BLOCK), rel, -1).astype(jnp.float32)
            parts.append(jnp.where(rel.astype(jnp.bfloat16) == ids, w, zero))
        table = parts[0] if count == 1 else jnp.concatenate(parts, axis=0)
        total = total + jnp.dot(table, aug[start : start + chunk, :], preferred_element_type=jnp.float32)
    return total


def sat_kernel(split, v_ref, c_ref, o_ref, tbl, low, high, aug, cells_s, w_s):
    n, d_in = v_ref.shape
    aug[:, :d_in] = v_ref[...]
    aug[:, d_in:] = jnp.ones((n, aug.shape[1] - d_in), jnp.bfloat16)
    cells_s[...] = c_ref[...]
    w_s[...] = lookup(o_ref[...], tbl, 0)
    high[...] = deposit_rows(aug, cells_s, w_s, split, high.shape[0] // CELL_BLOCK)
    low[...] = deposit_rows(aug, cells_s, w_s, 0, split)


def station_kernel(capacity, first, count, bands, acc, *refs):
    got = refs[:bands]
    tbl, embed, out, aug, cells_s, w_s = refs[bands:]
    d_in = out.shape[1]
    aug[:, d_in:] = jnp.ones((aug.shape[0], aug.shape[1] - d_in), jnp.bfloat16)
    for t in range(bands):
        aug[t * capacity : (t + 1) * capacity, :d_in] = got[t][:capacity, :]
        meta = got[t][capacity : capacity + 6, :].astype(jnp.float32).astype(jnp.int32)
        for h in range(2):
            at = slice(t * capacity + h * d_in, t * capacity + (h + 1) * d_in)
            cells_s[:, at] = meta[h : h + 1] * 64 + meta[2 + h : 3 + h]
            w_s[:, at] = lookup(meta[4 + h : 5 + h], tbl, 1)
    total = acc[...] + deposit_rows(aug, cells_s, w_s, first, count)
    sums = total[:, :d_in]
    density = total[:, d_in:]
    grid = sums / jnp.maximum(density, 1.0) + density * embed[...]
    out[...] = grid.astype(out.dtype)


def whole(shape):
    return pl.BlockSpec(shape, lambda c: (0,) * len(shape))


SMEM = pl.BlockSpec(memory_space=pltpu.SMEM)


def sat_deposit(values, cells, offsets, table, split, total_cells):
    n, d_in = values.shape
    wide = 2 * d_in
    low_rows = split * CELL_BLOCK
    high_rows = total_cells - low_rows
    return pl.pallas_call(
        functools.partial(sat_kernel, split),
        grid=(1,),
        in_specs=[whole((n, d_in)), whole((1, n)), whole((1, n)), SMEM],
        out_specs=[whole((low_rows, wide)), whole((high_rows, wide))],
        out_shape=[
            jax.ShapeDtypeStruct((low_rows, wide), jnp.float32),
            jax.ShapeDtypeStruct((high_rows, wide), jnp.float32),
        ],
        scratch_shapes=[
            pltpu.VMEM((n, wide), jnp.bfloat16),
            pltpu.VMEM((1, n), jnp.int32),
            pltpu.VMEM((1, n), jnp.float32),
        ],
        cost_estimate=pl.CostEstimate(
            flops=2 * total_cells * n * wide, transcendentals=0, bytes_accessed=2 * n * (d_in + 4)
        ),
    )(values, cells.reshape(1, n), offsets.reshape(1, n), table)


def station_deposit(acc, got, table, embed, capacity, first, count):
    bands = len(got)
    rows, d_in = got[0].shape
    n = bands * capacity
    wide = 2 * d_in
    cells = count * CELL_BLOCK
    return pl.pallas_call(
        functools.partial(station_kernel, capacity, first, count, bands),
        grid=(1,),
        in_specs=[whole((cells, wide))] + [whole((rows, d_in))] * bands + [SMEM, whole((1, d_in))],
        out_specs=whole((cells, d_in)),
        out_shape=jax.ShapeDtypeStruct((cells, d_in), jnp.bfloat16),
        scratch_shapes=[
            pltpu.VMEM((n, wide), jnp.bfloat16),
            pltpu.VMEM((1, n), jnp.int32),
            pltpu.VMEM((1, n), jnp.float32),
        ],
        cost_estimate=pl.CostEstimate(
            flops=2 * cells * n * wide, transcendentals=0, bytes_accessed=2 * n * (d_in + 4)
        ),
    )(acc, *got, table, embed.reshape(1, d_in))


def pick(scratch, value, start):
    rows, cols = value.shape
    lanes = scratch.shape[2]
    parts = []
    for k in range(cols // lanes):
        scratch[k, :rows, :] = value[:, k * lanes : (k + 1) * lanes]
        parts.append(scratch[k, pl.ds(start, rows // 2, stride=2), :])
    return parts[0] if len(parts) == 1 else jnp.concatenate(parts, axis=1)


def shifted_odd(scratch, value, period):
    odd = pick(scratch, value, 1)
    odd = pltpu.roll(odd, 1, 0)
    first = lax.broadcasted_iota(jnp.int32, odd.shape, 0) % period == 0
    return jnp.where(first, 0.0, odd)


def conv_taps(source, rows, width, weights):
    taps = []
    for e in range(3):
        total = None
        for a in range(3):
            piece = source[pl.ds(a, rows, stride=2)].reshape(rows * width, source.shape[2])
            part = jnp.dot(piece, weights[a, e], preferred_element_type=jnp.float32)
            total = part if total is None else total + part
        taps.append(total)
    return taps


def gelu(x):
    return 0.5 * x * (1.0 + lax.erf(x * 0.7071067811865476))


def conv_kernel(above, low, high, w1, b1, w2, b2, wp, out, xs, s1, h1, s2):
    halo, width, d_in = above.shape
    lat = low.shape[0] + high.shape[0]
    xs[:halo] = above[...]
    xs[halo : halo + low.shape[0]] = low[...]
    xs[halo + low.shape[0] :] = high[...]
    rows1 = (halo + lat - 1) // 2
    half = width // 2
    taps = conv_taps(xs, rows1, width, w1)
    pre1 = pick(s1, taps[1], 0) + pick(s1, taps[2], 1) + shifted_odd(s1, taps[0], half) + b1[...]
    hid = gelu(pre1)
    keep = (lax.broadcasted_iota(jnp.int32, hid.shape, 0) >= half) | (lax.axis_index("band") > 0)
    hid = jnp.where(keep, hid, 0.0).astype(jnp.bfloat16)
    h1[...] = hid.reshape(rows1, half, d_in)
    rows2 = (rows1 - 1) // 2
    quarter = half // 2
    taps = conv_taps(h1, rows2, half, w2)
    pre2 = pick(s2, taps[1], 0) + pick(s2, taps[2], 1) + shifted_odd(s2, taps[0], quarter) + b2[...]
    latent = gelu(pre2).astype(jnp.bfloat16)
    flat = jnp.dot(latent, wp[...], preferred_element_type=jnp.float32)
    out[...] = flat.astype(out.dtype).reshape(out.shape)


def convolve(bands, above, low, high, w1, b1, w2, b2, wp):
    halo, width, d_in = above.shape
    lat = low.shape[0] + high.shape[0]
    d_lat = w2.shape[3]
    rows1 = (halo + lat - 1) // 2
    rows2 = (rows1 - 1) // 2
    vmem = pl.BlockSpec(memory_space=pltpu.VMEM)
    return pl.pallas_call(
        conv_kernel,
        in_specs=[vmem] * 8,
        out_specs=vmem,
        out_shape=jax.ShapeDtypeStruct((1, rows2, width // 4, d_lat), jnp.bfloat16),
        scratch_shapes=[
            pltpu.VMEM((halo + lat, width, d_in), jnp.bfloat16),
            pltpu.VMEM((1, rows1 * width, 128), jnp.float32),
            pltpu.VMEM((rows1, width // 2, d_in), jnp.bfloat16),
            pltpu.VMEM((d_lat // 128, rows2 * width // 2, 128), jnp.float32),
        ],
    )(above, low, high, w1, b1.reshape(1, -1), w2, b2.reshape(1, -1), wp)


def prefix_count(mask):
    total = mask
    step = 1
    lanes = lax.broadcasted_iota(jnp.int32, mask.shape, 1)
    while step < mask.shape[1]:
        moved = pltpu.roll(total, step, 1)
        total = total + jnp.where(lanes >= step, moved, 0)
        step *= 2
    return total - mask


def route_kernel(capacity, target, cells, offsets, values, *refs):
    outs, vaug = refs[:-1], refs[-1]
    bands = len(outs)
    rows, d_in = outs[0].shape
    n = values.shape[0]
    t = target[...]
    band_ids = lax.broadcasted_iota(jnp.int32, (bands, n), 0)
    mask = (t == band_ids).astype(jnp.int32)
    rank = jnp.sum(mask * prefix_count(mask), axis=0, keepdims=True)
    c = cells[...]
    meta = jnp.concatenate(
        [c // 64, c % 64, offsets[...] + 1, jnp.zeros((d_in - 3, n), jnp.int32)], axis=0
    ).astype(jnp.float32)
    vaug[:, :d_in] = values[...]
    vaug[:, d_in:] = jnp.transpose(meta).astype(jnp.bfloat16)
    slots = lax.broadcasted_iota(jnp.int32, (capacity, n), 0).astype(jnp.float32).astype(jnp.bfloat16)
    per_row = capacity // d_in
    one = jnp.ones((), jnp.bfloat16)
    zero = jnp.zeros((), jnp.bfloat16)
    me = lax.axis_index("band")
    for k in range(bands):
        out = outs[k]
        b = (me + k) % bands
        mine = jnp.where(t == b, rank, -1).astype(jnp.float32).astype(jnp.bfloat16)
        table = jnp.where(mine == slots, one, zero)
        res = jnp.dot(table, vaug[...], preferred_element_type=jnp.float32)
        out[:capacity, :] = res[:, :d_in].astype(out.dtype)
        sent = jnp.transpose(res[:, d_in:]).astype(out.dtype)
        for m in range(3):
            for h in range(per_row):
                row = capacity + m * per_row + h
                out[row : row + 1, :] = sent[m : m + 1, h * d_in : (h + 1) * d_in]
        out[capacity + 3 * per_row :, :] = jnp.zeros((rows - capacity - 3 * per_row, d_in), out.dtype)


def route(obs_values, obs_band, obs_cell, obs_offset, bands):
    obs_rows, d_in = obs_values.shape
    capacity = obs_rows // 8
    vmem = pl.BlockSpec(memory_space=pltpu.VMEM)
    packet = pl.pallas_call(
        functools.partial(route_kernel, capacity),
        in_specs=[vmem] * 4,
        out_specs=[vmem] * bands,
        out_shape=[jax.ShapeDtypeStruct((capacity + META, d_in), jnp.bfloat16)] * bands,
        scratch_shapes=[pltpu.VMEM((obs_rows, 2 * d_in), jnp.bfloat16)],
    )(
        obs_band.reshape(1, obs_rows),
        obs_cell.reshape(1, obs_rows),
        obs_offset.reshape(1, obs_rows),
        obs_values,
    )
    moved = [packet[0]]
    for k in range(1, bands):
        pairs = [(j, (j + k) % bands) for j in range(bands)]
        moved.append(lax.ppermute(packet[k], "band", pairs))
    return moved


def body(
    obs_values,
    obs_band,
    obs_cell,
    obs_offset,
    sat_values,
    sat_cell,
    sat_offset,
    density_embed,
    conv1_weight,
    conv1_bias,
    conv2_weight,
    conv2_bias,
    proj_weight,
):
    bands = lax.axis_size("band")
    position_index = lax.axis_index("band")
    d_in = obs_values.shape[1]
    band_cells = LAT_DEV * LON
    table = weights_of(jnp.arange(8, dtype=jnp.int32)).astype(jnp.float32)
    halo = 3
    lat_blocks = band_cells // CELL_BLOCK
    high_blocks = halo * LON // CELL_BLOCK
    low_blocks = lat_blocks - high_blocks
    sat_low, sat_high = sat_deposit(sat_values, sat_cell, sat_offset, table, low_blocks, band_cells)
    got = route(obs_values, obs_band, obs_cell, obs_offset, bands)
    capacity = obs_values.shape[0] // 8
    high = station_deposit(sat_high, got, table, density_embed, capacity, low_blocks, high_blocks)
    high = high.reshape(halo, LON, d_in)
    above = passed_along(high, "band", 1)
    low = station_deposit(sat_low, got, table, density_embed, capacity, 0, low_blocks)
    low = low.reshape(LAT_DEV - halo, LON, d_in)
    spread = convolve(bands, above, low, high, conv1_weight, conv1_bias, conv2_weight, conv2_bias, proj_weight)
    moved = [spread]
    for k in range(1, bands):
        pairs = [(j, (j + k) % bands) for j in range(bands)]
        moved.append(lax.ppermute(spread, "band", pairs))
    stacked = jnp.concatenate(moved, axis=0)
    order = (position_index - jnp.arange(bands, dtype=jnp.int32) + bands) % bands
    gathered = jnp.take(stacked, order, axis=0, mode="clip")
    return gathered.reshape((bands * spread.shape[1],) + spread.shape[2:])


def solution(mesh):
    placed = (
        P(("member", "band"), None),
        P(("member", "band"), None),
        P(("member", "band")),
        P(("member", "band")),
        P(("member", "band"), None),
        P(("member", "band")),
        P(("member", "band")),
        P(),
        P(),
        P(),
        P(),
        P(),
        P(),
    )
    return jax.shard_map(
        body, mesh=mesh, in_specs=placed, out_specs=P("member", None, None), check_vma=False
    )
```
